32 devices in a mesh: grp: 2 (over x), cand: 8 (over z, y), seq: 2 (over core).
Axes of the slice: x: 2, y: 2, z: 4, core: 2. Of those that a mesh axis runs over, the one named last changes fastest.
Arguments:
- x_prefix: bfloat16 [8192, 2560], P(('grp', 'cand', 'seq')), parts along dimension 0, may hold values from -6 to 6
- b_prefix: bfloat16 [8192, 128], P(('grp', 'cand', 'seq')), parts along dimension 0, may hold values from -0.5 to 0.5
- code_prefix: int32 [8192, 40], P(('grp', 'cand', 'seq')), parts along dimension 0, may hold values from 0 to 500
- x_cand: bfloat16 [32, 512, 2560], P(('grp', 'cand'), None, 'seq'), parts along dimension 0, may hold values from -6 to 6
- b_cand: bfloat16 [32, 512, 128], P(('grp', 'cand')), parts along dimension 0, may hold values from -0.5 to 0.5
- c_cand: bfloat16 [32, 512, 128], P(('grp', 'cand')), parts along dimension 0, may hold values from -0.5 to 0.5
- code_cand: int32 [32, 512, 40], P(('grp', 'cand'), None, 'seq'), parts along dimension 0, may hold values from 0 to 500
- lengths: int32 [32], P(('grp', 'cand')), parts along dimension 0, may hold values from 1 to 2, as said below
- dy_cand: bfloat16 [32, 512, 2560], P(('grp', 'cand'), None, 'seq'), parts along dimension 0, may hold values from -1.5 to 1.5
Outputs:
- dx_prefix: bfloat16 [8192, 2560], P(('grp', 'cand', 'seq')), parts along dimension 0
- db_prefix: float32 [8192, 128], P(('grp', 'cand', 'seq')), parts along dimension 0
- dx_cand: bfloat16 [32, 512, 2560], P(('grp', 'cand'), None, 'seq'), parts along dimension 0
- db_cand: float32 [32, 512, 128], P(('grp', 'cand'), 'seq'), parts along dimension 0
- dc_cand: float32 [32, 512, 128], P(('grp', 'cand'), 'seq'), parts along dimension 0
The draws below stay inside these ranges and needn't reach their ends.
There are 2 independent parts, one for each index of `grp`. The reference program is written for one: setup_inputs(seed, part) draws one part's arguments, and reference() takes and returns one part's arrays. A program takes and returns all parts, laid end to end along the dimension named above; each array names one. Nothing has to cross between parts.
Inputs may be any that keep to these rules, and one draw needn't show every extreme that they name: lengths count blocks of 256 tokens.
All inputs are finite; a program needn't handle non-finite values.
Results may differ from the reference program's by a relative error of at most 0.0015.
The reference program's roundings to bfloat16 on the way count: a program that leaves them out, or rounds other values in their place, can miss the bound.
Values may be sent and summed in bfloat16 or wider, within the bound.
No kernel may reach another device: no remote copies, remote signals or barrier semaphores. Data moves between devices by JAX's collectives and lax.ppermute only.
A program may use at most 256 MiB of HBM per device.

```python
import jax
import jax.numpy as jnp
from jax import lax

HEADS_HALF = 40
P_SIZE = 64
N = 128
BLOCK = 256
CAND_BLOCKS = 2
PREFIX_PER_SHARD = 256
CAND_LEN = 512
PREFIX_TOKENS = 4096
CANDS = 16


def head_codes(key, rows_total, heads_total):
    first_key, second_key = jax.random.split(jax.random.fold_in(key, 7))
    ceiling = jax.random.randint(first_key, (heads_total,), 1, 501)
    codes = jax.random.randint(second_key, (rows_total, heads_total), 0, ceiling[None, :] + 1)
    codes = codes.at[0, 0].set(500).at[0, 1].set(0)
    return codes.astype(jnp.int32)


def packed_codes(key, rows_total, heads_total, block_of_rows):
    block_count = rows_total // block_of_rows
    first_key, second_key, third_key, fourth_key = jax.random.split(jax.random.fold_in(key, 13), 4)
    high_flag = jax.random.randint(first_key, (block_count, heads_total), 0, 2)
    offset = jax.random.randint(second_key, (), 0, heads_total)
    block_at = jnp.arange(block_count, dtype=jnp.int32)[:, None]
    head_at = jnp.arange(heads_total, dtype=jnp.int32)[None, :]
    forced_high = (block_at + offset) % heads_total
    forced_low = (block_at + offset + 1) % heads_total
    high_flag = jnp.where(head_at == forced_high, 1, high_flag)
    high_flag = jnp.where(head_at == forced_low, 0, high_flag)
    high_rows = jnp.repeat(high_flag, block_of_rows, axis=0)
    high_codes = jax.random.randint(third_key, (rows_total, heads_total), 450, 501)
    low_codes = jax.random.randint(fourth_key, (rows_total, heads_total), 0, 51)
    codes = jnp.where(high_rows == 1, high_codes, low_codes)
    codes = codes.at[0, 0].set(500).at[0, 1].set(0)
    return codes.astype(jnp.int32)


def draw_code_prefix(key, part):
    return packed_codes(key, PREFIX_TOKENS, HEADS_HALF, PREFIX_PER_SHARD)


def draw_code_cand(key, part):
    return head_codes(key, CANDS * CAND_LEN, HEADS_HALF).reshape(CANDS, CAND_LEN, HEADS_HALF)


def draw_lengths(key, part):
    drawn = jax.random.randint(jax.random.fold_in(key, 11), (CANDS,), 1, CAND_BLOCKS + 1)
    return drawn.at[0].set(CAND_BLOCKS).astype(jnp.int32)


def steps_of(own_key, shape, cuts, low, top_value):
    loudness, own = 1.0, jax.random.fold_in(own_key, 6)
    for dim, shards_of in cuts:
        steps = jnp.exp(jax.random.uniform(jax.random.fold_in(own, dim), (shards_of,), jnp.float32, low / len(cuts), top_value / len(cuts)))
        loudness = loudness * jnp.repeat(steps, shape[dim] // shards_of).reshape([-1 if axis == dim else 1 for axis in range(len(shape))])
    return loudness


def bell_draw(rng, shape, deviation, bound, cuts=(), held_as=jnp.bfloat16):
    entries = deviation * jax.random.normal(rng, shape, jnp.float32)
    if cuts:
        entries = entries * steps_of(rng, shape, cuts, -0.22, 0.18)
    return jnp.clip(entries, -bound, bound).astype(held_as)


def setup_inputs(seed: int = 0, part: int = 0) -> dict:
    key_of = jax.random.split(jax.random.key(seed), 10)
    own_keys = jax.random.split(jax.random.fold_in(key_of[9], part), 10)
    return {
        "x_prefix": bell_draw(own_keys[0], (PREFIX_TOKENS, HEADS_HALF * P_SIZE), 1.0, 6.0, ((0, 16),)),
        "b_prefix": bell_draw(own_keys[1], (PREFIX_TOKENS, N), N ** -0.5, 0.5, ((0, 16),)),
        "code_prefix": draw_code_prefix(jax.random.fold_in(jax.random.fold_in(key_of[9], part), 71), part),
        "x_cand": bell_draw(own_keys[3], (CANDS, CAND_LEN, HEADS_HALF * P_SIZE), 1.0, 6.0, ((0, 8), (2, 2))),
        "b_cand": bell_draw(own_keys[4], (CANDS, CAND_LEN, N), N ** -0.5, 0.5, ((0, 8),)),
        "c_cand": bell_draw(own_keys[5], (CANDS, CAND_LEN, N), N ** -0.5, 0.5, ((0, 8),)),
        "code_cand": draw_code_cand(jax.random.fold_in(jax.random.fold_in(key_of[9], part), 71), part),
        "lengths": draw_lengths(jax.random.fold_in(jax.random.fold_in(key_of[9], part), 71), part),
        "dy_cand": bell_draw(own_keys[8], (CANDS, CAND_LEN, HEADS_HALF * P_SIZE), 0.25, 1.5, ((0, 8), (2, 2))),
    }


def rate_log(codes):
    return jnp.log1p(-codes.astype(jnp.float32) * 1e-6)


def reference(x_prefix, b_prefix, code_prefix, x_cand, b_cand, c_cand, code_cand, lengths, dy_cand):
    log_prefix = rate_log(code_prefix)
    after_all = jnp.flip(jnp.cumsum(jnp.flip(log_prefix, 0), axis=0), 0) - log_prefix
    weight = jnp.exp(after_all)
    b_wide = b_prefix.astype(jnp.float32)

    def head_slice(head_at):
        x_head = lax.dynamic_slice_in_dim(x_prefix, head_at * P_SIZE, P_SIZE, 1)
        w_head = lax.dynamic_slice_in_dim(weight, head_at, 1, 1)
        weighted = (w_head * b_wide).astype(jnp.bfloat16)
        return x_head, w_head, weighted

    def forward_head(head_at):
        x_head, w_head, weighted = head_slice(head_at)
        return jnp.dot(x_head.T, weighted, preferred_element_type=jnp.float32)

    init_state = lax.map(forward_head, jnp.arange(HEADS_HALF, dtype=jnp.int32))
    init_b = init_state.astype(jnp.bfloat16)

    def one_candidate(candidate):
        x_one, dy_one, b_one, c_one, code_one, length_one = candidate
        position = jnp.arange(CAND_LEN, dtype=jnp.int32)
        g_one = jnp.where((position < length_one * BLOCK)[:, None], dy_one, jnp.zeros_like(dy_one))
        level_sum = jnp.cumsum(rate_log(code_one), axis=0)
        causal = position[:, None] >= position[None, :]
        scores = jnp.dot(c_one, b_one.T, preferred_element_type=jnp.float32)

        def per_head(weight_sum, head_at):
            x_head = lax.dynamic_slice_in_dim(x_one, head_at * P_SIZE, P_SIZE, 1)
            g_head = lax.dynamic_slice_in_dim(g_one, head_at * P_SIZE, P_SIZE, 1)
            level_head = lax.dynamic_slice_in_dim(level_sum, head_at, 1, 1)[:, 0]
            decay_mat = jnp.where(causal, jnp.exp(level_head[:, None] - level_head[None, :]), jnp.zeros((), jnp.float32))
            kernel = (scores * decay_mat).astype(jnp.bfloat16)
            dx_head = jnp.dot(kernel.T, g_head, preferred_element_type=jnp.float32).astype(jnp.bfloat16)
            inner_prod = jnp.dot(g_head, x_head.T, preferred_element_type=jnp.float32)
            return weight_sum + inner_prod * decay_mat, dx_head

        weight_sum, dx_heads = lax.scan(per_head, jnp.zeros((CAND_LEN, CAND_LEN), jnp.float32), jnp.arange(HEADS_HALF, dtype=jnp.int32))
        dx_one = jnp.transpose(dx_heads, (1, 0, 2)).reshape(CAND_LEN, HEADS_HALF * P_SIZE)
        db_one = jnp.dot(weight_sum.T, c_one.astype(jnp.float32), precision=lax.Precision.HIGHEST)
        dc_local = jnp.dot(weight_sum, b_one.astype(jnp.float32), precision=lax.Precision.HIGHEST)
        amplitude = jnp.exp(level_sum)
        decayed_g = (g_one.reshape(CAND_LEN, HEADS_HALF, P_SIZE).astype(jnp.float32) * amplitude[:, :, None]).astype(jnp.bfloat16)
        dc_one = dc_local + jnp.dot(decayed_g.reshape(CAND_LEN, HEADS_HALF * P_SIZE), init_b.reshape(HEADS_HALF * P_SIZE, N), preferred_element_type=jnp.float32)
        dstate_one = jnp.einsum("thp,tn->hpn", decayed_g.astype(jnp.float32), c_one.astype(jnp.float32))
        return dx_one, db_one, dc_one, dstate_one

    dx_cand, db_cand, dc_cand, dstates = lax.map(one_candidate, (x_cand, dy_cand, b_cand, c_cand, code_cand, lengths))
    grad_state = jnp.sum(dstates, axis=0).astype(jnp.bfloat16)

    def backward_head(db_acc, head_at):
        x_head, w_head, weighted = head_slice(head_at)
        g_head = grad_state[head_at]
        dx_head = jnp.dot(weighted, g_head.T, preferred_element_type=jnp.float32).astype(jnp.bfloat16)
        projected = jnp.dot(x_head, g_head, preferred_element_type=jnp.float32)
        return db_acc + projected * w_head, dx_head

    db_prefix, dx_heads = lax.scan(backward_head, jnp.zeros((PREFIX_TOKENS, N), jnp.float32), jnp.arange(HEADS_HALF, dtype=jnp.int32))
    dx_prefix = jnp.transpose(dx_heads, (1, 0, 2)).reshape(PREFIX_TOKENS, HEADS_HALF * P_SIZE)
    return (dx_prefix, db_prefix, dx_cand, db_cand, dc_cand)
```

```python
import jax
import jax.numpy as jnp
from jax import lax
from jax.sharding import PartitionSpec as P

BLOCK = 256


def split_bf16(value):
    high = lax.reduce_precision(value, exponent_bits=8, mantissa_bits=7)
    low = (value - high).astype(jnp.bfloat16)
    return high.astype(jnp.bfloat16), low


def shards(x_prefix, b_prefix, code_prefix, x_cand, b_cand, c_cand, code_cand, lengths, dy_cand):
    pre_len, width = x_prefix.shape
    heads_total = code_prefix.shape[1]
    head_size = width // heads_total
    nstate = b_prefix.shape[1]
    cand_dev, cand_len, half_width = x_cand.shape
    half_heads = code_cand.shape[2]
    pre_axes = ("cand", "seq")

    log_prefix = jnp.log1p(-code_prefix.astype(jnp.float32) * 1e-06)
    own_total = jnp.sum(log_prefix, axis=0)
    totals = lax.all_gather(own_total, pre_axes)
    mine = lax.axis_index(pre_axes)
    shard_at = jnp.arange(totals.shape[0], dtype=jnp.int32)
    later_total = jnp.sum(jnp.where((shard_at > mine)[:, None], totals, 0.0), axis=0)
    after_local = own_total[None, :] - jnp.cumsum(log_prefix, axis=0)
    weight = jnp.exp(after_local + later_total[None, :])
    weighted_b = (weight[:, :, None] * b_prefix[:, None, :].astype(jnp.float32)).astype(
        jnp.bfloat16
    )
    x_heads = x_prefix.reshape(pre_len, heads_total, head_size)
    state_full = jnp.einsum("jhp,jhn->hpn", x_heads, weighted_b, preferred_element_type=jnp.float32)
    init_part = lax.psum_scatter(state_full, "seq", scatter_dimension=0, tiled=True)
    init_half = lax.psum(init_part, "cand").astype(jnp.bfloat16)

    position = jnp.arange(cand_len, dtype=jnp.int32)
    valid_rows = position[None, :] < lengths[:, None] * BLOCK
    g_cand = jnp.where(valid_rows[:, :, None], dy_cand, jnp.zeros_like(dy_cand))
    level_all = jnp.cumsum(jnp.log1p(-code_cand.astype(jnp.float32) * 1e-06), axis=1)
    amplitude = jnp.exp(level_all)
    inverse = jnp.exp(-level_all)
    g_heads = g_cand.reshape(cand_dev, cand_len, half_heads, head_size)
    xc_heads = x_cand.reshape(cand_dev, cand_len, half_heads, head_size)
    scaled_g = g_heads.astype(jnp.float32) * amplitude[:, :, :, None]
    decayed_g, g_low = split_bf16(scaled_g)
    x_high, x_low = split_bf16(xc_heads.astype(jnp.float32) * inverse[:, :, :, None])

    dstate = jnp.einsum("cthp,ctn->hpn", decayed_g, c_cand, preferred_element_type=jnp.float32)
    grad_half = lax.psum(dstate, "cand").astype(jnp.bfloat16)
    grad_state = lax.all_gather(grad_half, "seq", axis=0, tiled=True)

    causal = position[:, None] >= position[None, :]
    flat = (cand_dev, cand_len, half_width)

    def pair(left, right):
        return jnp.einsum(
            "ctk,csk->cts", left.reshape(flat), right.reshape(flat),
            preferred_element_type=jnp.float32,
        )

    weight_sum = pair(decayed_g, x_high) + pair(decayed_g, x_low) + pair(g_low, x_high)
    weight_sum = jnp.where(causal[None], weight_sum, 0.0)
    db_part = jnp.einsum(
        "cts,ctn->csn", weight_sum, c_cand.astype(jnp.float32), precision=lax.Precision.HIGHEST
    )
    dc_part = jnp.einsum(
        "cts,csn->ctn", weight_sum, b_cand.astype(jnp.float32), precision=lax.Precision.HIGHEST
    )

    scores = jnp.einsum("ctn,csn->cts", c_cand, b_cand, preferred_element_type=jnp.float32)
    amp_t = jnp.transpose(amplitude, (0, 2, 1))
    inv_t = jnp.transpose(inverse, (0, 2, 1))
    decay_mat = amp_t[:, :, :, None] * inv_t[:, :, None, :]
    kernel = jnp.where(causal[None, None], scores[:, None] * decay_mat, 0.0).astype(jnp.bfloat16)
    dx_cand = jnp.einsum("chts,cthp->cshp", kernel, g_heads, preferred_element_type=jnp.float32)
    dx_cand = dx_cand.astype(jnp.bfloat16).reshape(flat)

    dc_state = jnp.dot(
        decayed_g.reshape(cand_dev * cand_len, half_width),
        init_half.reshape(half_width, nstate),
        preferred_element_type=jnp.float32,
    )
    dc_total = dc_part + dc_state.reshape(cand_dev, cand_len, nstate)
    db_cand = lax.psum_scatter(db_part, "seq", scatter_dimension=1, tiled=True)
    dc_cand = lax.psum_scatter(dc_total, "seq", scatter_dimension=1, tiled=True)

    dx_prefix = jnp.einsum(
        "jhn,hpn->jhp", weighted_b, grad_state, preferred_element_type=jnp.float32
    )
    dx_prefix = dx_prefix.astype(jnp.bfloat16).reshape(pre_len, width)
    projected = jnp.einsum("jhp,hpn->jhn", x_heads, grad_state, preferred_element_type=jnp.float32)
    db_prefix = jnp.sum(projected * weight[:, :, None], axis=1)
    return (dx_prefix, db_prefix, dx_cand, db_cand, dc_cand)


def solution(mesh):
    return jax.shard_map(
        shards,
        mesh=mesh,
        in_specs=(
            P(("grp", "cand", "seq"), None),
            P(("grp", "cand", "seq"), None),
            P(("grp", "cand", "seq"), None),
            P(("grp", "cand"), None, "seq"),
            P(("grp", "cand"), None, None),
            P(("grp", "cand"), None, None),
            P(("grp", "cand"), None, "seq"),
            P(("grp", "cand")),
            P(("grp", "cand"), None, "seq"),
        ),
        out_specs=(
            P(("grp", "cand", "seq"), None),
            P(("grp", "cand", "seq"), None),
            P(("grp", "cand"), None, "seq"),
            P(("grp", "cand"), "seq", None),
            P(("grp", "cand"), "seq", None),
        ),
        check_vma=False,
    )
```

```python
import jax
import jax.numpy as jnp
from jax import lax
from jax.sharding import PartitionSpec as P

BLOCK = 256


def split_bf16(value):
    high = lax.reduce_precision(value, exponent_bits=8, mantissa_bits=7)
    low = (value - high).astype(jnp.bfloat16)
    return high.astype(jnp.bfloat16), low


def shards(x_prefix, b_prefix, code_prefix, x_cand, b_cand, c_cand, code_cand, lengths, dy_cand):
    pre_len, width = x_prefix.shape
    heads_total = code_prefix.shape[1]
    head_size = width // heads_total
    nstate = b_prefix.shape[1]
    cand_dev, cand_len, half_width = x_cand.shape
    half_heads = code_cand.shape[2]
    pre_axes = ("cand", "seq")

    log_prefix = jnp.log1p(-code_prefix.astype(jnp.float32) * 1e-06)
    own_total = jnp.sum(log_prefix, axis=0)
    shard_count = lax.axis_size(pre_axes)
    mine = lax.axis_index(pre_axes)
    shard_at = jnp.arange(shard_count, dtype=jnp.int32)
    rows = jnp.where((shard_at < mine)[:, None], own_total[None, :], 0.0)
    later_total = lax.psum_scatter(rows, pre_axes, scatter_dimension=0, tiled=True)[0]
    after_local = own_total[None, :] - jnp.cumsum(log_prefix, axis=0)
    weight = jnp.exp(after_local + later_total[None, :])
    weighted_b = (weight[:, :, None] * b_prefix[:, None, :].astype(jnp.float32)).astype(
        jnp.bfloat16
    )
    x_heads = x_prefix.reshape(pre_len, heads_total, head_size)
    state_full = jnp.einsum("jhp,jhn->hpn", x_heads, weighted_b, preferred_element_type=jnp.float32)
    cand_count = lax.axis_size("cand")
    seq_count = lax.axis_size("seq")
    piece = head_size // cand_count
    state_pieces = state_full.reshape(seq_count, half_heads, cand_count, piece, nstate)
    state_pieces = jnp.transpose(state_pieces, (2, 0, 1, 3, 4)).reshape(-1, piece, nstate)
    init_piece = lax.psum_scatter(state_pieces, pre_axes, scatter_dimension=0, tiled=True)
    init_pieces = lax.all_gather(init_piece.astype(jnp.bfloat16), "cand")
    init_half = jnp.transpose(init_pieces, (1, 0, 2, 3)).reshape(half_heads, head_size, nstate)

    position = jnp.arange(cand_len, dtype=jnp.int32)
    valid_rows = position[None, :] < lengths[:, None] * BLOCK
    g_cand = jnp.where(valid_rows[:, :, None], dy_cand, jnp.zeros_like(dy_cand))
    level_all = jnp.cumsum(jnp.log1p(-code_cand.astype(jnp.float32) * 1e-06), axis=1)
    amplitude = jnp.exp(level_all)
    inverse = jnp.exp(-level_all)
    g_heads = g_cand.reshape(cand_dev, cand_len, half_heads, head_size)
    xc_heads = x_cand.reshape(cand_dev, cand_len, half_heads, head_size)
    scaled_g = g_heads.astype(jnp.float32) * amplitude[:, :, :, None]
    decayed_g, g_low = split_bf16(scaled_g)
    x_high, x_low = split_bf16(xc_heads.astype(jnp.float32) * inverse[:, :, :, None])

    dstate = jnp.einsum("cthp,ctn->hpn", decayed_g, c_cand, preferred_element_type=jnp.float32)
    dstate_pieces = dstate.reshape(half_heads, cand_count, piece, nstate)
    dstate_pieces = jnp.transpose(dstate_pieces, (1, 0, 2, 3)).reshape(-1, piece, nstate)
    grad_piece = lax.psum_scatter(dstate_pieces, "cand", scatter_dimension=0, tiled=True)
    grad_pieces = lax.all_gather(grad_piece.astype(jnp.bfloat16), pre_axes)
    grad_pieces = grad_pieces.reshape(cand_count, seq_count, half_heads, piece, nstate)
    grad_state = jnp.transpose(grad_pieces, (1, 2, 0, 3, 4)).reshape(heads_total, head_size, nstate)

    causal = position[:, None] >= position[None, :]
    flat = (cand_dev, cand_len, half_width)

    def pair(left, right):
        return jnp.einsum(
            "ctk,csk->cts", left.reshape(flat), right.reshape(flat),
            preferred_element_type=jnp.float32,
        )

    weight_sum = pair(decayed_g, x_high) + pair(decayed_g, x_low) + pair(g_low, x_high)
    weight_sum = jnp.where(causal[None], weight_sum, 0.0)
    db_part = jnp.einsum(
        "cts,ctn->csn", weight_sum, c_cand.astype(jnp.float32), precision=lax.Precision.HIGHEST
    )
    dc_part = jnp.einsum(
        "cts,csn->ctn", weight_sum, b_cand.astype(jnp.float32), precision=lax.Precision.HIGHEST
    )

    scores = jnp.einsum("ctn,csn->cts", c_cand, b_cand, preferred_element_type=jnp.float32)
    amp_t = jnp.transpose(amplitude, (0, 2, 1))
    inv_t = jnp.transpose(inverse, (0, 2, 1))
    decay_mat = amp_t[:, :, :, None] * inv_t[:, :, None, :]
    kernel = jnp.where(causal[None, None], scores[:, None] * decay_mat, 0.0).astype(jnp.bfloat16)
    dx_cand = jnp.einsum("chts,cthp->cshp", kernel, g_heads, preferred_element_type=jnp.float32)
    dx_cand = dx_cand.astype(jnp.bfloat16).reshape(flat)

    dc_state = jnp.dot(
        decayed_g.reshape(cand_dev * cand_len, half_width),
        init_half.reshape(half_width, nstate),
        preferred_element_type=jnp.float32,
    )
    dc_total = dc_part + dc_state.reshape(cand_dev, cand_len, nstate)
    db_cand = lax.psum_scatter(db_part, "seq", scatter_dimension=1, tiled=True)
    dc_cand = lax.psum_scatter(dc_total, "seq", scatter_dimension=1, tiled=True)

    dx_prefix = jnp.einsum(
        "jhn,hpn->jhp", weighted_b, grad_state, preferred_element_type=jnp.float32
    )
    dx_prefix = dx_prefix.astype(jnp.bfloat16).reshape(pre_len, width)
    projected = jnp.einsum("jhp,hpn->jhn", x_heads, grad_state, preferred_element_type=jnp.float32)
    db_prefix = jnp.sum(projected * weight[:, :, None], axis=1)
    return (dx_prefix, db_prefix, dx_cand, db_cand, dc_cand)


def solution(mesh):
    return jax.shard_map(
        shards,
        mesh=mesh,
        in_specs=(
            P(("grp", "cand", "seq"), None),
            P(("grp", "cand", "seq"), None),
            P(("grp", "cand", "seq"), None),
            P(("grp", "cand"), None, "seq"),
            P(("grp", "cand"), None, None),
            P(("grp", "cand"), None, None),
            P(("grp", "cand"), None, "seq"),
            P(("grp", "cand")),
            P(("grp", "cand"), None, "seq"),
        ),
        out_specs=(
            P(("grp", "cand", "seq"), None),
            P(("grp", "cand", "seq"), None),
            P(("grp", "cand"), None, "seq"),
            P(("grp", "cand"), "seq", None),
            P(("grp", "cand"), "seq", None),
        ),
        check_vma=False,
    )
```

```python
import jax
import jax.numpy as jnp
from jax import lax
from jax.sharding import PartitionSpec as P

BLOCK = 256


def split_bf16(value):
    high = lax.reduce_precision(value, exponent_bits=8, mantissa_bits=7)
    low = (value - high).astype(jnp.bfloat16)
    return high.astype(jnp.bfloat16), low


def shards(x_prefix, b_prefix, code_prefix, x_cand, b_cand, c_cand, code_cand, lengths, dy_cand):
    pre_len, width = x_prefix.shape
    heads_total = code_prefix.shape[1]
    head_size = width // heads_total
    nstate = b_prefix.shape[1]
    cand_dev, cand_len, half_width = x_cand.shape
    half_heads = code_cand.shape[2]
    pre_axes = ("cand", "seq")

    log_prefix = jnp.log1p(-code_prefix.astype(jnp.float32) * 1e-06)
    own_total = jnp.sum(log_prefix, axis=0)
    shard_count = lax.axis_size(pre_axes)
    mine = lax.axis_index(pre_axes)
    shard_at = jnp.arange(shard_count, dtype=jnp.int32)
    lanes = -(-heads_total // 128) * 128
    padded = jnp.pad(own_total, (0, lanes - heads_total))
    rows = jnp.where((shard_at < mine)[:, None], padded[None, :], 0.0)
    rows = jnp.broadcast_to(rows[:, None, :], (shard_count, 8, lanes))
    later_total = lax.psum_scatter(rows, pre_axes, scatter_dimension=0, tiled=True)
    later_total = later_total[0, 0, :heads_total]
    after_local = own_total[None, :] - jnp.cumsum(log_prefix, axis=0)
    weight = jnp.exp(after_local + later_total[None, :])
    weighted_b = (weight[:, :, None] * b_prefix[:, None, :].astype(jnp.float32)).astype(
        jnp.bfloat16
    )
    x_heads = x_prefix.reshape(pre_len, heads_total, head_size)
    state_full = jnp.einsum("jhp,jhn->hpn", x_heads, weighted_b, preferred_element_type=jnp.float32)
    seq_at = lax.axis_index("seq")
    traced_zero = later_total[0] * 0.0
    init_full = lax.psum(state_full, pre_axes) + traced_zero
    init_half = lax.dynamic_slice_in_dim(init_full, seq_at * half_heads, half_heads, 0)
    init_half = init_half.astype(jnp.bfloat16)

    position = jnp.arange(cand_len, dtype=jnp.int32)
    valid_rows = position[None, :] < lengths[:, None] * BLOCK
    g_cand = jnp.where(valid_rows[:, :, None], dy_cand, jnp.zeros_like(dy_cand))
    level_all = jnp.cumsum(jnp.log1p(-code_cand.astype(jnp.float32) * 1e-06), axis=1)
    amplitude = jnp.exp(level_all)
    inverse = jnp.exp(-level_all)
    g_heads = g_cand.reshape(cand_dev, cand_len, half_heads, head_size)
    xc_heads = x_cand.reshape(cand_dev, cand_len, half_heads, head_size)
    scaled_g = g_heads.astype(jnp.float32) * amplitude[:, :, :, None]
    decayed_g, g_low = split_bf16(scaled_g)
    x_high, x_low = split_bf16(xc_heads.astype(jnp.float32) * inverse[:, :, :, None])

    dstate = jnp.einsum("cthp,ctn->hpn", decayed_g, c_cand, preferred_element_type=jnp.float32)
    grad_half = (lax.psum(dstate, "cand") + traced_zero).astype(jnp.bfloat16)
    grad_state = lax.all_gather(grad_half, "seq", axis=0, tiled=True)

    causal = position[:, None] >= position[None, :]
    flat = (cand_dev, cand_len, half_width)

    def pair(left, right):
        return jnp.einsum(
            "ctk,csk->cts", left.reshape(flat), right.reshape(flat),
            preferred_element_type=jnp.float32,
        )

    weight_sum = pair(decayed_g, x_high) + pair(decayed_g, x_low) + pair(g_low, x_high)
    weight_sum = jnp.where(causal[None], weight_sum, 0.0)
    db_part = jnp.einsum(
        "cts,ctn->csn", weight_sum, c_cand.astype(jnp.float32), precision=lax.Precision.HIGHEST
    )
    dc_part = jnp.einsum(
        "cts,csn->ctn", weight_sum, b_cand.astype(jnp.float32), precision=lax.Precision.HIGHEST
    )

    scores = jnp.einsum("ctn,csn->cts", c_cand, b_cand, preferred_element_type=jnp.float32)
    amp_t = jnp.transpose(amplitude, (0, 2, 1))
    inv_t = jnp.transpose(inverse, (0, 2, 1))
    decay_mat = amp_t[:, :, :, None] * inv_t[:, :, None, :]
    kernel = jnp.where(causal[None, None], scores[:, None] * decay_mat, 0.0).astype(jnp.bfloat16)
    dx_cand = jnp.einsum("chts,cthp->cshp", kernel, g_heads, preferred_element_type=jnp.float32)
    dx_cand = dx_cand.astype(jnp.bfloat16).reshape(flat)

    dc_state = jnp.dot(
        decayed_g.reshape(cand_dev * cand_len, half_width),
        init_half.reshape(half_width, nstate),
        preferred_element_type=jnp.float32,
    )
    dc_total = dc_part + dc_state.reshape(cand_dev, cand_len, nstate)
    db_cand = lax.psum_scatter(db_part, "seq", scatter_dimension=1, tiled=True)
    dc_cand = lax.psum_scatter(dc_total, "seq", scatter_dimension=1, tiled=True)

    dx_prefix = jnp.einsum(
        "jhn,hpn->jhp", weighted_b, grad_state, preferred_element_type=jnp.float32
    )
    dx_prefix = dx_prefix.astype(jnp.bfloat16).reshape(pre_len, width)
    projected = jnp.einsum("jhp,hpn->jhn", x_heads, grad_state, preferred_element_type=jnp.float32)
    db_prefix = jnp.sum(projected * weight[:, :, None], axis=1)
    return (dx_prefix, db_prefix, dx_cand, db_cand, dc_cand)


def solution(mesh):
    return jax.shard_map(
        shards,
        mesh=mesh,
        in_specs=(
            P(("grp", "cand", "seq"), None),
            P(("grp", "cand", "seq"), None),
            P(("grp", "cand", "seq"), None),
            P(("grp", "cand"), None, "seq"),
            P(("grp", "cand"), None, None),
            P(("grp", "cand"), None, None),
            P(("grp", "cand"), None, "seq"),
            P(("grp", "cand")),
            P(("grp", "cand"), None, "seq"),
        ),
        out_specs=(
            P(("grp", "cand", "seq"), None),
            P(("grp", "cand", "seq"), None),
            P(("grp", "cand"), None, "seq"),
            P(("grp", "cand"), "seq", None),
            P(("grp", "cand"), "seq", None),
        ),
        check_vma=False,
    )
```

```python
import jax
import jax.numpy as jnp
from jax import lax
from jax.sharding import PartitionSpec as P

BLOCK = 256


def split_bf16(value):
    high = lax.reduce_precision(value, exponent_bits=8, mantissa_bits=7)
    low = (value - high).astype(jnp.bfloat16)
    return high.astype(jnp.bfloat16), low


def butterfly_sum(value, axis):
    count = lax.axis_size(axis)
    step = 1
    while step < count:
        partner = [(at, at ^ step) for at in range(count)]
        value = value + lax.ppermute(value, axis, partner)
        step *= 2
    return value


def suffix_sum(value, axis):
    count = lax.axis_size(axis)
    step = 1
    while step < count:
        back = [(at, at - step) for at in range(step, count)]
        value = value + lax.ppermute(value, axis, back)
        step *= 2
    return value


def other_core(value):
    count = lax.axis_size("seq")
    return lax.ppermute(value, "seq", [(at, (at + 1) % count) for at in range(count)])


def shards(x_prefix, b_prefix, code_prefix, x_cand, b_cand, c_cand, code_cand, lengths, dy_cand):
    pre_len, width = x_prefix.shape
    heads_total = code_prefix.shape[1]
    head_size = width // heads_total
    nstate = b_prefix.shape[1]
    cand_dev, cand_len, half_width = x_cand.shape
    half_heads = code_cand.shape[2]
    pre_axes = ("cand", "seq")

    log_prefix = jnp.log1p(-code_prefix.astype(jnp.float32) * 1e-06)
    own_total = jnp.sum(log_prefix, axis=0)
    later_total = suffix_sum(own_total, pre_axes) - own_total
    after_local = own_total[None, :] - jnp.cumsum(log_prefix, axis=0)
    weight = jnp.exp(after_local + later_total[None, :])
    weighted_b = (weight[:, :, None] * b_prefix[:, None, :].astype(jnp.float32)).astype(
        jnp.bfloat16
    )
    x_heads = x_prefix.reshape(pre_len, heads_total, head_size)
    state_full = jnp.einsum("jhp,jhn->hpn", x_heads, weighted_b, preferred_element_type=jnp.float32)
    seq_at = lax.axis_index("seq")
    state_halves = state_full.reshape(2, half_heads, head_size, nstate)
    mine_first = seq_at == 0
    own_half = jnp.where(mine_first, state_halves[0], state_halves[1])
    give_half = jnp.where(mine_first, state_halves[1], state_halves[0])
    init_half = butterfly_sum(own_half + other_core(give_half), "cand").astype(jnp.bfloat16)

    position = jnp.arange(cand_len, dtype=jnp.int32)
    valid_rows = position[None, :] < lengths[:, None] * BLOCK
    g_cand = jnp.where(valid_rows[:, :, None], dy_cand, jnp.zeros_like(dy_cand))
    level_all = jnp.cumsum(jnp.log1p(-code_cand.astype(jnp.float32) * 1e-06), axis=1)
    amplitude = jnp.exp(level_all)
    inverse = jnp.exp(-level_all)
    g_heads = g_cand.reshape(cand_dev, cand_len, half_heads, head_size)
    xc_heads = x_cand.reshape(cand_dev, cand_len, half_heads, head_size)
    scaled_g = g_heads.astype(jnp.float32) * amplitude[:, :, :, None]
    decayed_g, g_low = split_bf16(scaled_g)
    x_high, x_low = split_bf16(xc_heads.astype(jnp.float32) * inverse[:, :, :, None])

    dstate = jnp.einsum("cthp,ctn->hpn", decayed_g, c_cand, preferred_element_type=jnp.float32)
    grad_half = butterfly_sum(dstate, "cand").astype(jnp.bfloat16)
    grad_other = other_core(grad_half)
    grad_state = jnp.where(
        mine_first,
        jnp.concatenate([grad_half, grad_other], axis=0),
        jnp.concatenate([grad_other, grad_half], axis=0),
    )

    causal = position[:, None] >= position[None, :]
    flat = (cand_dev, cand_len, half_width)

    def pair(left, right):
        return jnp.einsum(
            "ctk,csk->cts", left.reshape(flat), right.reshape(flat),
            preferred_element_type=jnp.float32,
        )

    weight_sum = pair(decayed_g, x_high) + pair(decayed_g, x_low) + pair(g_low, x_high)
    weight_sum = jnp.where(causal[None], weight_sum, 0.0)
    db_part = jnp.einsum(
        "cts,ctn->csn", weight_sum, c_cand.astype(jnp.float32), precision=lax.Precision.HIGHEST
    )
    dc_part = jnp.einsum(
        "cts,csn->ctn", weight_sum, b_cand.astype(jnp.float32), precision=lax.Precision.HIGHEST
    )

    scores = jnp.einsum("ctn,csn->cts", c_cand, b_cand, preferred_element_type=jnp.float32)
    amp_t = jnp.transpose(amplitude, (0, 2, 1))
    inv_t = jnp.transpose(inverse, (0, 2, 1))
    decay_mat = amp_t[:, :, :, None] * inv_t[:, :, None, :]
    kernel = jnp.where(causal[None, None], scores[:, None] * decay_mat, 0.0).astype(jnp.bfloat16)
    dx_cand = jnp.einsum("chts,cthp->cshp", kernel, g_heads, preferred_element_type=jnp.float32)
    dx_cand = dx_cand.astype(jnp.bfloat16).reshape(flat)

    dc_state = jnp.dot(
        decayed_g.reshape(cand_dev * cand_len, half_width),
        init_half.reshape(half_width, nstate),
        preferred_element_type=jnp.float32,
    )
    dc_total = dc_part + dc_state.reshape(cand_dev, cand_len, nstate)
    def token_half_sum(part):
        halves = part.reshape(cand_dev, 2, cand_len // 2, nstate)
        own = jnp.where(mine_first, halves[:, 0], halves[:, 1])
        give = jnp.where(mine_first, halves[:, 1], halves[:, 0])
        return own + other_core(give)

    db_cand = token_half_sum(db_part)
    dc_cand = token_half_sum(dc_total)

    dx_prefix = jnp.einsum(
        "jhn,hpn->jhp", weighted_b, grad_state, preferred_element_type=jnp.float32
    )
    dx_prefix = dx_prefix.astype(jnp.bfloat16).reshape(pre_len, width)
    projected = jnp.einsum("jhp,hpn->jhn", x_heads, grad_state, preferred_element_type=jnp.float32)
    db_prefix = jnp.sum(projected * weight[:, :, None], axis=1)
    return (dx_prefix, db_prefix, dx_cand, db_cand, dc_cand)


def solution(mesh):
    return jax.shard_map(
        shards,
        mesh=mesh,
        in_specs=(
            P(("grp", "cand", "seq"), None),
            P(("grp", "cand", "seq"), None),
            P(("grp", "cand", "seq"), None),
            P(("grp", "cand"), None, "seq"),
            P(("grp", "cand"), None, None),
            P(("grp", "cand"), None, None),
            P(("grp", "cand"), None, "seq"),
            P(("grp", "cand")),
            P(("grp", "cand"), None, "seq"),
        ),
        out_specs=(
            P(("grp", "cand", "seq"), None),
            P(("grp", "cand", "seq"), None),
            P(("grp", "cand"), None, "seq"),
            P(("grp", "cand"), "seq", None),
            P(("grp", "cand"), "seq", None),
        ),
        check_vma=False,
    )
```

```python
import jax
import jax.numpy as jnp
from jax import lax
from jax.sharding import PartitionSpec as P

BLOCK = 256


def split_bf16(value):
    high = lax.reduce_precision(value, exponent_bits=8, mantissa_bits=7)
    low = (value - high).astype(jnp.bfloat16)
    return high.astype(jnp.bfloat16), low


def butterfly_sum(value, axis):
    count = lax.axis_size(axis)
    step = 1
    while step < count:
        partner = [(at, at ^ step) for at in range(count)]
        value = value + lax.ppermute(value, axis, partner)
        step *= 2
    return value


def suffix_sum(value, axis):
    count = lax.axis_size(axis)
    step = 1
    while step < count:
        back = [(at, at - step) for at in range(step, count)]
        value = value + lax.ppermute(value, axis, back)
        step *= 2
    return value


def halving_scatter(blocks, axis):
    count = lax.axis_size(axis)
    me = lax.axis_index(axis)
    rest = blocks.shape[1:]
    value = blocks
    step = count // 2
    while step >= 1:
        value = value.reshape((2, -1) + rest)
        upper = me // step % 2 == 1
        keep = jnp.where(upper, value[1], value[0])
        give = jnp.where(upper, value[0], value[1])
        value = keep + lax.ppermute(give, axis, [(at, at ^ step) for at in range(count)])
        step //= 2
    return value[0]


def doubling_gather(piece, axis):
    count = lax.axis_size(axis)
    me = lax.axis_index(axis)
    value = piece[None]
    step = 1
    while step < count:
        other = lax.ppermute(value, axis, [(at, at ^ step) for at in range(count)])
        upper = me // step % 2 == 1
        value = jnp.where(
            upper, jnp.concatenate([other, value]), jnp.concatenate([value, other])
        )
        step *= 2
    return value


def cand_sum_bf16(state):
    heads, size, width = state.shape
    count = lax.axis_size("cand")
    piece = size // count
    blocks = jnp.transpose(state.reshape(heads, count, piece, width), (1, 0, 2, 3))
    summed = halving_scatter(blocks, "cand").astype(jnp.bfloat16)
    gathered = doubling_gather(summed, "cand")
    return jnp.transpose(gathered, (1, 0, 2, 3)).reshape(heads, size, width)


def other_core(value):
    count = lax.axis_size("seq")
    return lax.ppermute(value, "seq", [(at, (at + 1) % count) for at in range(count)])


def shards(x_prefix, b_prefix, code_prefix, x_cand, b_cand, c_cand, code_cand, lengths, dy_cand):
    pre_len, width = x_prefix.shape
    heads_total = code_prefix.shape[1]
    head_size = width // heads_total
    nstate = b_prefix.shape[1]
    cand_dev, cand_len, half_width = x_cand.shape
    half_heads = code_cand.shape[2]
    pre_axes = ("cand", "seq")

    log_prefix = jnp.log1p(-code_prefix.astype(jnp.float32) * 1e-06)
    own_total = jnp.sum(log_prefix, axis=0)
    later_total = suffix_sum(own_total, pre_axes) - own_total
    after_local = own_total[None, :] - jnp.cumsum(log_prefix, axis=0)
    weight = jnp.exp(after_local + later_total[None, :])
    weighted_b = (weight[:, :, None] * b_prefix[:, None, :].astype(jnp.float32)).astype(
        jnp.bfloat16
    )
    x_heads = x_prefix.reshape(pre_len, heads_total, head_size)
    state_full = jnp.einsum("jhp,jhn->hpn", x_heads, weighted_b, preferred_element_type=jnp.float32)
    seq_at = lax.axis_index("seq")
    state_halves = state_full.reshape(2, half_heads, head_size, nstate)
    mine_first = seq_at == 0
    own_half = jnp.where(mine_first, state_halves[0], state_halves[1])
    give_half = jnp.where(mine_first, state_halves[1], state_halves[0])
    init_half = cand_sum_bf16(own_half + other_core(give_half))

    position = jnp.arange(cand_len, dtype=jnp.int32)
    valid_rows = position[None, :] < lengths[:, None] * BLOCK
    g_cand = jnp.where(valid_rows[:, :, None], dy_cand, jnp.zeros_like(dy_cand))
    level_all = jnp.cumsum(jnp.log1p(-code_cand.astype(jnp.float32) * 1e-06), axis=1)
    amplitude = jnp.exp(level_all)
    inverse = jnp.exp(-level_all)
    g_heads = g_cand.reshape(cand_dev, cand_len, half_heads, head_size)
    xc_heads = x_cand.reshape(cand_dev, cand_len, half_heads, head_size)
    scaled_g = g_heads.astype(jnp.float32) * amplitude[:, :, :, None]
    decayed_g, g_low = split_bf16(scaled_g)
    x_high, x_low = split_bf16(xc_heads.astype(jnp.float32) * inverse[:, :, :, None])

    dstate = jnp.einsum("cthp,ctn->hpn", decayed_g, c_cand, preferred_element_type=jnp.float32)
    grad_half = cand_sum_bf16(dstate)
    grad_other = other_core(grad_half)
    grad_state = jnp.where(
        mine_first,
        jnp.concatenate([grad_half, grad_other], axis=0),
        jnp.concatenate([grad_other, grad_half], axis=0),
    )

    causal = position[:, None] >= position[None, :]
    flat = (cand_dev, cand_len, half_width)

    def pair(left, right):
        return jnp.einsum(
            "ctk,csk->cts", left.reshape(flat), right.reshape(flat),
            preferred_element_type=jnp.float32,
        )

    weight_sum = pair(decayed_g, x_high) + pair(decayed_g, x_low) + pair(g_low, x_high)
    weight_sum = jnp.where(causal[None], weight_sum, 0.0)
    db_part = jnp.einsum(
        "cts,ctn->csn", weight_sum, c_cand.astype(jnp.float32), precision=lax.Precision.HIGHEST
    )
    dc_part = jnp.einsum(
        "cts,csn->ctn", weight_sum, b_cand.astype(jnp.float32), precision=lax.Precision.HIGHEST
    )

    scores = jnp.einsum("ctn,csn->cts", c_cand, b_cand, preferred_element_type=jnp.float32)
    amp_t = jnp.transpose(amplitude, (0, 2, 1))
    inv_t = jnp.transpose(inverse, (0, 2, 1))
    decay_mat = amp_t[:, :, :, None] * inv_t[:, :, None, :]
    kernel = jnp.where(causal[None, None], scores[:, None] * decay_mat, 0.0).astype(jnp.bfloat16)
    dx_cand = jnp.einsum("chts,cthp->cshp", kernel, g_heads, preferred_element_type=jnp.float32)
    dx_cand = dx_cand.astype(jnp.bfloat16).reshape(flat)

    dc_state = jnp.dot(
        decayed_g.reshape(cand_dev * cand_len, half_width),
        init_half.reshape(half_width, nstate),
        preferred_element_type=jnp.float32,
    )
    dc_total = dc_part + dc_state.reshape(cand_dev, cand_len, nstate)
    def token_half_sum(part):
        halves = part.reshape(cand_dev, 2, cand_len // 2, nstate)
        own = jnp.where(mine_first, halves[:, 0], halves[:, 1])
        give = jnp.where(mine_first, halves[:, 1], halves[:, 0])
        return own + other_core(give)

    db_cand = token_half_sum(db_part)
    dc_cand = token_half_sum(dc_total)

    dx_prefix = jnp.einsum(
        "jhn,hpn->jhp", weighted_b, grad_state, preferred_element_type=jnp.float32
    )
    dx_prefix = dx_prefix.astype(jnp.bfloat16).reshape(pre_len, width)
    projected = jnp.einsum("jhp,hpn->jhn", x_heads, grad_state, preferred_element_type=jnp.float32)
    db_prefix = jnp.sum(projected * weight[:, :, None], axis=1)
    return (dx_prefix, db_prefix, dx_cand, db_cand, dc_cand)


def solution(mesh):
    return jax.shard_map(
        shards,
        mesh=mesh,
        in_specs=(
            P(("grp", "cand", "seq"), None),
            P(("grp", "cand", "seq"), None),
            P(("grp", "cand", "seq"), None),
            P(("grp", "cand"), None, "seq"),
            P(("grp", "cand"), None, None),
            P(("grp", "cand"), None, None),
            P(("grp", "cand"), None, "seq"),
            P(("grp", "cand")),
            P(("grp", "cand"), None, "seq"),
        ),
        out_specs=(
            P(("grp", "cand", "seq"), None),
            P(("grp", "cand", "seq"), None),
            P(("grp", "cand"), None, "seq"),
            P(("grp", "cand"), "seq", None),
            P(("grp", "cand"), "seq", None),
        ),
        check_vma=False,
    )
```

```python
import jax
import jax.numpy as jnp
from jax import lax
from jax.sharding import PartitionSpec as P

BLOCK = 256


def split_bf16(value):
    high = lax.reduce_precision(value, exponent_bits=8, mantissa_bits=7)
    low = (value - high).astype(jnp.bfloat16)
    return high.astype(jnp.bfloat16), low


def butterfly_sum(value, axis):
    count = lax.axis_size(axis)
    step = 1
    while step < count:
        partner = [(at, at ^ step) for at in range(count)]
        value = value + lax.ppermute(value, axis, partner)
        step *= 2
    return value


def suffix_sum(value, axis):
    count = lax.axis_size(axis)
    step = 1
    while step < count:
        back = [(at, at - step) for at in range(step, count)]
        value = value + lax.ppermute(value, axis, back)
        step *= 2
    return value


def halving_scatter(blocks, axis):
    count = lax.axis_size(axis)
    me = lax.axis_index(axis)
    rest = blocks.shape[1:]
    value = blocks
    step = count // 2
    while step >= 1:
        value = value.reshape((2, -1) + rest)
        upper = me // step % 2 == 1
        keep = jnp.where(upper, value[1], value[0])
        give = jnp.where(upper, value[0], value[1])
        value = keep + lax.ppermute(give, axis, [(at, at ^ step) for at in range(count)])
        step //= 2
    return value[0]


def doubling_gather(piece, axis):
    count = lax.axis_size(axis)
    me = lax.axis_index(axis)
    value = piece[None]
    step = 1
    while step < count:
        other = lax.ppermute(value, axis, [(at, at ^ step) for at in range(count)])
        upper = me // step % 2 == 1
        value = jnp.where(
            upper, jnp.concatenate([other, value]), jnp.concatenate([value, other])
        )
        step *= 2
    return value


def cand_sum_bf16(state):
    heads, size, width = state.shape
    count = lax.axis_size("cand")
    piece = size // count
    blocks = jnp.transpose(state.reshape(heads, count, piece, width), (1, 0, 2, 3))
    summed = halving_scatter(blocks, "cand").astype(jnp.bfloat16)
    gathered = doubling_gather(summed, "cand")
    return jnp.transpose(gathered, (1, 0, 2, 3)).reshape(heads, size, width)


def other_core(value):
    count = lax.axis_size("seq")
    return lax.ppermute(value, "seq", [(at, (at + 1) % count) for at in range(count)])


def shards(x_prefix, b_prefix, code_prefix, x_cand, b_cand, c_cand, code_cand, lengths, dy_cand):
    pre_len, width = x_prefix.shape
    heads_total = code_prefix.shape[1]
    head_size = width // heads_total
    nstate = b_prefix.shape[1]
    cand_dev, cand_len, half_width = x_cand.shape
    half_heads = code_cand.shape[2]
    pre_axes = ("cand", "seq")

    log_prefix = jnp.log1p(-code_prefix.astype(jnp.float32) * 1e-06)
    own_total = jnp.sum(log_prefix, axis=0)
    later_total = suffix_sum(own_total, pre_axes) - own_total
    after_local = own_total[None, :] - jnp.cumsum(log_prefix, axis=0)
    weight = jnp.exp(after_local + later_total[None, :])
    weighted_b = (weight[:, :, None] * b_prefix[:, None, :].astype(jnp.float32)).astype(
        jnp.bfloat16
    )
    x_heads = x_prefix.reshape(pre_len, heads_total, head_size)
    state_full = jnp.einsum("jhp,jhn->hpn", x_heads, weighted_b, preferred_element_type=jnp.float32)
    seq_at = lax.axis_index("seq")
    state_halves = state_full.reshape(2, half_heads, head_size, nstate)
    mine_first = seq_at == 0
    own_half = jnp.where(mine_first, state_halves[0], state_halves[1])
    give_half = jnp.where(mine_first, state_halves[1], state_halves[0])
    init_local = own_half + other_core(give_half)

    position = jnp.arange(cand_len, dtype=jnp.int32)
    valid_rows = position[None, :] < lengths[:, None] * BLOCK
    g_cand = jnp.where(valid_rows[:, :, None], dy_cand, jnp.zeros_like(dy_cand))
    level_all = jnp.cumsum(jnp.log1p(-code_cand.astype(jnp.float32) * 1e-06), axis=1)
    amplitude = jnp.exp(level_all)
    inverse = jnp.exp(-level_all)
    g_heads = g_cand.reshape(cand_dev, cand_len, half_heads, head_size)
    xc_heads = x_cand.reshape(cand_dev, cand_len, half_heads, head_size)
    scaled_g = g_heads.astype(jnp.float32) * amplitude[:, :, :, None]
    decayed_g, g_low = split_bf16(scaled_g)
    x_high, x_low = split_bf16(xc_heads.astype(jnp.float32) * inverse[:, :, :, None])

    dstate = jnp.einsum("cthp,ctn->hpn", decayed_g, c_cand, preferred_element_type=jnp.float32)
    both = cand_sum_bf16(jnp.concatenate([init_local, dstate], axis=0))
    init_half, grad_half = both[:half_heads], both[half_heads:]
    grad_other = other_core(grad_half)
    grad_state = jnp.where(
        mine_first,
        jnp.concatenate([grad_half, grad_other], axis=0),
        jnp.concatenate([grad_other, grad_half], axis=0),
    )

    causal = position[:, None] >= position[None, :]
    flat = (cand_dev, cand_len, half_width)

    def pair(left, right):
        return jnp.einsum(
            "ctk,csk->cts", left.reshape(flat), right.reshape(flat),
            preferred_element_type=jnp.float32,
        )

    weight_sum = pair(decayed_g, x_high) + pair(decayed_g, x_low) + pair(g_low, x_high)
    weight_sum = jnp.where(causal[None], weight_sum, 0.0)
    db_part = jnp.einsum(
        "cts,ctn->csn", weight_sum, c_cand.astype(jnp.float32), precision=lax.Precision.HIGHEST
    )
    dc_part = jnp.einsum(
        "cts,csn->ctn", weight_sum, b_cand.astype(jnp.float32), precision=lax.Precision.HIGHEST
    )

    scores = jnp.einsum("ctn,csn->cts", c_cand, b_cand, preferred_element_type=jnp.float32)
    amp_t = jnp.transpose(amplitude, (0, 2, 1))
    inv_t = jnp.transpose(inverse, (0, 2, 1))
    decay_mat = amp_t[:, :, :, None] * inv_t[:, :, None, :]
    kernel = jnp.where(causal[None, None], scores[:, None] * decay_mat, 0.0).astype(jnp.bfloat16)
    dx_cand = jnp.einsum("chts,cthp->cshp", kernel, g_heads, preferred_element_type=jnp.float32)
    dx_cand = dx_cand.astype(jnp.bfloat16).reshape(flat)

    dc_state = jnp.dot(
        decayed_g.reshape(cand_dev * cand_len, half_width),
        init_half.reshape(half_width, nstate),
        preferred_element_type=jnp.float32,
    )
    dc_total = dc_part + dc_state.reshape(cand_dev, cand_len, nstate)
    def token_half_sum(part):
        halves = part.reshape(cand_dev, 2, cand_len // 2, part.shape[2])
        own = jnp.where(mine_first, halves[:, 0], halves[:, 1])
        give = jnp.where(mine_first, halves[:, 1], halves[:, 0])
        return own + other_core(give)

    db_dc = token_half_sum(jnp.concatenate([db_part, dc_total], axis=2))
    db_cand, dc_cand = db_dc[:, :, :nstate], db_dc[:, :, nstate:]

    dx_prefix = jnp.einsum(
        "jhn,hpn->jhp", weighted_b, grad_state, preferred_element_type=jnp.float32
    )
    dx_prefix = dx_prefix.astype(jnp.bfloat16).reshape(pre_len, width)
    projected = jnp.einsum("jhp,hpn->jhn", x_heads, grad_state, preferred_element_type=jnp.float32)
    db_prefix = jnp.sum(projected * weight[:, :, None], axis=1)
    return (dx_prefix, db_prefix, dx_cand, db_cand, dc_cand)


def solution(mesh):
    return jax.shard_map(
        shards,
        mesh=mesh,
        in_specs=(
            P(("grp", "cand", "seq"), None),
            P(("grp", "cand", "seq"), None),
            P(("grp", "cand", "seq"), None),
            P(("grp", "cand"), None, "seq"),
            P(("grp", "cand"), None, None),
            P(("grp", "cand"), None, None),
            P(("grp", "cand"), None, "seq"),
            P(("grp", "cand")),
            P(("grp", "cand"), None, "seq"),
        ),
        out_specs=(
            P(("grp", "cand", "seq"), None),
            P(("grp", "cand", "seq"), None),
            P(("grp", "cand"), None, "seq"),
            P(("grp", "cand"), "seq", None),
            P(("grp", "cand"), "seq", None),
        ),
        check_vma=False,
    )
```

```python
import jax
import jax.numpy as jnp
from jax import lax
from jax.sharding import PartitionSpec as P

BLOCK = 256


def split_bf16(value):
    high = lax.reduce_precision(value, exponent_bits=8, mantissa_bits=7)
    low = (value - high).astype(jnp.bfloat16)
    return high.astype(jnp.bfloat16), low


def butterfly_sum(value, axis):
    count = lax.axis_size(axis)
    step = 1
    while step < count:
        partner = [(at, at ^ step) for at in range(count)]
        value = value + lax.ppermute(value, axis, partner)
        step *= 2
    return value


def suffix_sum(value, axis):
    count = lax.axis_size(axis)
    step = 1
    while step < count:
        back = [(at, at - step) for at in range(step, count)]
        value = value + lax.ppermute(value, axis, back)
        step *= 2
    return value


def bit_order(value, count, first_bits):
    nbits = count.bit_length() - 1
    rest = value.shape[1:]
    value = value.reshape((2,) * nbits + rest)
    axes = [nbits - 1 - bit for bit in first_bits]
    value = jnp.transpose(value, axes + list(range(nbits, nbits + len(rest))))
    return value.reshape((count,) + rest)


def halving_scatter(blocks, axis):
    count = lax.axis_size(axis)
    me = lax.axis_index(axis)
    rest = blocks.shape[1:]
    nbits = count.bit_length() - 1
    value = bit_order(blocks, count, list(range(nbits)))
    for bit in range(nbits):
        step = 1 << bit
        value = value.reshape((2, -1) + rest)
        upper = me // step % 2 == 1
        keep = jnp.where(upper, value[1], value[0])
        give = jnp.where(upper, value[0], value[1])
        value = keep + lax.ppermute(give, axis, [(at, at ^ step) for at in range(count)])
    return value[0]


def doubling_gather(piece, axis):
    count = lax.axis_size(axis)
    me = lax.axis_index(axis)
    nbits = count.bit_length() - 1
    value = piece[None]
    for bit in reversed(range(nbits)):
        step = 1 << bit
        other = lax.ppermute(value, axis, [(at, at ^ step) for at in range(count)])
        upper = me // step % 2 == 1
        value = jnp.where(
            upper, jnp.concatenate([other, value]), jnp.concatenate([value, other])
        )
    rest = piece.shape
    value = value.reshape((2,) * nbits + rest)
    axes = list(reversed(range(nbits)))
    value = jnp.transpose(value, axes + list(range(nbits, nbits + len(rest))))
    return value.reshape((count,) + rest)


def cand_sum_bf16(state):
    heads, size, width = state.shape
    count = lax.axis_size("cand")
    piece = size // count
    blocks = jnp.transpose(state.reshape(heads, count, piece, width), (1, 0, 2, 3))
    summed = halving_scatter(blocks, "cand").astype(jnp.bfloat16)
    gathered = doubling_gather(summed, "cand")
    return jnp.transpose(gathered, (1, 0, 2, 3)).reshape(heads, size, width)


def other_core(value):
    count = lax.axis_size("seq")
    return lax.ppermute(value, "seq", [(at, (at + 1) % count) for at in range(count)])


def shards(x_prefix, b_prefix, code_prefix, x_cand, b_cand, c_cand, code_cand, lengths, dy_cand):
    pre_len, width = x_prefix.shape
    heads_total = code_prefix.shape[1]
    head_size = width // heads_total
    nstate = b_prefix.shape[1]
    cand_dev, cand_len, half_width = x_cand.shape
    half_heads = code_cand.shape[2]
    pre_axes = ("cand", "seq")

    log_prefix = jnp.log1p(-code_prefix.astype(jnp.float32) * 1e-06)
    own_total = jnp.sum(log_prefix, axis=0)
    later_total = suffix_sum(own_total, pre_axes) - own_total
    after_local = own_total[None, :] - jnp.cumsum(log_prefix, axis=0)
    weight = jnp.exp(after_local + later_total[None, :])
    weighted_b = (weight[:, :, None] * b_prefix[:, None, :].astype(jnp.float32)).astype(
        jnp.bfloat16
    )
    x_heads = x_prefix.reshape(pre_len, heads_total, head_size)
    state_full = jnp.einsum("jhp,jhn->hpn", x_heads, weighted_b, preferred_element_type=jnp.float32)
    seq_at = lax.axis_index("seq")
    state_halves = state_full.reshape(2, half_heads, head_size, nstate)
    mine_first = seq_at == 0
    own_half = jnp.where(mine_first, state_halves[0], state_halves[1])
    give_half = jnp.where(mine_first, state_halves[1], state_halves[0])
    init_local = own_half + other_core(give_half)

    position = jnp.arange(cand_len, dtype=jnp.int32)
    valid_rows = position[None, :] < lengths[:, None] * BLOCK
    g_cand = jnp.where(valid_rows[:, :, None], dy_cand, jnp.zeros_like(dy_cand))
    level_all = jnp.cumsum(jnp.log1p(-code_cand.astype(jnp.float32) * 1e-06), axis=1)
    amplitude = jnp.exp(level_all)
    inverse = jnp.exp(-level_all)
    g_heads = g_cand.reshape(cand_dev, cand_len, half_heads, head_size)
    xc_heads = x_cand.reshape(cand_dev, cand_len, half_heads, head_size)
    scaled_g = g_heads.astype(jnp.float32) * amplitude[:, :, :, None]
    decayed_g, g_low = split_bf16(scaled_g)
    x_high, x_low = split_bf16(xc_heads.astype(jnp.float32) * inverse[:, :, :, None])

    dstate = jnp.einsum("cthp,ctn->hpn", decayed_g, c_cand, preferred_element_type=jnp.float32)
    both = cand_sum_bf16(jnp.concatenate([init_local, dstate], axis=0))
    init_half, grad_half = both[:half_heads], both[half_heads:]
    grad_other = other_core(grad_half)
    grad_state = jnp.where(
        mine_first,
        jnp.concatenate([grad_half, grad_other], axis=0),
        jnp.concatenate([grad_other, grad_half], axis=0),
    )

    causal = position[:, None] >= position[None, :]
    flat = (cand_dev, cand_len, half_width)

    def pair(left, right):
        return jnp.einsum(
            "ctk,csk->cts", left.reshape(flat), right.reshape(flat),
            preferred_element_type=jnp.float32,
        )

    weight_sum = pair(decayed_g, x_high) + pair(decayed_g, x_low) + pair(g_low, x_high)
    weight_sum = jnp.where(causal[None], weight_sum, 0.0)
    db_part = jnp.einsum(
        "cts,ctn->csn", weight_sum, c_cand.astype(jnp.float32), precision=lax.Precision.HIGHEST
    )
    dc_part = jnp.einsum(
        "cts,csn->ctn", weight_sum, b_cand.astype(jnp.float32), precision=lax.Precision.HIGHEST
    )

    scores = jnp.einsum("ctn,csn->cts", c_cand, b_cand, preferred_element_type=jnp.float32)
    amp_t = jnp.transpose(amplitude, (0, 2, 1))
    inv_t = jnp.transpose(inverse, (0, 2, 1))
    decay_mat = amp_t[:, :, :, None] * inv_t[:, :, None, :]
    kernel = jnp.where(causal[None, None], scores[:, None] * decay_mat, 0.0).astype(jnp.bfloat16)
    dx_cand = jnp.einsum("chts,cthp->cshp", kernel, g_heads, preferred_element_type=jnp.float32)
    dx_cand = dx_cand.astype(jnp.bfloat16).reshape(flat)

    dc_state = jnp.dot(
        decayed_g.reshape(cand_dev * cand_len, half_width),
        init_half.reshape(half_width, nstate),
        preferred_element_type=jnp.float32,
    )
    dc_total = dc_part + dc_state.reshape(cand_dev, cand_len, nstate)
    def token_half_sum(part):
        halves = part.reshape(cand_dev, 2, cand_len // 2, part.shape[2])
        own = jnp.where(mine_first, halves[:, 0], halves[:, 1])
        give = jnp.where(mine_first, halves[:, 1], halves[:, 0])
        return own + other_core(give)

    db_dc = token_half_sum(jnp.concatenate([db_part, dc_total], axis=2))
    db_cand, dc_cand = db_dc[:, :, :nstate], db_dc[:, :, nstate:]

    dx_prefix = jnp.einsum(
        "jhn,hpn->jhp", weighted_b, grad_state, preferred_element_type=jnp.float32
    )
    dx_prefix = dx_prefix.astype(jnp.bfloat16).reshape(pre_len, width)
    projected = jnp.einsum("jhp,hpn->jhn", x_heads, grad_state, preferred_element_type=jnp.float32)
    db_prefix = jnp.sum(projected * weight[:, :, None], axis=1)
    return (dx_prefix, db_prefix, dx_cand, db_cand, dc_cand)


def solution(mesh):
    return jax.shard_map(
        shards,
        mesh=mesh,
        in_specs=(
            P(("grp", "cand", "seq"), None),
            P(("grp", "cand", "seq"), None),
            P(("grp", "cand", "seq"), None),
            P(("grp", "cand"), None, "seq"),
            P(("grp", "cand"), None, None),
            P(("grp", "cand"), None, None),
            P(("grp", "cand"), None, "seq"),
            P(("grp", "cand")),
            P(("grp", "cand"), None, "seq"),
        ),
        out_specs=(
            P(("grp", "cand", "seq"), None),
            P(("grp", "cand", "seq"), None),
            P(("grp", "cand"), None, "seq"),
            P(("grp", "cand"), "seq", None),
            P(("grp", "cand"), "seq", None),
        ),
        check_vma=False,
    )
```

```python
import jax
import jax.numpy as jnp
from jax import lax
from jax.sharding import PartitionSpec as P

BLOCK = 256


def split_bf16(value):
    high = lax.reduce_precision(value, exponent_bits=8, mantissa_bits=7)
    low = (value - high).astype(jnp.bfloat16)
    return high.astype(jnp.bfloat16), low


def butterfly_sum(value, axis):
    count = lax.axis_size(axis)
    step = 1
    while step < count:
        partner = [(at, at ^ step) for at in range(count)]
        value = value + lax.ppermute(value, axis, partner)
        step *= 2
    return value


def suffix_sum(value, axis, works):
    count = lax.axis_size(axis)
    step = 1
    done = []
    rounds = 0
    while step < count:
        back = [(at, at - step) for at in range(step, count)]
        if rounds < len(works):
            fn, args = works[rounds]
            value, args = lax.optimization_barrier((value, args))
        value = value + lax.ppermute(value, axis, back)
        if rounds < len(works):
            value, piece = lax.optimization_barrier((value, fn(*args)))
            done.append(piece)
        step *= 2
        rounds += 1
    return value, done


def bit_order(value, count, first_bits):
    nbits = count.bit_length() - 1
    rest = value.shape[1:]
    value = value.reshape((2,) * nbits + rest)
    axes = [nbits - 1 - bit for bit in first_bits]
    value = jnp.transpose(value, axes + list(range(nbits, nbits + len(rest))))
    return value.reshape((count,) + rest)


def halving_scatter(blocks, axis):
    count = lax.axis_size(axis)
    me = lax.axis_index(axis)
    rest = blocks.shape[1:]
    nbits = count.bit_length() - 1
    value = bit_order(blocks, count, list(range(nbits)))
    for bit in range(nbits):
        step = 1 << bit
        value = value.reshape((2, -1) + rest)
        upper = me // step % 2 == 1
        keep = jnp.where(upper, value[1], value[0])
        give = jnp.where(upper, value[0], value[1])
        value = keep + lax.ppermute(give, axis, [(at, at ^ step) for at in range(count)])
    return value[0]


def doubling_gather(piece, axis):
    count = lax.axis_size(axis)
    me = lax.axis_index(axis)
    nbits = count.bit_length() - 1
    value = piece[None]
    for bit in reversed(range(nbits)):
        step = 1 << bit
        other = lax.ppermute(value, axis, [(at, at ^ step) for at in range(count)])
        upper = me // step % 2 == 1
        value = jnp.where(
            upper, jnp.concatenate([other, value]), jnp.concatenate([value, other])
        )
    rest = piece.shape
    value = value.reshape((2,) * nbits + rest)
    axes = list(reversed(range(nbits)))
    value = jnp.transpose(value, axes + list(range(nbits, nbits + len(rest))))
    return value.reshape((count,) + rest)


def cand_sum_bf16(state):
    heads, size, width = state.shape
    count = lax.axis_size("cand")
    piece = size // count
    blocks = jnp.transpose(state.reshape(heads, count, piece, width), (1, 0, 2, 3))
    summed = halving_scatter(blocks, "cand").astype(jnp.bfloat16)
    gathered = doubling_gather(summed, "cand")
    return jnp.transpose(gathered, (1, 0, 2, 3)).reshape(heads, size, width)


def other_core(value):
    count = lax.axis_size("seq")
    return lax.ppermute(value, "seq", [(at, (at + 1) % count) for at in range(count)])


def shards(x_prefix, b_prefix, code_prefix, x_cand, b_cand, c_cand, code_cand, lengths, dy_cand):
    pre_len, width = x_prefix.shape
    heads_total = code_prefix.shape[1]
    head_size = width // heads_total
    nstate = b_prefix.shape[1]
    cand_dev, cand_len, half_width = x_cand.shape
    half_heads = code_cand.shape[2]
    pre_axes = ("cand", "seq")

    log_prefix = jnp.log1p(-code_prefix.astype(jnp.float32) * 1e-06)
    own_total = jnp.sum(log_prefix, axis=0)
    position = jnp.arange(cand_len, dtype=jnp.int32)

    def level_work(code_cand):
        level_all = jnp.cumsum(jnp.log1p(-code_cand.astype(jnp.float32) * 1e-06), axis=1)
        return jnp.exp(level_all), jnp.exp(-level_all)

    def g_work(dy_cand, lengths):
        valid_rows = position[None, :] < lengths[:, None] * BLOCK
        g_cand = jnp.where(valid_rows[:, :, None], dy_cand, jnp.zeros_like(dy_cand))
        return g_cand.reshape(cand_dev, cand_len, half_heads, head_size)

    def scores_work(c_cand, b_cand):
        return jnp.einsum("ctn,csn->cts", c_cand, b_cand, preferred_element_type=jnp.float32)

    inclusive, (levels, g_heads, scores) = suffix_sum(
        own_total,
        pre_axes,
        [(level_work, (code_cand,)), (g_work, (dy_cand, lengths)), (scores_work, (c_cand, b_cand))],
    )
    amplitude, inverse = levels
    later_total = inclusive - own_total
    after_local = own_total[None, :] - jnp.cumsum(log_prefix, axis=0)
    weight = jnp.exp(after_local + later_total[None, :])
    weighted_b = (weight[:, :, None] * b_prefix[:, None, :].astype(jnp.float32)).astype(
        jnp.bfloat16
    )
    x_heads = x_prefix.reshape(pre_len, heads_total, head_size)
    state_full = jnp.einsum("jhp,jhn->hpn", x_heads, weighted_b, preferred_element_type=jnp.float32)
    seq_at = lax.axis_index("seq")
    state_halves = state_full.reshape(2, half_heads, head_size, nstate)
    mine_first = seq_at == 0
    own_half = jnp.where(mine_first, state_halves[0], state_halves[1])
    give_half = jnp.where(mine_first, state_halves[1], state_halves[0])
    init_local = own_half + other_core(give_half)

    xc_heads = x_cand.reshape(cand_dev, cand_len, half_heads, head_size)
    scaled_g = g_heads.astype(jnp.float32) * amplitude[:, :, :, None]
    decayed_g, g_low = split_bf16(scaled_g)
    x_high, x_low = split_bf16(xc_heads.astype(jnp.float32) * inverse[:, :, :, None])

    dstate = jnp.einsum("cthp,ctn->hpn", decayed_g, c_cand, preferred_element_type=jnp.float32)
    both = cand_sum_bf16(jnp.concatenate([init_local, dstate], axis=0))
    init_half, grad_half = both[:half_heads], both[half_heads:]
    grad_other = other_core(grad_half)
    grad_state = jnp.where(
        mine_first,
        jnp.concatenate([grad_half, grad_other], axis=0),
        jnp.concatenate([grad_other, grad_half], axis=0),
    )

    causal = position[:, None] >= position[None, :]
    flat = (cand_dev, cand_len, half_width)

    def pair(left, right):
        return jnp.einsum(
            "ctk,csk->cts", left.reshape(flat), right.reshape(flat),
            preferred_element_type=jnp.float32,
        )

    weight_sum = pair(decayed_g, x_high) + pair(decayed_g, x_low) + pair(g_low, x_high)
    weight_sum = jnp.where(causal[None], weight_sum, 0.0)
    db_part = jnp.einsum(
        "cts,ctn->csn", weight_sum, c_cand.astype(jnp.float32), precision=lax.Precision.HIGHEST
    )
    dc_part = jnp.einsum(
        "cts,csn->ctn", weight_sum, b_cand.astype(jnp.float32), precision=lax.Precision.HIGHEST
    )

    amp_t = jnp.transpose(amplitude, (0, 2, 1))
    inv_t = jnp.transpose(inverse, (0, 2, 1))
    decay_mat = amp_t[:, :, :, None] * inv_t[:, :, None, :]
    kernel = jnp.where(causal[None, None], scores[:, None] * decay_mat, 0.0).astype(jnp.bfloat16)
    dx_cand = jnp.einsum("chts,cthp->cshp", kernel, g_heads, preferred_element_type=jnp.float32)
    dx_cand = dx_cand.astype(jnp.bfloat16).reshape(flat)

    dc_state = jnp.dot(
        decayed_g.reshape(cand_dev * cand_len, half_width),
        init_half.reshape(half_width, nstate),
        preferred_element_type=jnp.float32,
    )
    dc_total = dc_part + dc_state.reshape(cand_dev, cand_len, nstate)
    def token_half_sum(part):
        halves = part.reshape(cand_dev, 2, cand_len // 2, part.shape[2])
        own = jnp.where(mine_first, halves[:, 0], halves[:, 1])
        give = jnp.where(mine_first, halves[:, 1], halves[:, 0])
        return own + other_core(give)

    db_dc = token_half_sum(jnp.concatenate([db_part, dc_total], axis=2))
    db_cand, dc_cand = db_dc[:, :, :nstate], db_dc[:, :, nstate:]

    dx_prefix = jnp.einsum(
        "jhn,hpn->jhp", weighted_b, grad_state, preferred_element_type=jnp.float32
    )
    dx_prefix = dx_prefix.astype(jnp.bfloat16).reshape(pre_len, width)
    projected = jnp.einsum("jhp,hpn->jhn", x_heads, grad_state, preferred_element_type=jnp.float32)
    db_prefix = jnp.sum(projected * weight[:, :, None], axis=1)
    return (dx_prefix, db_prefix, dx_cand, db_cand, dc_cand)


def solution(mesh):
    return jax.shard_map(
        shards,
        mesh=mesh,
        in_specs=(
            P(("grp", "cand", "seq"), None),
            P(("grp", "cand", "seq"), None),
            P(("grp", "cand", "seq"), None),
            P(("grp", "cand"), None, "seq"),
            P(("grp", "cand"), None, None),
            P(("grp", "cand"), None, None),
            P(("grp", "cand"), None, "seq"),
            P(("grp", "cand")),
            P(("grp", "cand"), None, "seq"),
        ),
        out_specs=(
            P(("grp", "cand", "seq"), None),
            P(("grp", "cand", "seq"), None),
            P(("grp", "cand"), None, "seq"),
            P(("grp", "cand"), "seq", None),
            P(("grp", "cand"), "seq", None),
        ),
        check_vma=False,
    )
```

```python
import jax
import jax.numpy as jnp
from jax import lax
from jax.sharding import PartitionSpec as P

BLOCK = 256


def split_bf16(value):
    high = lax.reduce_precision(value, exponent_bits=8, mantissa_bits=7)
    low = (value - high).astype(jnp.bfloat16)
    return high.astype(jnp.bfloat16), low


def butterfly_sum(value, axis):
    count = lax.axis_size(axis)
    step = 1
    while step < count:
        partner = [(at, at ^ step) for at in range(count)]
        value = value + lax.ppermute(value, axis, partner)
        step *= 2
    return value


def suffix_sum(value, axis, works):
    count = lax.axis_size(axis)
    step = 1
    done = []
    rounds = 0
    while step < count:
        back = [(at, at - step) for at in range(step, count)]
        if rounds < len(works):
            fn, pick = works[rounds]
            value, args = lax.optimization_barrier((value, pick(done)))
        value = value + lax.ppermute(value, axis, back)
        if rounds < len(works):
            value, piece = lax.optimization_barrier((value, fn(*args)))
            done.append(piece)
        step *= 2
        rounds += 1
    return value, done


def bit_order(value, count, first_bits):
    nbits = count.bit_length() - 1
    rest = value.shape[1:]
    value = value.reshape((2,) * nbits + rest)
    axes = [nbits - 1 - bit for bit in first_bits]
    value = jnp.transpose(value, axes + list(range(nbits, nbits + len(rest))))
    return value.reshape((count,) + rest)


def halving_scatter(blocks, axis):
    count = lax.axis_size(axis)
    me = lax.axis_index(axis)
    rest = blocks.shape[1:]
    nbits = count.bit_length() - 1
    value = bit_order(blocks, count, list(range(nbits)))
    for bit in range(nbits):
        step = 1 << bit
        value = value.reshape((2, -1) + rest)
        upper = me // step % 2 == 1
        keep = jnp.where(upper, value[1], value[0])
        give = jnp.where(upper, value[0], value[1])
        value = keep + lax.ppermute(give, axis, [(at, at ^ step) for at in range(count)])
    return value[0]


def doubling_gather(piece, axis):
    count = lax.axis_size(axis)
    me = lax.axis_index(axis)
    nbits = count.bit_length() - 1
    value = piece[None]
    for bit in reversed(range(nbits)):
        step = 1 << bit
        other = lax.ppermute(value, axis, [(at, at ^ step) for at in range(count)])
        upper = me // step % 2 == 1
        value = jnp.where(
            upper, jnp.concatenate([other, value]), jnp.concatenate([value, other])
        )
    rest = piece.shape
    value = value.reshape((2,) * nbits + rest)
    axes = list(reversed(range(nbits)))
    value = jnp.transpose(value, axes + list(range(nbits, nbits + len(rest))))
    return value.reshape((count,) + rest)


def cand_sum_bf16(state):
    heads, size, width = state.shape
    count = lax.axis_size("cand")
    piece = size // count
    blocks = jnp.transpose(state.reshape(heads, count, piece, width), (1, 0, 2, 3))
    summed = halving_scatter(blocks, "cand").astype(jnp.bfloat16)
    gathered = doubling_gather(summed, "cand")
    return jnp.transpose(gathered, (1, 0, 2, 3)).reshape(heads, size, width)


def other_core(value):
    count = lax.axis_size("seq")
    return lax.ppermute(value, "seq", [(at, (at + 1) % count) for at in range(count)])


def shards(x_prefix, b_prefix, code_prefix, x_cand, b_cand, c_cand, code_cand, lengths, dy_cand):
    pre_len, width = x_prefix.shape
    heads_total = code_prefix.shape[1]
    head_size = width // heads_total
    nstate = b_prefix.shape[1]
    cand_dev, cand_len, half_width = x_cand.shape
    half_heads = code_cand.shape[2]
    pre_axes = ("cand", "seq")

    log_prefix = jnp.log1p(-code_prefix.astype(jnp.float32) * 1e-06)
    own_total = jnp.sum(log_prefix, axis=0)
    position = jnp.arange(cand_len, dtype=jnp.int32)

    def level_work(code_cand):
        level_all = jnp.cumsum(jnp.log1p(-code_cand.astype(jnp.float32) * 1e-06), axis=1)
        return jnp.exp(level_all), jnp.exp(-level_all)

    def g_work(dy_cand, lengths, amplitude, c_cand):
        valid_rows = position[None, :] < lengths[:, None] * BLOCK
        g_cand = jnp.where(valid_rows[:, :, None], dy_cand, jnp.zeros_like(dy_cand))
        g_heads = g_cand.reshape(cand_dev, cand_len, half_heads, head_size)
        scaled_g = g_heads.astype(jnp.float32) * amplitude[:, :, :, None]
        decayed_g, g_low = split_bf16(scaled_g)
        dstate = jnp.einsum("cthp,ctn->hpn", decayed_g, c_cand, preferred_element_type=jnp.float32)
        return g_heads, decayed_g, g_low, dstate

    def x_work(x_cand, inverse, c_cand, b_cand):
        xc_heads = x_cand.reshape(cand_dev, cand_len, half_heads, head_size)
        x_high, x_low = split_bf16(xc_heads.astype(jnp.float32) * inverse[:, :, :, None])
        scores = jnp.einsum("ctn,csn->cts", c_cand, b_cand, preferred_element_type=jnp.float32)
        return x_high, x_low, scores

    inclusive, (levels, g_parts, x_parts) = suffix_sum(
        own_total,
        pre_axes,
        [
            (level_work, lambda done: (code_cand,)),
            (g_work, lambda done: (dy_cand, lengths, done[0][0], c_cand)),
            (x_work, lambda done: (x_cand, done[0][1], c_cand, b_cand)),
        ],
    )
    amplitude, inverse = levels
    g_heads, decayed_g, g_low, dstate = g_parts
    x_high, x_low, scores = x_parts
    later_total = inclusive - own_total
    after_local = own_total[None, :] - jnp.cumsum(log_prefix, axis=0)
    weight = jnp.exp(after_local + later_total[None, :])
    weighted_b = (weight[:, :, None] * b_prefix[:, None, :].astype(jnp.float32)).astype(
        jnp.bfloat16
    )
    x_heads = x_prefix.reshape(pre_len, heads_total, head_size)
    state_full = jnp.einsum("jhp,jhn->hpn", x_heads, weighted_b, preferred_element_type=jnp.float32)
    seq_at = lax.axis_index("seq")
    state_halves = state_full.reshape(2, half_heads, head_size, nstate)
    mine_first = seq_at == 0
    own_half = jnp.where(mine_first, state_halves[0], state_halves[1])
    give_half = jnp.where(mine_first, state_halves[1], state_halves[0])
    init_local = own_half + other_core(give_half)

    grad_half = cand_sum_bf16(dstate)
    init_half = cand_sum_bf16(init_local)
    grad_other = other_core(grad_half)
    grad_state = jnp.where(
        mine_first,
        jnp.concatenate([grad_half, grad_other], axis=0),
        jnp.concatenate([grad_other, grad_half], axis=0),
    )

    causal = position[:, None] >= position[None, :]
    flat = (cand_dev, cand_len, half_width)

    def pair(left, right):
        return jnp.einsum(
            "ctk,csk->cts", left.reshape(flat), right.reshape(flat),
            preferred_element_type=jnp.float32,
        )

    weight_sum = pair(decayed_g, x_high) + pair(decayed_g, x_low) + pair(g_low, x_high)
    weight_sum = jnp.where(causal[None], weight_sum, 0.0)
    db_part = jnp.einsum(
        "cts,ctn->csn", weight_sum, c_cand.astype(jnp.float32), precision=lax.Precision.HIGHEST
    )
    dc_part = jnp.einsum(
        "cts,csn->ctn", weight_sum, b_cand.astype(jnp.float32), precision=lax.Precision.HIGHEST
    )

    amp_t = jnp.transpose(amplitude, (0, 2, 1))
    inv_t = jnp.transpose(inverse, (0, 2, 1))
    decay_mat = amp_t[:, :, :, None] * inv_t[:, :, None, :]
    kernel = jnp.where(causal[None, None], scores[:, None] * decay_mat, 0.0).astype(jnp.bfloat16)
    dx_cand = jnp.einsum("chts,cthp->cshp", kernel, g_heads, preferred_element_type=jnp.float32)
    dx_cand = dx_cand.astype(jnp.bfloat16).reshape(flat)

    dc_state = jnp.dot(
        decayed_g.reshape(cand_dev * cand_len, half_width),
        init_half.reshape(half_width, nstate),
        preferred_element_type=jnp.float32,
    )
    dc_total = dc_part + dc_state.reshape(cand_dev, cand_len, nstate)
    def token_half_sum(part):
        halves = part.reshape(cand_dev, 2, cand_len // 2, part.shape[2])
        own = jnp.where(mine_first, halves[:, 0], halves[:, 1])
        give = jnp.where(mine_first, halves[:, 1], halves[:, 0])
        return own + other_core(give)

    db_dc = token_half_sum(jnp.concatenate([db_part, dc_total], axis=2))
    db_cand, dc_cand = db_dc[:, :, :nstate], db_dc[:, :, nstate:]

    dx_prefix = jnp.einsum(
        "jhn,hpn->jhp", weighted_b, grad_state, preferred_element_type=jnp.float32
    )
    dx_prefix = dx_prefix.astype(jnp.bfloat16).reshape(pre_len, width)
    projected = jnp.einsum("jhp,hpn->jhn", x_heads, grad_state, preferred_element_type=jnp.float32)
    db_prefix = jnp.sum(projected * weight[:, :, None], axis=1)
    return (dx_prefix, db_prefix, dx_cand, db_cand, dc_cand)


def solution(mesh):
    return jax.shard_map(
        shards,
        mesh=mesh,
        in_specs=(
            P(("grp", "cand", "seq"), None),
            P(("grp", "cand", "seq"), None),
            P(("grp", "cand", "seq"), None),
            P(("grp", "cand"), None, "seq"),
            P(("grp", "cand"), None, None),
            P(("grp", "cand"), None, None),
            P(("grp", "cand"), None, "seq"),
            P(("grp", "cand")),
            P(("grp", "cand"), None, "seq"),
        ),
        out_specs=(
            P(("grp", "cand", "seq"), None),
            P(("grp", "cand", "seq"), None),
            P(("grp", "cand"), None, "seq"),
            P(("grp", "cand"), "seq", None),
            P(("grp", "cand"), "seq", None),
        ),
        check_vma=False,
    )
```

```python
import jax
import jax.numpy as jnp
from jax import lax
from jax.experimental import pallas as pl
from jax.sharding import PartitionSpec as P

BLOCK = 256


def split_bf16(value):
    high = lax.reduce_precision(value, exponent_bits=8, mantissa_bits=7)
    low = (value - high).astype(jnp.bfloat16)
    return high.astype(jnp.bfloat16), low


def butterfly_sum(value, axis):
    count = lax.axis_size(axis)
    step = 1
    while step < count:
        partner = [(at, at ^ step) for at in range(count)]
        value = value + lax.ppermute(value, axis, partner)
        step *= 2
    return value


def suffix_sum(value, axis, works):
    count = lax.axis_size(axis)
    step = 1
    done = []
    rounds = 0
    while step < count:
        back = [(at, at - step) for at in range(step, count)]
        if rounds < len(works):
            fn, pick = works[rounds]
            value, args = lax.optimization_barrier((value, pick(done)))
        value = value + lax.ppermute(value, axis, back)
        if rounds < len(works):
            value, piece = lax.optimization_barrier((value, fn(*args)))
            done.append(piece)
        step *= 2
        rounds += 1
    return value, done


def bit_order(value, count, first_bits):
    nbits = count.bit_length() - 1
    rest = value.shape[1:]
    value = value.reshape((2,) * nbits + rest)
    axes = [nbits - 1 - bit for bit in first_bits]
    value = jnp.transpose(value, axes + list(range(nbits, nbits + len(rest))))
    return value.reshape((count,) + rest)


def halving_scatter(blocks, axis):
    count = lax.axis_size(axis)
    me = lax.axis_index(axis)
    rest = blocks.shape[1:]
    nbits = count.bit_length() - 1
    value = bit_order(blocks, count, list(range(nbits)))
    for bit in range(nbits):
        step = 1 << bit
        value = value.reshape((2, -1) + rest)
        upper = me // step % 2 == 1
        keep = jnp.where(upper, value[1], value[0])
        give = jnp.where(upper, value[0], value[1])
        value = keep + lax.ppermute(give, axis, [(at, at ^ step) for at in range(count)])
    return value[0]


def doubling_gather(piece, axis):
    count = lax.axis_size(axis)
    me = lax.axis_index(axis)
    nbits = count.bit_length() - 1
    value = piece[None]
    for bit in reversed(range(nbits)):
        step = 1 << bit
        other = lax.ppermute(value, axis, [(at, at ^ step) for at in range(count)])
        upper = me // step % 2 == 1
        value = jnp.where(
            upper, jnp.concatenate([other, value]), jnp.concatenate([value, other])
        )
    rest = piece.shape
    value = value.reshape((2,) * nbits + rest)
    axes = list(reversed(range(nbits)))
    value = jnp.transpose(value, axes + list(range(nbits, nbits + len(rest))))
    return value.reshape((count,) + rest)


def cand_sum_bf16(state):
    heads, size, width = state.shape
    count = lax.axis_size("cand")
    piece = size // count
    blocks = jnp.transpose(state.reshape(heads, count, piece, width), (1, 0, 2, 3))
    summed = halving_scatter(blocks, "cand").astype(jnp.bfloat16)
    gathered = doubling_gather(summed, "cand")
    return jnp.transpose(gathered, (1, 0, 2, 3)).reshape(heads, size, width)


def other_core(value):
    count = lax.axis_size("seq")
    return lax.ppermute(value, "seq", [(at, (at + 1) % count) for at in range(count)])


def dx_body(scores_ref, amp_ref, inv_ref, g_ref, out_ref):
    cand_len = scores_ref.shape[1]
    half = cand_len // 2
    head_size = g_ref.shape[2] // 2
    row = lax.broadcasted_iota(jnp.int32, (half, cand_len), 0)
    col = lax.broadcasted_iota(jnp.int32, (half, cand_len), 1)
    for j in range(2):
        cols = slice(j * head_size, (j + 1) * head_size)
        amp_row = amp_ref[0, 0, j:j + 1, :]
        g_head = g_ref[0, :, cols]
        inv_top = inv_ref[0, 0, :half, j:j + 1]
        top = scores_ref[0, :half, :] * (amp_row * inv_top)
        top = jnp.where(col >= row, top, 0.0).astype(jnp.bfloat16)
        out_ref[0, :half, cols] = jnp.dot(
            top, g_head, preferred_element_type=jnp.float32
        ).astype(out_ref.dtype)
        inv_low = inv_ref[0, 0, half:, j:j + 1]
        low = scores_ref[0, half:, half:] * (amp_row[:, half:] * inv_low)
        low = jnp.where(col[:, :half] >= row[:, :half], low, 0.0).astype(jnp.bfloat16)
        out_ref[0, half:, cols] = jnp.dot(
            low, g_head[half:], preferred_element_type=jnp.float32
        ).astype(out_ref.dtype)


def dx_kernel(scores_t, amplitude, inverse, g_flat):
    cand_dev, cand_len, half_width = g_flat.shape
    half_heads = amplitude.shape[2]
    head_size = half_width // half_heads
    pairs = half_heads // 2
    amp_rows = jnp.transpose(amplitude.reshape(cand_dev, cand_len, pairs, 2), (0, 2, 3, 1))
    inv_cols = jnp.transpose(inverse.reshape(cand_dev, cand_len, pairs, 2), (0, 2, 1, 3))
    return pl.pallas_call(
        dx_body,
        grid=(cand_dev, pairs),
        in_specs=[
            pl.BlockSpec((1, cand_len, cand_len), lambda c, h: (c, 0, 0)),
            pl.BlockSpec((1, 1, 2, cand_len), lambda c, h: (c, h, 0, 0)),
            pl.BlockSpec((1, 1, cand_len, 2), lambda c, h: (c, h, 0, 0)),
            pl.BlockSpec((1, cand_len, 2 * head_size), lambda c, h: (c, 0, h)),
        ],
        out_specs=pl.BlockSpec((1, cand_len, 2 * head_size), lambda c, h: (c, 0, h)),
        out_shape=jax.ShapeDtypeStruct((cand_dev, cand_len, half_width), jnp.bfloat16),
    )(scores_t, amp_rows, inv_cols, g_flat)


def shards(x_prefix, b_prefix, code_prefix, x_cand, b_cand, c_cand, code_cand, lengths, dy_cand):
    pre_len, width = x_prefix.shape
    heads_total = code_prefix.shape[1]
    head_size = width // heads_total
    nstate = b_prefix.shape[1]
    cand_dev, cand_len, half_width = x_cand.shape
    half_heads = code_cand.shape[2]
    pre_axes = ("cand", "seq")

    log_prefix = jnp.log1p(-code_prefix.astype(jnp.float32) * 1e-06)
    own_total = jnp.sum(log_prefix, axis=0)
    position = jnp.arange(cand_len, dtype=jnp.int32)

    def level_work(code_cand):
        level_all = jnp.cumsum(jnp.log1p(-code_cand.astype(jnp.float32) * 1e-06), axis=1)
        return jnp.exp(level_all), jnp.exp(-level_all)

    def g_work(dy_cand, lengths, amplitude, c_cand):
        valid_rows = position[None, :] < lengths[:, None] * BLOCK
        g_cand = jnp.where(valid_rows[:, :, None], dy_cand, jnp.zeros_like(dy_cand))
        g_heads = g_cand.reshape(cand_dev, cand_len, half_heads, head_size)
        scaled_g = g_heads.astype(jnp.float32) * amplitude[:, :, :, None]
        decayed_g, g_low = split_bf16(scaled_g)
        dstate = jnp.einsum("cthp,ctn->hpn", decayed_g, c_cand, preferred_element_type=jnp.float32)
        return g_heads, decayed_g, g_low, dstate

    def x_work(x_cand, inverse, c_cand, b_cand):
        xc_heads = x_cand.reshape(cand_dev, cand_len, half_heads, head_size)
        x_high, x_low = split_bf16(xc_heads.astype(jnp.float32) * inverse[:, :, :, None])
        scores_t = jnp.einsum("csn,ctn->cst", b_cand, c_cand, preferred_element_type=jnp.float32)
        return x_high, x_low, scores_t

    inclusive, (levels, g_parts, x_parts) = suffix_sum(
        own_total,
        pre_axes,
        [
            (level_work, lambda done: (code_cand,)),
            (g_work, lambda done: (dy_cand, lengths, done[0][0], c_cand)),
            (x_work, lambda done: (x_cand, done[0][1], c_cand, b_cand)),
        ],
    )
    amplitude, inverse = levels
    g_heads, decayed_g, g_low, dstate = g_parts
    x_high, x_low, scores_t = x_parts
    later_total = inclusive - own_total
    after_local = own_total[None, :] - jnp.cumsum(log_prefix, axis=0)
    weight = jnp.exp(after_local + later_total[None, :])
    weighted_b = (weight[:, :, None] * b_prefix[:, None, :].astype(jnp.float32)).astype(
        jnp.bfloat16
    )
    x_heads = x_prefix.reshape(pre_len, heads_total, head_size)
    state_full = jnp.einsum("jhp,jhn->hpn", x_heads, weighted_b, preferred_element_type=jnp.float32)
    seq_at = lax.axis_index("seq")
    state_halves = state_full.reshape(2, half_heads, head_size, nstate)
    mine_first = seq_at == 0
    own_half = jnp.where(mine_first, state_halves[0], state_halves[1])
    give_half = jnp.where(mine_first, state_halves[1], state_halves[0])
    init_local = own_half + other_core(give_half)

    grad_half = cand_sum_bf16(dstate)
    init_half = cand_sum_bf16(init_local)
    grad_other = other_core(grad_half)
    grad_state = jnp.where(
        mine_first,
        jnp.concatenate([grad_half, grad_other], axis=0),
        jnp.concatenate([grad_other, grad_half], axis=0),
    )

    causal = position[:, None] >= position[None, :]
    flat = (cand_dev, cand_len, half_width)

    def pair(left, right):
        return jnp.einsum(
            "ctk,csk->cts", left.reshape(flat), right.reshape(flat),
            preferred_element_type=jnp.float32,
        )

    weight_sum = pair(decayed_g, x_high) + pair(decayed_g, x_low) + pair(g_low, x_high)
    weight_sum = jnp.where(causal[None], weight_sum, 0.0)
    db_part = jnp.einsum(
        "cts,ctn->csn", weight_sum, c_cand.astype(jnp.float32), precision=lax.Precision.HIGHEST
    )
    dc_part = jnp.einsum(
        "cts,csn->ctn", weight_sum, b_cand.astype(jnp.float32), precision=lax.Precision.HIGHEST
    )

    dx_cand = dx_kernel(scores_t, amplitude, inverse, g_heads.reshape(flat))

    dc_state = jnp.dot(
        decayed_g.reshape(cand_dev * cand_len, half_width),
        init_half.reshape(half_width, nstate),
        preferred_element_type=jnp.float32,
    )
    dc_total = dc_part + dc_state.reshape(cand_dev, cand_len, nstate)
    def token_half_sum(part):
        halves = part.reshape(cand_dev, 2, cand_len // 2, part.shape[2])
        own = jnp.where(mine_first, halves[:, 0], halves[:, 1])
        give = jnp.where(mine_first, halves[:, 1], halves[:, 0])
        return own + other_core(give)

    db_dc = token_half_sum(jnp.concatenate([db_part, dc_total], axis=2))
    db_cand, dc_cand = db_dc[:, :, :nstate], db_dc[:, :, nstate:]

    dx_prefix = jnp.einsum(
        "jhn,hpn->jhp", weighted_b, grad_state, preferred_element_type=jnp.float32
    )
    dx_prefix = dx_prefix.astype(jnp.bfloat16).reshape(pre_len, width)
    projected = jnp.einsum("jhp,hpn->jhn", x_heads, grad_state, preferred_element_type=jnp.float32)
    db_prefix = jnp.sum(projected * weight[:, :, None], axis=1)
    return (dx_prefix, db_prefix, dx_cand, db_cand, dc_cand)


def solution(mesh):
    return jax.shard_map(
        shards,
        mesh=mesh,
        in_specs=(
            P(("grp", "cand", "seq"), None),
            P(("grp", "cand", "seq"), None),
            P(("grp", "cand", "seq"), None),
            P(("grp", "cand"), None, "seq"),
            P(("grp", "cand"), None, None),
            P(("grp", "cand"), None, None),
            P(("grp", "cand"), None, "seq"),
            P(("grp", "cand")),
            P(("grp", "cand"), None, "seq"),
        ),
        out_specs=(
            P(("grp", "cand", "seq"), None),
            P(("grp", "cand", "seq"), None),
            P(("grp", "cand"), None, "seq"),
            P(("grp", "cand"), "seq", None),
            P(("grp", "cand"), "seq", None),
        ),
        check_vma=False,
    )
```

```python
import jax
import jax.numpy as jnp
from jax import lax
from jax.sharding import PartitionSpec as P

BLOCK = 256


def split_bf16(value):
    high = lax.reduce_precision(value, exponent_bits=8, mantissa_bits=7)
    low = (value - high).astype(jnp.bfloat16)
    return high.astype(jnp.bfloat16), low


def butterfly_sum(value, axis):
    count = lax.axis_size(axis)
    step = 1
    while step < count:
        partner = [(at, at ^ step) for at in range(count)]
        value = value + lax.ppermute(value, axis, partner)
        step *= 2
    return value


def suffix_sum(value, axis, works):
    count = lax.axis_size(axis)
    step = 1
    done = []
    rounds = 0
    while step < count:
        back = [(at, at - step) for at in range(step, count)]
        if rounds < len(works):
            fn, pick = works[rounds]
            value, args = lax.optimization_barrier((value, pick(done)))
        value = value + lax.ppermute(value, axis, back)
        if rounds < len(works):
            value, piece = lax.optimization_barrier((value, fn(*args)))
            done.append(piece)
        step *= 2
        rounds += 1
    return value, done


def bit_order(value, count, first_bits):
    nbits = count.bit_length() - 1
    rest = value.shape[1:]
    value = value.reshape((2,) * nbits + rest)
    axes = [nbits - 1 - bit for bit in first_bits]
    value = jnp.transpose(value, axes + list(range(nbits, nbits + len(rest))))
    return value.reshape((count,) + rest)


def halving_scatter(blocks, axis):
    count = lax.axis_size(axis)
    me = lax.axis_index(axis)
    rest = blocks.shape[1:]
    nbits = count.bit_length() - 1
    value = bit_order(blocks, count, list(range(nbits)))
    for bit in range(nbits):
        step = 1 << bit
        value = value.reshape((2, -1) + rest)
        upper = me // step % 2 == 1
        keep = jnp.where(upper, value[1], value[0])
        give = jnp.where(upper, value[0], value[1])
        value = keep + lax.ppermute(give, axis, [(at, at ^ step) for at in range(count)])
    return value[0]


def doubling_gather(piece, axis):
    count = lax.axis_size(axis)
    me = lax.axis_index(axis)
    nbits = count.bit_length() - 1
    value = piece[None]
    for bit in reversed(range(nbits)):
        step = 1 << bit
        other = lax.ppermute(value, axis, [(at, at ^ step) for at in range(count)])
        upper = me // step % 2 == 1
        value = jnp.where(
            upper, jnp.concatenate([other, value]), jnp.concatenate([value, other])
        )
    rest = piece.shape
    value = value.reshape((2,) * nbits + rest)
    axes = list(reversed(range(nbits)))
    value = jnp.transpose(value, axes + list(range(nbits, nbits + len(rest))))
    return value.reshape((count,) + rest)


def cand_sum_bf16(state):
    heads, size, width = state.shape
    count = lax.axis_size("cand")
    piece = size // count
    blocks = jnp.transpose(state.reshape(heads, count, piece, width), (1, 0, 2, 3))
    summed = halving_scatter(blocks, "cand").astype(jnp.bfloat16)
    gathered = doubling_gather(summed, "cand")
    return jnp.transpose(gathered, (1, 0, 2, 3)).reshape(heads, size, width)


def other_core(value):
    count = lax.axis_size("seq")
    return lax.ppermute(value, "seq", [(at, (at + 1) % count) for at in range(count)])


def shards(x_prefix, b_prefix, code_prefix, x_cand, b_cand, c_cand, code_cand, lengths, dy_cand):
    pre_len, width = x_prefix.shape
    heads_total = code_prefix.shape[1]
    head_size = width // heads_total
    nstate = b_prefix.shape[1]
    cand_dev, cand_len, half_width = x_cand.shape
    half_heads = code_cand.shape[2]
    pre_axes = ("cand", "seq")

    log_prefix = jnp.log1p(-code_prefix.astype(jnp.float32) * 1e-06)
    own_total = jnp.sum(log_prefix, axis=0)
    position = jnp.arange(cand_len, dtype=jnp.int32)

    def level_work(code_cand):
        level_all = jnp.cumsum(jnp.log1p(-code_cand.astype(jnp.float32) * 1e-06), axis=1)
        return jnp.exp(level_all), jnp.exp(-level_all)

    def g_work(dy_cand, lengths, amplitude, c_cand):
        valid_rows = position[None, :] < lengths[:, None] * BLOCK
        g_cand = jnp.where(valid_rows[:, :, None], dy_cand, jnp.zeros_like(dy_cand))
        g_heads = g_cand.reshape(cand_dev, cand_len, half_heads, head_size)
        scaled_g = g_heads.astype(jnp.float32) * amplitude[:, :, :, None]
        decayed_g, g_low = split_bf16(scaled_g)
        dstate = jnp.einsum("cthp,ctn->hpn", decayed_g, c_cand, preferred_element_type=jnp.float32)
        return g_heads, decayed_g, g_low, dstate

    def x_work(x_cand, inverse, c_cand, b_cand):
        xc_heads = x_cand.reshape(cand_dev, cand_len, half_heads, head_size)
        x_high, x_low = split_bf16(xc_heads.astype(jnp.float32) * inverse[:, :, :, None])
        scores = jnp.einsum("ctn,csn->cts", c_cand, b_cand, preferred_element_type=jnp.float32)
        return x_high, x_low, scores

    inclusive, (levels, g_parts, x_parts) = suffix_sum(
        own_total,
        pre_axes,
        [
            (level_work, lambda done: (code_cand,)),
            (g_work, lambda done: (dy_cand, lengths, done[0][0], c_cand)),
            (x_work, lambda done: (x_cand, done[0][1], c_cand, b_cand)),
        ],
    )
    amplitude, inverse = levels
    g_heads, decayed_g, g_low, dstate = g_parts
    x_high, x_low, scores = x_parts
    later_total = inclusive - own_total
    after_local = own_total[None, :] - jnp.cumsum(log_prefix, axis=0)
    weight = jnp.exp(after_local + later_total[None, :])
    weighted_b = (weight[:, :, None] * b_prefix[:, None, :].astype(jnp.float32)).astype(
        jnp.bfloat16
    )
    x_heads = x_prefix.reshape(pre_len, heads_total, head_size)
    state_full = jnp.einsum("jhp,jhn->hpn", x_heads, weighted_b, preferred_element_type=jnp.float32)
    seq_at = lax.axis_index("seq")
    state_halves = state_full.reshape(2, half_heads, head_size, nstate)
    mine_first = seq_at == 0
    own_half = jnp.where(mine_first, state_halves[0], state_halves[1])
    give_half = jnp.where(mine_first, state_halves[1], state_halves[0])
    init_local = own_half + other_core(give_half)

    grad_half = cand_sum_bf16(dstate)
    init_local, late = lax.optimization_barrier(
        (init_local, (g_heads, decayed_g, g_low, x_high, x_low, scores))
    )
    g_heads, decayed_g, g_low, x_high, x_low, scores = late
    init_half = cand_sum_bf16(init_local)
    grad_other = other_core(grad_half)
    grad_state = jnp.where(
        mine_first,
        jnp.concatenate([grad_half, grad_other], axis=0),
        jnp.concatenate([grad_other, grad_half], axis=0),
    )

    causal = position[:, None] >= position[None, :]
    flat = (cand_dev, cand_len, half_width)

    def pair(left, right):
        return jnp.einsum(
            "ctk,csk->cts", left.reshape(flat), right.reshape(flat),
            preferred_element_type=jnp.float32,
        )

    weight_sum = pair(decayed_g, x_high) + pair(decayed_g, x_low) + pair(g_low, x_high)
    weight_sum = jnp.where(causal[None], weight_sum, 0.0)
    db_part = jnp.einsum(
        "cts,ctn->csn", weight_sum, c_cand.astype(jnp.float32), precision=lax.Precision.HIGHEST
    )
    dc_part = jnp.einsum(
        "cts,csn->ctn", weight_sum, b_cand.astype(jnp.float32), precision=lax.Precision.HIGHEST
    )

    amp_t = jnp.transpose(amplitude, (0, 2, 1))
    inv_t = jnp.transpose(inverse, (0, 2, 1))
    decay_mat = amp_t[:, :, :, None] * inv_t[:, :, None, :]
    kernel = jnp.where(causal[None, None], scores[:, None] * decay_mat, 0.0).astype(jnp.bfloat16)
    dx_cand = jnp.einsum("chts,cthp->cshp", kernel, g_heads, preferred_element_type=jnp.float32)
    dx_cand = dx_cand.astype(jnp.bfloat16).reshape(flat)

    dc_state = jnp.dot(
        decayed_g.reshape(cand_dev * cand_len, half_width),
        init_half.reshape(half_width, nstate),
        preferred_element_type=jnp.float32,
    )
    dc_total = dc_part + dc_state.reshape(cand_dev, cand_len, nstate)
    def token_half_sum(part):
        halves = part.reshape(cand_dev, 2, cand_len // 2, part.shape[2])
        own = jnp.where(mine_first, halves[:, 0], halves[:, 1])
        give = jnp.where(mine_first, halves[:, 1], halves[:, 0])
        return own + other_core(give)

    db_dc = token_half_sum(jnp.concatenate([db_part, dc_total], axis=2))
    db_cand, dc_cand = db_dc[:, :, :nstate], db_dc[:, :, nstate:]

    dx_prefix = jnp.einsum(
        "jhn,hpn->jhp", weighted_b, grad_state, preferred_element_type=jnp.float32
    )
    dx_prefix = dx_prefix.astype(jnp.bfloat16).reshape(pre_len, width)
    projected = jnp.einsum("jhp,hpn->jhn", x_heads, grad_state, preferred_element_type=jnp.float32)
    db_prefix = jnp.sum(projected * weight[:, :, None], axis=1)
    return (dx_prefix, db_prefix, dx_cand, db_cand, dc_cand)


def solution(mesh):
    return jax.shard_map(
        shards,
        mesh=mesh,
        in_specs=(
            P(("grp", "cand", "seq"), None),
            P(("grp", "cand", "seq"), None),
            P(("grp", "cand", "seq"), None),
            P(("grp", "cand"), None, "seq"),
            P(("grp", "cand"), None, None),
            P(("grp", "cand"), None, None),
            P(("grp", "cand"), None, "seq"),
            P(("grp", "cand")),
            P(("grp", "cand"), None, "seq"),
        ),
        out_specs=(
            P(("grp", "cand", "seq"), None),
            P(("grp", "cand", "seq"), None),
            P(("grp", "cand"), None, "seq"),
            P(("grp", "cand"), "seq", None),
            P(("grp", "cand"), "seq", None),
        ),
        check_vma=False,
    )
```

```python
import jax
import jax.numpy as jnp
from jax import lax
from jax.sharding import PartitionSpec as P

BLOCK = 256


def split_bf16(value):
    high = lax.reduce_precision(value, exponent_bits=8, mantissa_bits=7)
    low = (value - high).astype(jnp.bfloat16)
    return high.astype(jnp.bfloat16), low


def butterfly_sum(value, axis):
    count = lax.axis_size(axis)
    step = 1
    while step < count:
        partner = [(at, at ^ step) for at in range(count)]
        value = value + lax.ppermute(value, axis, partner)
        step *= 2
    return value


def suffix_sum(value, axis, works):
    count = lax.axis_size(axis)
    step = 1
    done = []
    rounds = 0
    while step < count:
        back = [(at, at - step) for at in range(step, count)]
        if rounds < len(works):
            fn, pick = works[rounds]
            value, args = lax.optimization_barrier((value, pick(done)))
        value = value + lax.ppermute(value, axis, back)
        if rounds < len(works):
            value, piece = lax.optimization_barrier((value, fn(*args)))
            done.append(piece)
        step *= 2
        rounds += 1
    return value, done


def bit_order(value, count, first_bits):
    nbits = count.bit_length() - 1
    rest = value.shape[1:]
    value = value.reshape((2,) * nbits + rest)
    axes = [nbits - 1 - bit for bit in first_bits]
    value = jnp.transpose(value, axes + list(range(nbits, nbits + len(rest))))
    return value.reshape((count,) + rest)


def halving_scatter(blocks, axis):
    count = lax.axis_size(axis)
    me = lax.axis_index(axis)
    rest = blocks.shape[1:]
    nbits = count.bit_length() - 1
    value = bit_order(blocks, count, list(range(nbits)))
    for bit in range(nbits):
        step = 1 << bit
        value = value.reshape((2, -1) + rest)
        upper = me // step % 2 == 1
        keep = jnp.where(upper, value[1], value[0])
        give = jnp.where(upper, value[0], value[1])
        value = keep + lax.ppermute(give, axis, [(at, at ^ step) for at in range(count)])
    return value[0]


def doubling_gather(piece, axis):
    count = lax.axis_size(axis)
    me = lax.axis_index(axis)
    nbits = count.bit_length() - 1
    value = piece[None]
    for bit in reversed(range(nbits)):
        step = 1 << bit
        other = lax.ppermute(value, axis, [(at, at ^ step) for at in range(count)])
        upper = me // step % 2 == 1
        value = jnp.where(
            upper, jnp.concatenate([other, value]), jnp.concatenate([value, other])
        )
    rest = piece.shape
    value = value.reshape((2,) * nbits + rest)
    axes = list(reversed(range(nbits)))
    value = jnp.transpose(value, axes + list(range(nbits, nbits + len(rest))))
    return value.reshape((count,) + rest)


def cand_sum_bf16(state):
    heads, size, width = state.shape
    count = lax.axis_size("cand")
    piece = size // count
    blocks = jnp.transpose(state.reshape(heads, count, piece, width), (1, 0, 2, 3))
    summed = halving_scatter(blocks, "cand").astype(jnp.bfloat16)
    gathered = doubling_gather(summed, "cand")
    return jnp.transpose(gathered, (1, 0, 2, 3)).reshape(heads, size, width)


def other_core(value):
    count = lax.axis_size("seq")
    return lax.ppermute(value, "seq", [(at, (at + 1) % count) for at in range(count)])


def shards(x_prefix, b_prefix, code_prefix, x_cand, b_cand, c_cand, code_cand, lengths, dy_cand):
    pre_len, width = x_prefix.shape
    heads_total = code_prefix.shape[1]
    head_size = width // heads_total
    nstate = b_prefix.shape[1]
    cand_dev, cand_len, half_width = x_cand.shape
    half_heads = code_cand.shape[2]
    pre_axes = ("cand", "seq")

    log_prefix = jnp.log1p(-code_prefix.astype(jnp.float32) * 1e-06)
    own_total = jnp.sum(log_prefix, axis=0)
    position = jnp.arange(cand_len, dtype=jnp.int32)

    def level_work(code_cand):
        level_all = jnp.cumsum(jnp.log1p(-code_cand.astype(jnp.float32) * 1e-06), axis=1)
        return jnp.exp(level_all), jnp.exp(-level_all)

    def g_work(dy_cand, lengths, amplitude, c_cand):
        valid_rows = position[None, :] < lengths[:, None] * BLOCK
        g_cand = jnp.where(valid_rows[:, :, None], dy_cand, jnp.zeros_like(dy_cand))
        g_heads = g_cand.reshape(cand_dev, cand_len, half_heads, head_size)
        scaled_g = g_heads.astype(jnp.float32) * amplitude[:, :, :, None]
        decayed_g, g_low = split_bf16(scaled_g)
        dstate = jnp.einsum("cthp,ctn->hpn", decayed_g, c_cand, preferred_element_type=jnp.float32)
        return g_heads, decayed_g, g_low, dstate

    def scores_work(c_cand, b_cand):
        return jnp.einsum("ctn,csn->cts", c_cand, b_cand, preferred_element_type=jnp.float32)

    inclusive, (levels, g_parts, scores) = suffix_sum(
        own_total,
        pre_axes,
        [
            (level_work, lambda done: (code_cand,)),
            (g_work, lambda done: (dy_cand, lengths, done[0][0], c_cand)),
            (scores_work, lambda done: (c_cand, b_cand)),
        ],
    )
    inclusive, late = lax.optimization_barrier((inclusive, (g_parts, levels, x_cand)))
    g_parts, levels, x_late = late
    amplitude, inverse = levels
    g_heads, decayed_g, g_low, dstate = g_parts
    xc_heads = x_late.reshape(cand_dev, cand_len, half_heads, head_size)
    x_high, x_low = split_bf16(xc_heads.astype(jnp.float32) * inverse[:, :, :, None])
    later_total = inclusive - own_total
    after_local = own_total[None, :] - jnp.cumsum(log_prefix, axis=0)
    weight = jnp.exp(after_local + later_total[None, :])
    weighted_b = (weight[:, :, None] * b_prefix[:, None, :].astype(jnp.float32)).astype(
        jnp.bfloat16
    )
    x_heads = x_prefix.reshape(pre_len, heads_total, head_size)
    state_full = jnp.einsum("jhp,jhn->hpn", x_heads, weighted_b, preferred_element_type=jnp.float32)
    seq_at = lax.axis_index("seq")
    state_halves = state_full.reshape(2, half_heads, head_size, nstate)
    mine_first = seq_at == 0
    own_half = jnp.where(mine_first, state_halves[0], state_halves[1])
    give_half = jnp.where(mine_first, state_halves[1], state_halves[0])
    init_local = own_half + other_core(give_half)

    grad_half = cand_sum_bf16(dstate)
    init_half = cand_sum_bf16(init_local)
    grad_other = other_core(grad_half)
    grad_state = jnp.where(
        mine_first,
        jnp.concatenate([grad_half, grad_other], axis=0),
        jnp.concatenate([grad_other, grad_half], axis=0),
    )

    causal = position[:, None] >= position[None, :]
    flat = (cand_dev, cand_len, half_width)

    def pair(left, right):
        return jnp.einsum(
            "ctk,csk->cts", left.reshape(flat), right.reshape(flat),
            preferred_element_type=jnp.float32,
        )

    weight_sum = pair(decayed_g, x_high) + pair(decayed_g, x_low) + pair(g_low, x_high)
    weight_sum = jnp.where(causal[None], weight_sum, 0.0)
    db_part = jnp.einsum(
        "cts,ctn->csn", weight_sum, c_cand.astype(jnp.float32), precision=lax.Precision.HIGHEST
    )
    dc_part = jnp.einsum(
        "cts,csn->ctn", weight_sum, b_cand.astype(jnp.float32), precision=lax.Precision.HIGHEST
    )

    amp_t = jnp.transpose(amplitude, (0, 2, 1))
    inv_t = jnp.transpose(inverse, (0, 2, 1))
    decay_mat = amp_t[:, :, :, None] * inv_t[:, :, None, :]
    kernel = jnp.where(causal[None, None], scores[:, None] * decay_mat, 0.0).astype(jnp.bfloat16)
    dx_cand = jnp.einsum("chts,cthp->cshp", kernel, g_heads, preferred_element_type=jnp.float32)
    dx_cand = dx_cand.astype(jnp.bfloat16).reshape(flat)

    dc_state = jnp.dot(
        decayed_g.reshape(cand_dev * cand_len, half_width),
        init_half.reshape(half_width, nstate),
        preferred_element_type=jnp.float32,
    )
    dc_total = dc_part + dc_state.reshape(cand_dev, cand_len, nstate)
    def token_half_sum(part):
        halves = part.reshape(cand_dev, 2, cand_len // 2, part.shape[2])
        own = jnp.where(mine_first, halves[:, 0], halves[:, 1])
        give = jnp.where(mine_first, halves[:, 1], halves[:, 0])
        return own + other_core(give)

    db_dc = token_half_sum(jnp.concatenate([db_part, dc_total], axis=2))
    db_cand, dc_cand = db_dc[:, :, :nstate], db_dc[:, :, nstate:]

    dx_prefix = jnp.einsum(
        "jhn,hpn->jhp", weighted_b, grad_state, preferred_element_type=jnp.float32
    )
    dx_prefix = dx_prefix.astype(jnp.bfloat16).reshape(pre_len, width)
    projected = jnp.einsum("jhp,hpn->jhn", x_heads, grad_state, preferred_element_type=jnp.float32)
    db_prefix = jnp.sum(projected * weight[:, :, None], axis=1)
    return (dx_prefix, db_prefix, dx_cand, db_cand, dc_cand)


def solution(mesh):
    return jax.shard_map(
        shards,
        mesh=mesh,
        in_specs=(
            P(("grp", "cand", "seq"), None),
            P(("grp", "cand", "seq"), None),
            P(("grp", "cand", "seq"), None),
            P(("grp", "cand"), None, "seq"),
            P(("grp", "cand"), None, None),
            P(("grp", "cand"), None, None),
            P(("grp", "cand"), None, "seq"),
            P(("grp", "cand")),
            P(("grp", "cand"), None, "seq"),
        ),
        out_specs=(
            P(("grp", "cand", "seq"), None),
            P(("grp", "cand", "seq"), None),
            P(("grp", "cand"), None, "seq"),
            P(("grp", "cand"), "seq", None),
            P(("grp", "cand"), "seq", None),
        ),
        check_vma=False,
    )
```

```python
import jax
import jax.numpy as jnp
from jax import lax
from jax.sharding import PartitionSpec as P

BLOCK = 256


def split_bf16(value):
    high = lax.reduce_precision(value, exponent_bits=8, mantissa_bits=7)
    low = (value - high).astype(jnp.bfloat16)
    return high.astype(jnp.bfloat16), low


def butterfly_sum(value, axis):
    count = lax.axis_size(axis)
    step = 1
    while step < count:
        partner = [(at, at ^ step) for at in range(count)]
        value = value + lax.ppermute(value, axis, partner)
        step *= 2
    return value


def suffix_sum(value, axis, works):
    count = lax.axis_size(axis)
    step = 1
    done = []
    rounds = 0
    while step < count:
        back = [(at, at - step) for at in range(step, count)]
        if rounds < len(works):
            fn, pick = works[rounds]
            value, args = lax.optimization_barrier((value, pick(done)))
        value = value + lax.ppermute(value, axis, back)
        if rounds < len(works):
            value, piece = lax.optimization_barrier((value, fn(*args)))
            done.append(piece)
        step *= 2
        rounds += 1
    return value, done


def bit_order(value, count, first_bits):
    nbits = count.bit_length() - 1
    rest = value.shape[1:]
    value = value.reshape((2,) * nbits + rest)
    axes = [nbits - 1 - bit for bit in first_bits]
    value = jnp.transpose(value, axes + list(range(nbits, nbits + len(rest))))
    return value.reshape((count,) + rest)


def halving_scatter(blocks, axis, works=()):
    count = lax.axis_size(axis)
    me = lax.axis_index(axis)
    rest = blocks.shape[1:]
    nbits = count.bit_length() - 1
    value = bit_order(blocks, count, list(range(nbits)))
    done = []
    for bit in range(nbits):
        step = 1 << bit
        value = value.reshape((2, -1) + rest)
        upper = me // step % 2 == 1
        keep = jnp.where(upper, value[1], value[0])
        give = jnp.where(upper, value[0], value[1])
        if bit < len(works):
            fn, pick = works[bit]
            give, args = lax.optimization_barrier((give, pick(done)))
        value = keep + lax.ppermute(give, axis, [(at, at ^ step) for at in range(count)])
        if bit < len(works):
            value, piece = lax.optimization_barrier((value, fn(*args)))
            done.append(piece)
    for bit in range(nbits, len(works)):
        fn, pick = works[bit]
        done.append(fn(*pick(done)))
    return value[0], done


def doubling_gather(piece, axis):
    count = lax.axis_size(axis)
    me = lax.axis_index(axis)
    nbits = count.bit_length() - 1
    value = piece[None]
    for bit in reversed(range(nbits)):
        step = 1 << bit
        other = lax.ppermute(value, axis, [(at, at ^ step) for at in range(count)])
        upper = me // step % 2 == 1
        value = jnp.where(
            upper, jnp.concatenate([other, value]), jnp.concatenate([value, other])
        )
    rest = piece.shape
    value = value.reshape((2,) * nbits + rest)
    axes = list(reversed(range(nbits)))
    value = jnp.transpose(value, axes + list(range(nbits, nbits + len(rest))))
    return value.reshape((count,) + rest)


def cand_sum_bf16(state, works=()):
    heads, size, width = state.shape
    count = lax.axis_size("cand")
    piece = size // count
    blocks = jnp.transpose(state.reshape(heads, count, piece, width), (1, 0, 2, 3))
    summed, done = halving_scatter(blocks, "cand", works)
    gathered = doubling_gather(summed.astype(jnp.bfloat16), "cand")
    return jnp.transpose(gathered, (1, 0, 2, 3)).reshape(heads, size, width), done


def other_core(value):
    count = lax.axis_size("seq")
    return lax.ppermute(value, "seq", [(at, (at + 1) % count) for at in range(count)])


def shards(x_prefix, b_prefix, code_prefix, x_cand, b_cand, c_cand, code_cand, lengths, dy_cand):
    pre_len, width = x_prefix.shape
    heads_total = code_prefix.shape[1]
    head_size = width // heads_total
    nstate = b_prefix.shape[1]
    cand_dev, cand_len, half_width = x_cand.shape
    half_heads = code_cand.shape[2]
    pre_axes = ("cand", "seq")

    log_prefix = jnp.log1p(-code_prefix.astype(jnp.float32) * 1e-06)
    own_total = jnp.sum(log_prefix, axis=0)
    position = jnp.arange(cand_len, dtype=jnp.int32)

    def level_work(code_cand):
        level_all = jnp.cumsum(jnp.log1p(-code_cand.astype(jnp.float32) * 1e-06), axis=1)
        return jnp.exp(level_all), jnp.exp(-level_all)

    def g_work(dy_cand, lengths, amplitude, c_cand):
        valid_rows = position[None, :] < lengths[:, None] * BLOCK
        g_cand = jnp.where(valid_rows[:, :, None], dy_cand, jnp.zeros_like(dy_cand))
        g_heads = g_cand.reshape(cand_dev, cand_len, half_heads, head_size)
        scaled_g = g_heads.astype(jnp.float32) * amplitude[:, :, :, None]
        decayed_g, g_low = split_bf16(scaled_g)
        dstate = jnp.einsum("cthp,ctn->hpn", decayed_g, c_cand, preferred_element_type=jnp.float32)
        return g_heads, decayed_g, g_low, dstate

    def scores_work(c_cand, b_cand):
        return jnp.einsum("ctn,csn->cts", c_cand, b_cand, preferred_element_type=jnp.float32)

    inclusive, (levels, g_parts, scores) = suffix_sum(
        own_total,
        pre_axes,
        [
            (level_work, lambda done: (code_cand,)),
            (g_work, lambda done: (dy_cand, lengths, done[0][0], c_cand)),
            (scores_work, lambda done: (c_cand, b_cand)),
        ],
    )
    inclusive, late = lax.optimization_barrier((inclusive, (g_parts, levels, x_cand)))
    g_parts, levels, x_late = late
    amplitude, inverse = levels
    g_heads, decayed_g, g_low, dstate = g_parts
    later_total = inclusive - own_total
    after_local = own_total[None, :] - jnp.cumsum(log_prefix, axis=0)
    weight = jnp.exp(after_local + later_total[None, :])
    weighted_b = (weight[:, :, None] * b_prefix[:, None, :].astype(jnp.float32)).astype(
        jnp.bfloat16
    )
    x_heads = x_prefix.reshape(pre_len, heads_total, head_size)
    state_full = jnp.einsum("jhp,jhn->hpn", x_heads, weighted_b, preferred_element_type=jnp.float32)
    seq_at = lax.axis_index("seq")
    state_halves = state_full.reshape(2, half_heads, head_size, nstate)
    mine_first = seq_at == 0
    own_half = jnp.where(mine_first, state_halves[0], state_halves[1])
    give_half = jnp.where(mine_first, state_halves[1], state_halves[0])
    init_local = own_half + other_core(give_half)

    causal = position[:, None] >= position[None, :]
    flat = (cand_dev, cand_len, half_width)

    def x_work(x_late, inverse):
        xc_heads = x_late.reshape(cand_dev, cand_len, half_heads, head_size)
        return split_bf16(xc_heads.astype(jnp.float32) * inverse[:, :, :, None])

    def pair(left, right):
        return jnp.einsum(
            "ctk,csk->cts", left.reshape(flat), right.reshape(flat),
            preferred_element_type=jnp.float32,
        )

    def sum_work(decayed_g, g_low, x_high, x_low, c_cand, b_cand):
        weight_sum = pair(decayed_g, x_high) + pair(decayed_g, x_low) + pair(g_low, x_high)
        weight_sum = jnp.where(causal[None], weight_sum, 0.0)
        db_part = jnp.einsum(
            "cts,ctn->csn", weight_sum, c_cand.astype(jnp.float32), precision=lax.Precision.HIGHEST
        )
        dc_part = jnp.einsum(
            "cts,csn->ctn", weight_sum, b_cand.astype(jnp.float32), precision=lax.Precision.HIGHEST
        )
        return db_part, dc_part

    def dx_work(amplitude, inverse, scores, g_heads):
        amp_t = jnp.transpose(amplitude, (0, 2, 1))
        inv_t = jnp.transpose(inverse, (0, 2, 1))
        decay_mat = amp_t[:, :, :, None] * inv_t[:, :, None, :]
        kernel = jnp.where(causal[None, None], scores[:, None] * decay_mat, 0.0).astype(jnp.bfloat16)
        dx = jnp.einsum("chts,cthp->cshp", kernel, g_heads, preferred_element_type=jnp.float32)
        return dx.astype(jnp.bfloat16).reshape(flat)

    grad_half, _ = cand_sum_bf16(dstate)
    init_half, (x_parts, sums, dx_cand) = cand_sum_bf16(
        init_local,
        [
            (x_work, lambda done: (x_late, inverse)),
            (sum_work, lambda done: (decayed_g, g_low) + tuple(done[0]) + (c_cand, b_cand)),
            (dx_work, lambda done: (amplitude, inverse, scores, g_heads)),
        ],
    )
    db_part, dc_part = sums
    grad_other = other_core(grad_half)
    grad_state = jnp.where(
        mine_first,
        jnp.concatenate([grad_half, grad_other], axis=0),
        jnp.concatenate([grad_other, grad_half], axis=0),
    )

    dc_state = jnp.dot(
        decayed_g.reshape(cand_dev * cand_len, half_width),
        init_half.reshape(half_width, nstate),
        preferred_element_type=jnp.float32,
    )
    dc_total = dc_part + dc_state.reshape(cand_dev, cand_len, nstate)
    def token_half_sum(part):
        halves = part.reshape(cand_dev, 2, cand_len // 2, part.shape[2])
        own = jnp.where(mine_first, halves[:, 0], halves[:, 1])
        give = jnp.where(mine_first, halves[:, 1], halves[:, 0])
        return own + other_core(give)

    db_dc = token_half_sum(jnp.concatenate([db_part, dc_total], axis=2))
    db_cand, dc_cand = db_dc[:, :, :nstate], db_dc[:, :, nstate:]

    dx_prefix = jnp.einsum(
        "jhn,hpn->jhp", weighted_b, grad_state, preferred_element_type=jnp.float32
    )
    dx_prefix = dx_prefix.astype(jnp.bfloat16).reshape(pre_len, width)
    projected = jnp.einsum("jhp,hpn->jhn", x_heads, grad_state, preferred_element_type=jnp.float32)
    db_prefix = jnp.sum(projected * weight[:, :, None], axis=1)
    return (dx_prefix, db_prefix, dx_cand, db_cand, dc_cand)


def solution(mesh):
    return jax.shard_map(
        shards,
        mesh=mesh,
        in_specs=(
            P(("grp", "cand", "seq"), None),
            P(("grp", "cand", "seq"), None),
            P(("grp", "cand", "seq"), None),
            P(("grp", "cand"), None, "seq"),
            P(("grp", "cand"), None, None),
            P(("grp", "cand"), None, None),
            P(("grp", "cand"), None, "seq"),
            P(("grp", "cand")),
            P(("grp", "cand"), None, "seq"),
        ),
        out_specs=(
            P(("grp", "cand", "seq"), None),
            P(("grp", "cand", "seq"), None),
            P(("grp", "cand"), None, "seq"),
            P(("grp", "cand"), "seq", None),
            P(("grp", "cand"), "seq", None),
        ),
        check_vma=False,
    )
```

```python
import jax
import jax.numpy as jnp
from jax import lax
from jax.sharding import PartitionSpec as P

BLOCK = 256


def split_bf16(value):
    high = lax.reduce_precision(value, exponent_bits=8, mantissa_bits=7)
    low = (value - high).astype(jnp.bfloat16)
    return high.astype(jnp.bfloat16), low


def butterfly_sum(value, axis):
    count = lax.axis_size(axis)
    step = 1
    while step < count:
        partner = [(at, at ^ step) for at in range(count)]
        value = value + lax.ppermute(value, axis, partner)
        step *= 2
    return value


def suffix_sum(value, axis, works):
    count = lax.axis_size(axis)
    step = 1
    done = []
    rounds = 0
    while step < count:
        back = [(at, at - step) for at in range(step, count)]
        if rounds < len(works):
            fn, pick = works[rounds]
            value, args = lax.optimization_barrier((value, pick(done)))
        value = value + lax.ppermute(value, axis, back)
        if rounds < len(works):
            value, piece = lax.optimization_barrier((value, fn(*args)))
            done.append(piece)
        step *= 2
        rounds += 1
    return value, done


def bit_order(value, count, first_bits):
    nbits = count.bit_length() - 1
    rest = value.shape[1:]
    value = value.reshape((2,) * nbits + rest)
    axes = [nbits - 1 - bit for bit in first_bits]
    value = jnp.transpose(value, axes + list(range(nbits, nbits + len(rest))))
    return value.reshape((count,) + rest)


def halving_scatter(blocks, axis):
    count = lax.axis_size(axis)
    me = lax.axis_index(axis)
    rest = blocks.shape[1:]
    nbits = count.bit_length() - 1
    value = bit_order(blocks, count, list(range(nbits)))
    for bit in range(nbits):
        step = 1 << bit
        value = value.reshape((2, -1) + rest)
        upper = me // step % 2
        keep = lax.dynamic_index_in_dim(value, upper, 0, keepdims=False)
        give = lax.dynamic_index_in_dim(value, 1 - upper, 0, keepdims=False)
        value = keep + lax.ppermute(give, axis, [(at, at ^ step) for at in range(count)])
    return value[0]


def doubling_gather(piece, axis):
    count = lax.axis_size(axis)
    me = lax.axis_index(axis)
    nbits = count.bit_length() - 1
    value = piece[None]
    for bit in reversed(range(nbits)):
        step = 1 << bit
        other = lax.ppermute(value, axis, [(at, at ^ step) for at in range(count)])
        upper = me // step % 2 == 1
        value = jnp.where(
            upper, jnp.concatenate([other, value]), jnp.concatenate([value, other])
        )
    rest = piece.shape
    value = value.reshape((2,) * nbits + rest)
    axes = list(reversed(range(nbits)))
    value = jnp.transpose(value, axes + list(range(nbits, nbits + len(rest))))
    return value.reshape((count,) + rest)


def cand_sum_bf16(state):
    heads, size, width = state.shape
    count = lax.axis_size("cand")
    piece = size // count
    blocks = jnp.transpose(state.reshape(heads, count, piece, width), (1, 0, 2, 3))
    summed = halving_scatter(blocks, "cand").astype(jnp.bfloat16)
    gathered = doubling_gather(summed, "cand")
    return jnp.transpose(gathered, (1, 0, 2, 3)).reshape(heads, size, width)


def other_core(value):
    count = lax.axis_size("seq")
    return lax.ppermute(value, "seq", [(at, (at + 1) % count) for at in range(count)])


def shards(x_prefix, b_prefix, code_prefix, x_cand, b_cand, c_cand, code_cand, lengths, dy_cand):
    pre_len, width = x_prefix.shape
    heads_total = code_prefix.shape[1]
    head_size = width // heads_total
    nstate = b_prefix.shape[1]
    cand_dev, cand_len, half_width = x_cand.shape
    half_heads = code_cand.shape[2]
    pre_axes = ("cand", "seq")

    log_prefix = jnp.log1p(-code_prefix.astype(jnp.float32) * 1e-06)
    own_total = jnp.sum(log_prefix, axis=0)
    position = jnp.arange(cand_len, dtype=jnp.int32)

    def level_work(code_cand):
        level_all = jnp.cumsum(jnp.log1p(-code_cand.astype(jnp.float32) * 1e-06), axis=1)
        return jnp.exp(level_all), jnp.exp(-level_all)

    def g_work(dy_cand, lengths, amplitude, c_cand):
        valid_rows = position[None, :] < lengths[:, None] * BLOCK
        g_cand = jnp.where(valid_rows[:, :, None], dy_cand, jnp.zeros_like(dy_cand))
        g_heads = g_cand.reshape(cand_dev, cand_len, half_heads, head_size)
        scaled_g = g_heads.astype(jnp.float32) * amplitude[:, :, :, None]
        decayed_g, g_low = split_bf16(scaled_g)
        dstate = jnp.einsum("cthp,ctn->hpn", decayed_g, c_cand, preferred_element_type=jnp.float32)
        return g_heads, decayed_g, g_low, dstate

    def x_work(x_cand, inverse, c_cand, b_cand):
        xc_heads = x_cand.reshape(cand_dev, cand_len, half_heads, head_size)
        x_high, x_low = split_bf16(xc_heads.astype(jnp.float32) * inverse[:, :, :, None])
        scores = jnp.einsum("ctn,csn->cts", c_cand, b_cand, preferred_element_type=jnp.float32)
        return x_high, x_low, scores

    inclusive, (levels, g_parts, x_parts) = suffix_sum(
        own_total,
        pre_axes,
        [
            (level_work, lambda done: (code_cand,)),
            (g_work, lambda done: (dy_cand, lengths, done[0][0], c_cand)),
            (x_work, lambda done: (x_cand, done[0][1], c_cand, b_cand)),
        ],
    )
    amplitude, inverse = levels
    g_heads, decayed_g, g_low, dstate = g_parts
    x_high, x_low, scores = x_parts
    later_total = inclusive - own_total
    after_local = own_total[None, :] - jnp.cumsum(log_prefix, axis=0)
    weight = jnp.exp(after_local + later_total[None, :])
    weighted_b = (weight[:, :, None] * b_prefix[:, None, :].astype(jnp.float32)).astype(
        jnp.bfloat16
    )
    x_heads = x_prefix.reshape(pre_len, heads_total, head_size)
    state_full = jnp.einsum("jhp,jhn->hpn", x_heads, weighted_b, preferred_element_type=jnp.float32)
    seq_at = lax.axis_index("seq")
    state_halves = state_full.reshape(2, half_heads, head_size, nstate)
    mine_first = seq_at == 0
    own_half = lax.dynamic_index_in_dim(state_halves, seq_at, 0, keepdims=False)
    give_half = lax.dynamic_index_in_dim(state_halves, 1 - seq_at, 0, keepdims=False)
    init_local = own_half + other_core(give_half)

    grad_half = cand_sum_bf16(dstate)
    init_half = cand_sum_bf16(init_local)
    grad_other = other_core(grad_half)
    grad_state = jnp.where(
        mine_first,
        jnp.concatenate([grad_half, grad_other], axis=0),
        jnp.concatenate([grad_other, grad_half], axis=0),
    )

    causal = position[:, None] >= position[None, :]
    flat = (cand_dev, cand_len, half_width)

    def pair(left, right):
        return jnp.einsum(
            "ctk,csk->cts", left.reshape(flat), right.reshape(flat),
            preferred_element_type=jnp.float32,
        )

    weight_sum = pair(decayed_g, x_high) + pair(decayed_g, x_low) + pair(g_low, x_high)
    weight_sum = jnp.where(causal[None], weight_sum, 0.0)
    db_part = jnp.einsum(
        "cts,ctn->csn", weight_sum, c_cand.astype(jnp.float32), precision=lax.Precision.HIGHEST
    )
    dc_part = jnp.einsum(
        "cts,csn->ctn", weight_sum, b_cand.astype(jnp.float32), precision=lax.Precision.HIGHEST
    )

    amp_t = jnp.transpose(amplitude, (0, 2, 1))
    inv_t = jnp.transpose(inverse, (0, 2, 1))
    decay_mat = amp_t[:, :, :, None] * inv_t[:, :, None, :]
    kernel = jnp.where(causal[None, None], scores[:, None] * decay_mat, 0.0).astype(jnp.bfloat16)
    dx_cand = jnp.einsum("chts,cthp->cshp", kernel, g_heads, preferred_element_type=jnp.float32)
    dx_cand = dx_cand.astype(jnp.bfloat16).reshape(flat)

    dc_state = jnp.dot(
        decayed_g.reshape(cand_dev * cand_len, half_width),
        init_half.reshape(half_width, nstate),
        preferred_element_type=jnp.float32,
    )
    dc_total = dc_part + dc_state.reshape(cand_dev, cand_len, nstate)
    def token_half_sum(part):
        halves = part.reshape(cand_dev, 2, cand_len // 2, part.shape[2])
        own = lax.dynamic_index_in_dim(halves, seq_at, 1, keepdims=False)
        give = lax.dynamic_index_in_dim(halves, 1 - seq_at, 1, keepdims=False)
        return own + other_core(give)

    db_dc = token_half_sum(jnp.concatenate([db_part, dc_total], axis=2))
    db_cand, dc_cand = db_dc[:, :, :nstate], db_dc[:, :, nstate:]

    dx_prefix = jnp.einsum(
        "jhn,hpn->jhp", weighted_b, grad_state, preferred_element_type=jnp.float32
    )
    dx_prefix = dx_prefix.astype(jnp.bfloat16).reshape(pre_len, width)
    projected = jnp.einsum("jhp,hpn->jhn", x_heads, grad_state, preferred_element_type=jnp.float32)
    db_prefix = jnp.sum(projected * weight[:, :, None], axis=1)
    return (dx_prefix, db_prefix, dx_cand, db_cand, dc_cand)


def solution(mesh):
    return jax.shard_map(
        shards,
        mesh=mesh,
        in_specs=(
            P(("grp", "cand", "seq"), None),
            P(("grp", "cand", "seq"), None),
            P(("grp", "cand", "seq"), None),
            P(("grp", "cand"), None, "seq"),
            P(("grp", "cand"), None, None),
            P(("grp", "cand"), None, None),
            P(("grp", "cand"), None, "seq"),
            P(("grp", "cand")),
            P(("grp", "cand"), None, "seq"),
        ),
        out_specs=(
            P(("grp", "cand", "seq"), None),
            P(("grp", "cand", "seq"), None),
            P(("grp", "cand"), None, "seq"),
            P(("grp", "cand"), "seq", None),
            P(("grp", "cand"), "seq", None),
        ),
        check_vma=False,
    )
```

```python
import jax
import jax.numpy as jnp
from jax import lax
from jax.sharding import PartitionSpec as P

BLOCK = 256


def split_bf16(value):
    high = lax.reduce_precision(value, exponent_bits=8, mantissa_bits=7)
    low = (value - high).astype(jnp.bfloat16)
    return high.astype(jnp.bfloat16), low


def butterfly_sum(value, axis):
    count = lax.axis_size(axis)
    step = 1
    while step < count:
        partner = [(at, at ^ step) for at in range(count)]
        value = value + lax.ppermute(value, axis, partner)
        step *= 2
    return value


def suffix_sum(value, axis, works):
    count = lax.axis_size(axis)
    step = 1
    done = []
    rounds = 0
    while step < count:
        back = [(at, at - step) for at in range(step, count)]
        if rounds < len(works):
            fn, pick = works[rounds]
            value, args = lax.optimization_barrier((value, pick(done)))
        value = value + lax.ppermute(value, axis, back)
        if rounds < len(works):
            value, piece = lax.optimization_barrier((value, fn(*args)))
            done.append(piece)
        step *= 2
        rounds += 1
    return value, done


def bit_order(value, count, first_bits):
    nbits = count.bit_length() - 1
    rest = value.shape[1:]
    value = value.reshape((2,) * nbits + rest)
    axes = [nbits - 1 - bit for bit in first_bits]
    value = jnp.transpose(value, axes + list(range(nbits, nbits + len(rest))))
    return value.reshape((count,) + rest)


def halving_scatter(blocks, axis):
    count = lax.axis_size(axis)
    me = lax.axis_index(axis)
    rest = blocks.shape[1:]
    nbits = count.bit_length() - 1
    value = bit_order(blocks, count, list(range(nbits)))
    for bit in range(nbits):
        step = 1 << bit
        value = value.reshape((2, -1) + rest)
        upper = me // step % 2
        keep = lax.dynamic_index_in_dim(value, upper, 0, keepdims=False)
        give = lax.dynamic_index_in_dim(value, 1 - upper, 0, keepdims=False)
        value = keep + lax.ppermute(give, axis, [(at, at ^ step) for at in range(count)])
    return value[0]


def doubling_gather(piece, axis):
    count = lax.axis_size(axis)
    me = lax.axis_index(axis)
    nbits = count.bit_length() - 1
    value = piece[None]
    for bit in reversed(range(nbits)):
        step = 1 << bit
        other = lax.ppermute(value, axis, [(at, at ^ step) for at in range(count)])
        upper = me // step % 2 == 1
        value = jnp.where(
            upper, jnp.concatenate([other, value]), jnp.concatenate([value, other])
        )
    rest = piece.shape
    value = value.reshape((2,) * nbits + rest)
    axes = list(reversed(range(nbits)))
    value = jnp.transpose(value, axes + list(range(nbits, nbits + len(rest))))
    return value.reshape((count,) + rest)


def cand_sum_bf16(state):
    heads, size, width = state.shape
    count = lax.axis_size("cand")
    piece = size // count
    blocks = jnp.transpose(state.reshape(heads, count, piece, width), (1, 0, 2, 3))
    summed = halving_scatter(blocks, "cand").astype(jnp.bfloat16)
    gathered = doubling_gather(summed, "cand")
    return jnp.transpose(gathered, (1, 0, 2, 3)).reshape(heads, size, width)


def other_core(value):
    count = lax.axis_size("seq")
    return lax.ppermute(value, "seq", [(at, (at + 1) % count) for at in range(count)])


def shards(x_prefix, b_prefix, code_prefix, x_cand, b_cand, c_cand, code_cand, lengths, dy_cand):
    pre_len, width = x_prefix.shape
    heads_total = code_prefix.shape[1]
    head_size = width // heads_total
    nstate = b_prefix.shape[1]
    cand_dev, cand_len, half_width = x_cand.shape
    half_heads = code_cand.shape[2]
    pre_axes = ("cand", "seq")

    log_prefix = jnp.log1p(-code_prefix.astype(jnp.float32) * 1e-06)
    own_total = jnp.sum(log_prefix, axis=0)
    position = jnp.arange(cand_len, dtype=jnp.int32)

    def level_work(code_cand):
        rates = jnp.log1p(-code_cand.astype(jnp.float32) * 1e-06)
        lower = (position[:, None] >= position[None, :]).astype(jnp.float32)
        level_all = jnp.einsum("ts,csh->cth", lower, rates, precision=lax.Precision.HIGHEST)
        return jnp.exp(level_all), jnp.exp(-level_all)

    def g_work(dy_cand, lengths, amplitude, c_cand):
        valid_rows = position[None, :] < lengths[:, None] * BLOCK
        g_cand = jnp.where(valid_rows[:, :, None], dy_cand, jnp.zeros_like(dy_cand))
        g_heads = g_cand.reshape(cand_dev, cand_len, half_heads, head_size)
        scaled_g = g_heads.astype(jnp.float32) * amplitude[:, :, :, None]
        decayed_g, g_low = split_bf16(scaled_g)
        dstate = jnp.einsum("cthp,ctn->hpn", decayed_g, c_cand, preferred_element_type=jnp.float32)
        return g_heads, decayed_g, g_low, dstate

    def x_work(x_cand, inverse, c_cand, b_cand):
        xc_heads = x_cand.reshape(cand_dev, cand_len, half_heads, head_size)
        x_high, x_low = split_bf16(xc_heads.astype(jnp.float32) * inverse[:, :, :, None])
        scores = jnp.einsum("ctn,csn->cts", c_cand, b_cand, preferred_element_type=jnp.float32)
        return x_high, x_low, scores

    inclusive, (levels, g_parts, x_parts) = suffix_sum(
        own_total,
        pre_axes,
        [
            (level_work, lambda done: (code_cand,)),
            (g_work, lambda done: (dy_cand, lengths, done[0][0], c_cand)),
            (x_work, lambda done: (x_cand, done[0][1], c_cand, b_cand)),
        ],
    )
    amplitude, inverse = levels
    g_heads, decayed_g, g_low, dstate = g_parts
    x_high, x_low, scores = x_parts
    later_total = inclusive - own_total
    after_local = own_total[None, :] - jnp.cumsum(log_prefix, axis=0)
    weight = jnp.exp(after_local + later_total[None, :])
    weighted_b = (weight[:, :, None] * b_prefix[:, None, :].astype(jnp.float32)).astype(
        jnp.bfloat16
    )
    x_heads = x_prefix.reshape(pre_len, heads_total, head_size)
    state_full = jnp.einsum("jhp,jhn->hpn", x_heads, weighted_b, preferred_element_type=jnp.float32)
    seq_at = lax.axis_index("seq")
    state_halves = state_full.reshape(2, half_heads, head_size, nstate)
    mine_first = seq_at == 0
    own_half = lax.dynamic_index_in_dim(state_halves, seq_at, 0, keepdims=False)
    give_half = lax.dynamic_index_in_dim(state_halves, 1 - seq_at, 0, keepdims=False)
    init_local = own_half + other_core(give_half)

    grad_half = cand_sum_bf16(dstate)
    init_half = cand_sum_bf16(init_local)
    grad_other = other_core(grad_half)
    grad_state = jnp.where(
        mine_first,
        jnp.concatenate([grad_half, grad_other], axis=0),
        jnp.concatenate([grad_other, grad_half], axis=0),
    )

    causal = position[:, None] >= position[None, :]
    flat = (cand_dev, cand_len, half_width)

    def pair(left, right):
        return jnp.einsum(
            "ctk,csk->cts", left.reshape(flat), right.reshape(flat),
            preferred_element_type=jnp.float32,
        )

    weight_sum = pair(decayed_g, x_high) + pair(decayed_g, x_low) + pair(g_low, x_high)
    weight_sum = jnp.where(causal[None], weight_sum, 0.0)
    db_part = jnp.einsum(
        "cts,ctn->csn", weight_sum, c_cand.astype(jnp.float32), precision=lax.Precision.HIGHEST
    )
    dc_part = jnp.einsum(
        "cts,csn->ctn", weight_sum, b_cand.astype(jnp.float32), precision=lax.Precision.HIGHEST
    )

    amp_t = jnp.transpose(amplitude, (0, 2, 1))
    inv_t = jnp.transpose(inverse, (0, 2, 1))
    decay_mat = amp_t[:, :, :, None] * inv_t[:, :, None, :]
    kernel = jnp.where(causal[None, None], scores[:, None] * decay_mat, 0.0).astype(jnp.bfloat16)
    dx_cand = jnp.einsum("chts,cthp->cshp", kernel, g_heads, preferred_element_type=jnp.float32)
    dx_cand = dx_cand.astype(jnp.bfloat16).reshape(flat)

    dc_state = jnp.dot(
        decayed_g.reshape(cand_dev * cand_len, half_width),
        init_half.reshape(half_width, nstate),
        preferred_element_type=jnp.float32,
    )
    dc_total = dc_part + dc_state.reshape(cand_dev, cand_len, nstate)
    def token_half_sum(part):
        halves = part.reshape(cand_dev, 2, cand_len // 2, part.shape[2])
        own = lax.dynamic_index_in_dim(halves, seq_at, 1, keepdims=False)
        give = lax.dynamic_index_in_dim(halves, 1 - seq_at, 1, keepdims=False)
        return own + other_core(give)

    db_dc = token_half_sum(jnp.concatenate([db_part, dc_total], axis=2))
    db_cand, dc_cand = db_dc[:, :, :nstate], db_dc[:, :, nstate:]

    dx_prefix = jnp.einsum(
        "jhn,hpn->jhp", weighted_b, grad_state, preferred_element_type=jnp.float32
    )
    dx_prefix = dx_prefix.astype(jnp.bfloat16).reshape(pre_len, width)
    projected = jnp.einsum("jhp,hpn->jhn", x_heads, grad_state, preferred_element_type=jnp.float32)
    db_prefix = jnp.sum(projected * weight[:, :, None], axis=1)
    return (dx_prefix, db_prefix, dx_cand, db_cand, dc_cand)


def solution(mesh):
    return jax.shard_map(
        shards,
        mesh=mesh,
        in_specs=(
            P(("grp", "cand", "seq"), None),
            P(("grp", "cand", "seq"), None),
            P(("grp", "cand", "seq"), None),
            P(("grp", "cand"), None, "seq"),
            P(("grp", "cand"), None, None),
            P(("grp", "cand"), None, None),
            P(("grp", "cand"), None, "seq"),
            P(("grp", "cand")),
            P(("grp", "cand"), None, "seq"),
        ),
        out_specs=(
            P(("grp", "cand", "seq"), None),
            P(("grp", "cand", "seq"), None),
            P(("grp", "cand"), None, "seq"),
            P(("grp", "cand"), "seq", None),
            P(("grp", "cand"), "seq", None),
        ),
        check_vma=False,
    )
```

```python
import jax
import jax.numpy as jnp
from jax import lax
from jax.sharding import PartitionSpec as P

BLOCK = 256


def split_bf16(value):
    high = lax.reduce_precision(value, exponent_bits=8, mantissa_bits=7)
    low = (value - high).astype(jnp.bfloat16)
    return high.astype(jnp.bfloat16), low


def butterfly_sum(value, axis):
    count = lax.axis_size(axis)
    step = 1
    while step < count:
        partner = [(at, at ^ step) for at in range(count)]
        value = value + lax.ppermute(value, axis, partner)
        step *= 2
    return value


def suffix_sum(value, axis, works):
    count = lax.axis_size(axis)
    step = 1
    done = []
    rounds = 0
    while step < count:
        back = [(at, at - step) for at in range(step, count)]
        if rounds < len(works):
            fn, pick = works[rounds]
            value, args = lax.optimization_barrier((value, pick(done)))
        value = value + lax.ppermute(value, axis, back)
        if rounds < len(works):
            value, piece = lax.optimization_barrier((value, fn(*args)))
            done.append(piece)
        step *= 2
        rounds += 1
    return value, done


def bit_order(value, count, first_bits):
    nbits = count.bit_length() - 1
    rest = value.shape[1:]
    value = value.reshape((2,) * nbits + rest)
    axes = [nbits - 1 - bit for bit in first_bits]
    value = jnp.transpose(value, axes + list(range(nbits, nbits + len(rest))))
    return value.reshape((count,) + rest)


def halving_scatter(blocks, axis):
    count = lax.axis_size(axis)
    me = lax.axis_index(axis)
    rest = blocks.shape[1:]
    nbits = count.bit_length() - 1
    value = bit_order(blocks, count, list(range(nbits)))
    for bit in range(nbits):
        step = 1 << bit
        value = value.reshape((2, -1) + rest)
        upper = me // step % 2
        keep = lax.dynamic_index_in_dim(value, upper, 0, keepdims=False)
        give = lax.dynamic_index_in_dim(value, 1 - upper, 0, keepdims=False)
        value = keep + lax.ppermute(give, axis, [(at, at ^ step) for at in range(count)])
    return value[0]


def doubling_gather(piece, axis):
    count = lax.axis_size(axis)
    me = lax.axis_index(axis)
    nbits = count.bit_length() - 1
    value = piece[None]
    for bit in reversed(range(nbits)):
        step = 1 << bit
        other = lax.ppermute(value, axis, [(at, at ^ step) for at in range(count)])
        upper = me // step % 2 == 1
        value = jnp.where(
            upper, jnp.concatenate([other, value]), jnp.concatenate([value, other])
        )
    rest = piece.shape
    value = value.reshape((2,) * nbits + rest)
    axes = list(reversed(range(nbits)))
    value = jnp.transpose(value, axes + list(range(nbits, nbits + len(rest))))
    return value.reshape((count,) + rest)


def cand_sum_bf16(state):
    heads, size, width = state.shape
    count = lax.axis_size("cand")
    piece = size // count
    blocks = jnp.transpose(state.reshape(heads, count, piece, width), (1, 0, 2, 3))
    summed = halving_scatter(blocks, "cand").astype(jnp.bfloat16)
    gathered = doubling_gather(summed, "cand")
    return jnp.transpose(gathered, (1, 0, 2, 3)).reshape(heads, size, width)


def other_core(value):
    count = lax.axis_size("seq")
    return lax.ppermute(value, "seq", [(at, (at + 1) % count) for at in range(count)])


def shards(x_prefix, b_prefix, code_prefix, x_cand, b_cand, c_cand, code_cand, lengths, dy_cand):
    pre_len, width = x_prefix.shape
    heads_total = code_prefix.shape[1]
    head_size = width // heads_total
    nstate = b_prefix.shape[1]
    cand_dev, cand_len, half_width = x_cand.shape
    half_heads = code_cand.shape[2]
    pre_axes = ("cand", "seq")

    log_prefix = jnp.log1p(-code_prefix.astype(jnp.float32) * 1e-06)
    own_total = jnp.sum(log_prefix, axis=0)
    position = jnp.arange(cand_len, dtype=jnp.int32)

    def level_work(code_cand):
        rates = jnp.log1p(-code_cand.astype(jnp.float32) * 1e-06)
        lower = (position[:, None] >= position[None, :]).astype(jnp.float32)
        level_all = jnp.einsum("ts,csh->cth", lower, rates, precision=lax.Precision.HIGHEST)
        return jnp.exp(level_all), jnp.exp(-level_all)

    def g_work(dy_cand, lengths, amplitude, c_cand):
        valid_rows = position[None, :] < lengths[:, None] * BLOCK
        g_cand = jnp.where(valid_rows[:, :, None], dy_cand, jnp.zeros_like(dy_cand))
        g_heads = g_cand.reshape(cand_dev, cand_len, half_heads, head_size)
        scaled_g = g_heads.astype(jnp.float32) * amplitude[:, :, :, None]
        decayed_g, g_low = split_bf16(scaled_g)
        dstate = jnp.einsum("cthp,ctn->hpn", decayed_g, c_cand, preferred_element_type=jnp.float32)
        return g_heads, decayed_g, g_low, dstate

    def x_work(x_cand, inverse, c_cand, b_cand):
        xc_heads = x_cand.reshape(cand_dev, cand_len, half_heads, head_size)
        x_high, x_low = split_bf16(xc_heads.astype(jnp.float32) * inverse[:, :, :, None])
        scores = jnp.einsum("ctn,csn->cts", c_cand, b_cand, preferred_element_type=jnp.float32)
        return x_high, x_low, scores

    inclusive, (levels, g_parts, x_parts) = suffix_sum(
        own_total,
        pre_axes,
        [
            (level_work, lambda done: (code_cand,)),
            (g_work, lambda done: (dy_cand, lengths, done[0][0], c_cand)),
            (x_work, lambda done: (x_cand, done[0][1], c_cand, b_cand)),
        ],
    )
    amplitude, inverse = levels
    g_heads, decayed_g, g_low, dstate = g_parts
    x_high, x_low, scores = x_parts
    later_total = inclusive - own_total
    token_at = jnp.arange(pre_len, dtype=jnp.int32)
    later_rows = (token_at[None, :] > token_at[:, None]).astype(jnp.float32)
    after_local = jnp.dot(later_rows, log_prefix, precision=lax.Precision.HIGHEST)
    weight = jnp.exp(after_local + later_total[None, :])
    weighted_b = (weight[:, :, None] * b_prefix[:, None, :].astype(jnp.float32)).astype(
        jnp.bfloat16
    )
    x_heads = x_prefix.reshape(pre_len, heads_total, head_size)
    state_full = jnp.einsum("jhp,jhn->hpn", x_heads, weighted_b, preferred_element_type=jnp.float32)
    seq_at = lax.axis_index("seq")
    state_halves = state_full.reshape(2, half_heads, head_size, nstate)
    mine_first = seq_at == 0
    own_half = lax.dynamic_index_in_dim(state_halves, seq_at, 0, keepdims=False)
    give_half = lax.dynamic_index_in_dim(state_halves, 1 - seq_at, 0, keepdims=False)
    init_local = own_half + other_core(give_half)

    grad_half = cand_sum_bf16(dstate)
    init_half = cand_sum_bf16(init_local)
    grad_other = other_core(grad_half)
    grad_state = jnp.where(
        mine_first,
        jnp.concatenate([grad_half, grad_other], axis=0),
        jnp.concatenate([grad_other, grad_half], axis=0),
    )

    causal = position[:, None] >= position[None, :]
    flat = (cand_dev, cand_len, half_width)

    def pair(left, right):
        return jnp.einsum(
            "ctk,csk->cts", left.reshape(flat), right.reshape(flat),
            preferred_element_type=jnp.float32,
        )

    weight_sum = pair(decayed_g, x_high) + pair(decayed_g, x_low) + pair(g_low, x_high)
    weight_sum = jnp.where(causal[None], weight_sum, 0.0)
    db_part = jnp.einsum(
        "cts,ctn->csn", weight_sum, c_cand.astype(jnp.float32), precision=lax.Precision.HIGHEST
    )
    dc_part = jnp.einsum(
        "cts,csn->ctn", weight_sum, b_cand.astype(jnp.float32), precision=lax.Precision.HIGHEST
    )

    amp_t = jnp.transpose(amplitude, (0, 2, 1))
    inv_t = jnp.transpose(inverse, (0, 2, 1))
    decay_mat = amp_t[:, :, :, None] * inv_t[:, :, None, :]
    kernel = jnp.where(causal[None, None], scores[:, None] * decay_mat, 0.0).astype(jnp.bfloat16)
    dx_cand = jnp.einsum("chts,cthp->cshp", kernel, g_heads, preferred_element_type=jnp.float32)
    dx_cand = dx_cand.astype(jnp.bfloat16).reshape(flat)

    dc_state = jnp.dot(
        decayed_g.reshape(cand_dev * cand_len, half_width),
        init_half.reshape(half_width, nstate),
        preferred_element_type=jnp.float32,
    )
    dc_total = dc_part + dc_state.reshape(cand_dev, cand_len, nstate)
    def token_half_sum(part):
        halves = part.reshape(cand_dev, 2, cand_len // 2, part.shape[2])
        own = lax.dynamic_index_in_dim(halves, seq_at, 1, keepdims=False)
        give = lax.dynamic_index_in_dim(halves, 1 - seq_at, 1, keepdims=False)
        return own + other_core(give)

    db_dc = token_half_sum(jnp.concatenate([db_part, dc_total], axis=2))
    db_cand, dc_cand = db_dc[:, :, :nstate], db_dc[:, :, nstate:]

    dx_prefix = jnp.einsum(
        "jhn,hpn->jhp", weighted_b, grad_state, preferred_element_type=jnp.float32
    )
    dx_prefix = dx_prefix.astype(jnp.bfloat16).reshape(pre_len, width)
    projected = jnp.einsum("jhp,hpn->jhn", x_heads, grad_state, preferred_element_type=jnp.float32)
    db_prefix = jnp.sum(projected * weight[:, :, None], axis=1)
    return (dx_prefix, db_prefix, dx_cand, db_cand, dc_cand)


def solution(mesh):
    return jax.shard_map(
        shards,
        mesh=mesh,
        in_specs=(
            P(("grp", "cand", "seq"), None),
            P(("grp", "cand", "seq"), None),
            P(("grp", "cand", "seq"), None),
            P(("grp", "cand"), None, "seq"),
            P(("grp", "cand"), None, None),
            P(("grp", "cand"), None, None),
            P(("grp", "cand"), None, "seq"),
            P(("grp", "cand")),
            P(("grp", "cand"), None, "seq"),
        ),
        out_specs=(
            P(("grp", "cand", "seq"), None),
            P(("grp", "cand", "seq"), None),
            P(("grp", "cand"), None, "seq"),
            P(("grp", "cand"), "seq", None),
            P(("grp", "cand"), "seq", None),
        ),
        check_vma=False,
    )
```

```python
import jax
import jax.numpy as jnp
from jax import lax
from jax.sharding import PartitionSpec as P

BLOCK = 256


def split_bf16(value):
    high = lax.reduce_precision(value, exponent_bits=8, mantissa_bits=7)
    low = (value - high).astype(jnp.bfloat16)
    return high.astype(jnp.bfloat16), low


def butterfly_sum(value, axis):
    count = lax.axis_size(axis)
    step = 1
    while step < count:
        partner = [(at, at ^ step) for at in range(count)]
        value = value + lax.ppermute(value, axis, partner)
        step *= 2
    return value


def suffix_sum(value, axis, works):
    count = lax.axis_size(axis)
    step = 1
    done = []
    rounds = 0
    while step < count:
        back = [(at, at - step) for at in range(step, count)]
        if rounds < len(works):
            fn, pick = works[rounds]
            value, args = lax.optimization_barrier((value, pick(done)))
        value = value + lax.ppermute(value, axis, back)
        if rounds < len(works):
            value, piece = lax.optimization_barrier((value, fn(*args)))
            done.append(piece)
        step *= 2
        rounds += 1
    return value, done


def bit_order(value, count, first_bits):
    nbits = count.bit_length() - 1
    rest = value.shape[1:]
    value = value.reshape((2,) * nbits + rest)
    axes = [nbits - 1 - bit for bit in first_bits]
    value = jnp.transpose(value, axes + list(range(nbits, nbits + len(rest))))
    return value.reshape((count,) + rest)


def halving_scatter(blocks, axis):
    count = lax.axis_size(axis)
    me = lax.axis_index(axis)
    rest = blocks.shape[1:]
    nbits = count.bit_length() - 1
    value = bit_order(blocks, count, list(range(nbits)))
    for bit in range(nbits):
        step = 1 << bit
        value = value.reshape((2, -1) + rest)
        upper = me // step % 2
        keep = lax.dynamic_index_in_dim(value, upper, 0, keepdims=False)
        give = lax.dynamic_index_in_dim(value, 1 - upper, 0, keepdims=False)
        value = keep + lax.ppermute(give, axis, [(at, at ^ step) for at in range(count)])
    return value[0]


def doubling_gather(piece, axis):
    count = lax.axis_size(axis)
    me = lax.axis_index(axis)
    nbits = count.bit_length() - 1
    value = piece[None]
    for bit in reversed(range(nbits)):
        step = 1 << bit
        other = lax.ppermute(value, axis, [(at, at ^ step) for at in range(count)])
        upper = me // step % 2
        both = jnp.stack([value, other])
        value = jnp.concatenate([
            lax.dynamic_index_in_dim(both, upper, 0, keepdims=False),
            lax.dynamic_index_in_dim(both, 1 - upper, 0, keepdims=False),
        ])
    rest = piece.shape
    value = value.reshape((2,) * nbits + rest)
    axes = list(reversed(range(nbits)))
    value = jnp.transpose(value, axes + list(range(nbits, nbits + len(rest))))
    return value.reshape((count,) + rest)


def cand_sum_bf16(state):
    heads, size, width = state.shape
    count = lax.axis_size("cand")
    piece = size // count
    blocks = jnp.transpose(state.reshape(heads, count, piece, width), (1, 0, 2, 3))
    summed = halving_scatter(blocks, "cand").astype(jnp.bfloat16)
    gathered = doubling_gather(summed, "cand")
    return jnp.transpose(gathered, (1, 0, 2, 3)).reshape(heads, size, width)


def other_core(value):
    count = lax.axis_size("seq")
    return lax.ppermute(value, "seq", [(at, (at + 1) % count) for at in range(count)])


def shards(x_prefix, b_prefix, code_prefix, x_cand, b_cand, c_cand, code_cand, lengths, dy_cand):
    pre_len, width = x_prefix.shape
    heads_total = code_prefix.shape[1]
    head_size = width // heads_total
    nstate = b_prefix.shape[1]
    cand_dev, cand_len, half_width = x_cand.shape
    half_heads = code_cand.shape[2]
    pre_axes = ("cand", "seq")

    log_prefix = jnp.log1p(-code_prefix.astype(jnp.float32) * 1e-06)
    own_total = jnp.sum(log_prefix, axis=0)
    position = jnp.arange(cand_len, dtype=jnp.int32)

    def level_work(code_cand):
        rates = jnp.log1p(-code_cand.astype(jnp.float32) * 1e-06)
        lower = (position[:, None] >= position[None, :]).astype(jnp.float32)
        level_all = jnp.einsum("ts,csh->cth", lower, rates, precision=lax.Precision.HIGHEST)
        return jnp.exp(level_all), jnp.exp(-level_all)

    def g_work(dy_cand, lengths, amplitude, c_cand):
        valid_rows = position[None, :] < lengths[:, None] * BLOCK
        g_cand = jnp.where(valid_rows[:, :, None], dy_cand, jnp.zeros_like(dy_cand))
        g_heads = g_cand.reshape(cand_dev, cand_len, half_heads, head_size)
        scaled_g = g_heads.astype(jnp.float32) * amplitude[:, :, :, None]
        decayed_g, g_low = split_bf16(scaled_g)
        dstate = jnp.einsum("cthp,ctn->hpn", decayed_g, c_cand, preferred_element_type=jnp.float32)
        return g_heads, decayed_g, g_low, dstate

    def x_work(x_cand, inverse, c_cand, b_cand):
        xc_heads = x_cand.reshape(cand_dev, cand_len, half_heads, head_size)
        x_high, x_low = split_bf16(xc_heads.astype(jnp.float32) * inverse[:, :, :, None])
        scores = jnp.einsum("ctn,csn->cts", c_cand, b_cand, preferred_element_type=jnp.float32)
        return x_high, x_low, scores

    inclusive, (levels, g_parts, x_parts) = suffix_sum(
        own_total,
        pre_axes,
        [
            (level_work, lambda done: (code_cand,)),
            (g_work, lambda done: (dy_cand, lengths, done[0][0], c_cand)),
            (x_work, lambda done: (x_cand, done[0][1], c_cand, b_cand)),
        ],
    )
    amplitude, inverse = levels
    g_heads, decayed_g, g_low, dstate = g_parts
    x_high, x_low, scores = x_parts
    later_total = inclusive - own_total
    token_at = jnp.arange(pre_len, dtype=jnp.int32)
    later_rows = (token_at[None, :] > token_at[:, None]).astype(jnp.float32)
    after_local = jnp.dot(later_rows, log_prefix, precision=lax.Precision.HIGHEST)
    weight = jnp.exp(after_local + later_total[None, :])
    weighted_b = (weight[:, :, None] * b_prefix[:, None, :].astype(jnp.float32)).astype(
        jnp.bfloat16
    )
    x_heads = x_prefix.reshape(pre_len, heads_total, head_size)
    state_full = jnp.einsum("jhp,jhn->hpn", x_heads, weighted_b, preferred_element_type=jnp.float32)
    seq_at = lax.axis_index("seq")
    state_halves = state_full.reshape(2, half_heads, head_size, nstate)
    mine_first = seq_at == 0
    own_half = lax.dynamic_index_in_dim(state_halves, seq_at, 0, keepdims=False)
    give_half = lax.dynamic_index_in_dim(state_halves, 1 - seq_at, 0, keepdims=False)
    init_local = own_half + other_core(give_half)

    grad_half = cand_sum_bf16(dstate)
    init_half = cand_sum_bf16(init_local)
    grad_other = other_core(grad_half)
    grad_state = jnp.where(
        mine_first,
        jnp.concatenate([grad_half, grad_other], axis=0),
        jnp.concatenate([grad_other, grad_half], axis=0),
    )

    causal = position[:, None] >= position[None, :]
    flat = (cand_dev, cand_len, half_width)

    def pair(left, right):
        return jnp.einsum(
            "ctk,csk->cts", left.reshape(flat), right.reshape(flat),
            preferred_element_type=jnp.float32,
        )

    weight_sum = pair(decayed_g, x_high) + pair(decayed_g, x_low) + pair(g_low, x_high)
    weight_sum = jnp.where(causal[None], weight_sum, 0.0)
    db_part = jnp.einsum(
        "cts,ctn->csn", weight_sum, c_cand.astype(jnp.float32), precision=lax.Precision.HIGHEST
    )
    dc_part = jnp.einsum(
        "cts,csn->ctn", weight_sum, b_cand.astype(jnp.float32), precision=lax.Precision.HIGHEST
    )

    amp_t = jnp.transpose(amplitude, (0, 2, 1))
    inv_t = jnp.transpose(inverse, (0, 2, 1))
    decay_mat = amp_t[:, :, :, None] * inv_t[:, :, None, :]
    kernel = jnp.where(causal[None, None], scores[:, None] * decay_mat, 0.0).astype(jnp.bfloat16)
    dx_cand = jnp.einsum("chts,cthp->cshp", kernel, g_heads, preferred_element_type=jnp.float32)
    dx_cand = dx_cand.astype(jnp.bfloat16).reshape(flat)

    dc_state = jnp.dot(
        decayed_g.reshape(cand_dev * cand_len, half_width),
        init_half.reshape(half_width, nstate),
        preferred_element_type=jnp.float32,
    )
    dc_total = dc_part + dc_state.reshape(cand_dev, cand_len, nstate)
    def token_half_sum(part):
        halves = part.reshape(cand_dev, 2, cand_len // 2, part.shape[2])
        own = lax.dynamic_index_in_dim(halves, seq_at, 1, keepdims=False)
        give = lax.dynamic_index_in_dim(halves, 1 - seq_at, 1, keepdims=False)
        return own + other_core(give)

    db_dc = token_half_sum(jnp.concatenate([db_part, dc_total], axis=2))
    db_cand, dc_cand = db_dc[:, :, :nstate], db_dc[:, :, nstate:]

    dx_prefix = jnp.einsum(
        "jhn,hpn->jhp", weighted_b, grad_state, preferred_element_type=jnp.float32
    )
    dx_prefix = dx_prefix.astype(jnp.bfloat16).reshape(pre_len, width)
    projected = jnp.einsum("jhp,hpn->jhn", x_heads, grad_state, preferred_element_type=jnp.float32)
    db_prefix = jnp.sum(projected * weight[:, :, None], axis=1)
    return (dx_prefix, db_prefix, dx_cand, db_cand, dc_cand)


def solution(mesh):
    return jax.shard_map(
        shards,
        mesh=mesh,
        in_specs=(
            P(("grp", "cand", "seq"), None),
            P(("grp", "cand", "seq"), None),
            P(("grp", "cand", "seq"), None),
            P(("grp", "cand"), None, "seq"),
            P(("grp", "cand"), None, None),
            P(("grp", "cand"), None, None),
            P(("grp", "cand"), None, "seq"),
            P(("grp", "cand")),
            P(("grp", "cand"), None, "seq"),
        ),
        out_specs=(
            P(("grp", "cand", "seq"), None),
            P(("grp", "cand", "seq"), None),
            P(("grp", "cand"), None, "seq"),
            P(("grp", "cand"), "seq", None),
            P(("grp", "cand"), "seq", None),
        ),
        check_vma=False,
    )
```

```python
import jax
import jax.numpy as jnp
from jax import lax
from jax.sharding import PartitionSpec as P

BLOCK = 256


def split_bf16(value):
    high = lax.reduce_precision(value, exponent_bits=8, mantissa_bits=7)
    low = (value - high).astype(jnp.bfloat16)
    return high.astype(jnp.bfloat16), low


def butterfly_sum(value, axis):
    count = lax.axis_size(axis)
    step = 1
    while step < count:
        partner = [(at, at ^ step) for at in range(count)]
        value = value + lax.ppermute(value, axis, partner)
        step *= 2
    return value


def suffix_sum(value, axis, works):
    count = lax.axis_size(axis)
    step = 1
    done = []
    rounds = 0
    while step < count:
        back = [(at, at - step) for at in range(step, count)]
        if rounds < len(works):
            fn, pick = works[rounds]
            value, args = lax.optimization_barrier((value, pick(done)))
        value = value + lax.ppermute(value, axis, back)
        if rounds < len(works):
            value, piece = lax.optimization_barrier((value, fn(*args)))
            done.append(piece)
        step *= 2
        rounds += 1
    return value, done


def bit_order(value, count, first_bits):
    nbits = count.bit_length() - 1
    rest = value.shape[1:]
    value = value.reshape((2,) * nbits + rest)
    axes = [nbits - 1 - bit for bit in first_bits]
    value = jnp.transpose(value, axes + list(range(nbits, nbits + len(rest))))
    return value.reshape((count,) + rest)


def halving_scatter(blocks, axis):
    count = lax.axis_size(axis)
    me = lax.axis_index(axis)
    rest = blocks.shape[1:]
    nbits = count.bit_length() - 1
    value = bit_order(blocks, count, list(range(nbits)))
    for bit in range(nbits):
        step = 1 << bit
        value = value.reshape((2, -1) + rest)
        upper = me // step % 2
        keep = lax.dynamic_index_in_dim(value, upper, 0, keepdims=False)
        give = lax.dynamic_index_in_dim(value, 1 - upper, 0, keepdims=False)
        value = keep + lax.ppermute(give, axis, [(at, at ^ step) for at in range(count)])
    return value[0]


def doubling_gather(piece, axis):
    count = lax.axis_size(axis)
    me = lax.axis_index(axis)
    nbits = count.bit_length() - 1
    value = piece[None]
    for bit in reversed(range(nbits)):
        step = 1 << bit
        other = lax.ppermute(value, axis, [(at, at ^ step) for at in range(count)])
        upper = me // step % 2 == 1
        value = jnp.where(
            upper, jnp.concatenate([other, value]), jnp.concatenate([value, other])
        )
    rest = piece.shape
    value = value.reshape((2,) * nbits + rest)
    axes = list(reversed(range(nbits)))
    value = jnp.transpose(value, axes + list(range(nbits, nbits + len(rest))))
    return value.reshape((count,) + rest)


def cand_sum_bf16(state):
    heads, size, width = state.shape
    count = lax.axis_size("cand")
    piece = size // count
    blocks = jnp.transpose(state.reshape(heads, count, piece, width), (1, 0, 2, 3))
    summed = halving_scatter(blocks, "cand").astype(jnp.bfloat16)
    gathered = doubling_gather(summed, "cand")
    return jnp.transpose(gathered, (1, 0, 2, 3)).reshape(heads, size, width)


def other_core(value):
    count = lax.axis_size("seq")
    return lax.ppermute(value, "seq", [(at, (at + 1) % count) for at in range(count)])


def shards(x_prefix, b_prefix, code_prefix, x_cand, b_cand, c_cand, code_cand, lengths, dy_cand):
    pre_len, width = x_prefix.shape
    heads_total = code_prefix.shape[1]
    head_size = width // heads_total
    nstate = b_prefix.shape[1]
    cand_dev, cand_len, half_width = x_cand.shape
    half_heads = code_cand.shape[2]
    pre_axes = ("cand", "seq")

    log_prefix = jnp.log1p(-code_prefix.astype(jnp.float32) * 1e-06)
    own_total = jnp.sum(log_prefix, axis=0)
    position = jnp.arange(cand_len, dtype=jnp.int32)

    def level_work(code_cand):
        rates = jnp.log1p(-code_cand.astype(jnp.float32) * 1e-06)
        lower = (position[:, None] >= position[None, :]).astype(jnp.float32)
        level_all = jnp.einsum("ts,csh->cth", lower, rates, precision=lax.Precision.HIGHEST)
        return jnp.exp(level_all), jnp.exp(-level_all)

    def g_work(dy_cand, lengths, amplitude, c_cand):
        valid_rows = position[None, :] < lengths[:, None] * BLOCK
        g_cand = jnp.where(valid_rows[:, :, None], dy_cand, jnp.zeros_like(dy_cand))
        g_heads = g_cand.reshape(cand_dev, cand_len, half_heads, head_size)
        scaled_g = g_heads.astype(jnp.float32) * amplitude[:, :, :, None]
        decayed_g, g_low = split_bf16(scaled_g)
        dstate = jnp.einsum("cthp,ctn->hpn", decayed_g, c_cand, preferred_element_type=jnp.float32)
        return g_heads, decayed_g, g_low, dstate

    def x_work(x_cand, inverse, c_cand, b_cand):
        xc_heads = x_cand.reshape(cand_dev, cand_len, half_heads, head_size)
        x_high, x_low = split_bf16(xc_heads.astype(jnp.float32) * inverse[:, :, :, None])
        scores = jnp.einsum("ctn,csn->cts", c_cand, b_cand, preferred_element_type=jnp.float32)
        return x_high, x_low, scores

    inclusive, (levels, g_parts, x_parts) = suffix_sum(
        own_total,
        pre_axes,
        [
            (level_work, lambda done: (code_cand,)),
            (g_work, lambda done: (dy_cand, lengths, done[0][0], c_cand)),
            (x_work, lambda done: (x_cand, done[0][1], c_cand, b_cand)),
        ],
    )
    amplitude, inverse = levels
    g_heads, decayed_g, g_low, dstate = g_parts
    x_high, x_low, scores = x_parts
    later_total = inclusive - own_total
    token_at = jnp.arange(pre_len, dtype=jnp.int32)
    later_rows = (token_at[None, :] > token_at[:, None]).astype(jnp.float32)
    after_local = jnp.dot(later_rows, log_prefix, precision=lax.Precision.HIGHEST)
    weight = jnp.exp(after_local + later_total[None, :])
    weighted_b = (weight[:, :, None] * b_prefix[:, None, :].astype(jnp.float32)).astype(
        jnp.bfloat16
    )
    x_heads = x_prefix.reshape(pre_len, heads_total, head_size)
    state_full = jnp.einsum("jhp,jhn->hpn", x_heads, weighted_b, preferred_element_type=jnp.float32)
    seq_at = lax.axis_index("seq")
    state_halves = state_full.reshape(2, half_heads, head_size, nstate)
    mine_first = seq_at == 0
    own_half = lax.dynamic_index_in_dim(state_halves, seq_at, 0, keepdims=False)
    give_half = lax.dynamic_index_in_dim(state_halves, 1 - seq_at, 0, keepdims=False)
    init_local = own_half + other_core(give_half)

    grad_half = cand_sum_bf16(dstate)
    init_half = cand_sum_bf16(init_local)
    grad_other = other_core(grad_half)
    grad_state = jnp.where(
        mine_first,
        jnp.concatenate([grad_half, grad_other], axis=0),
        jnp.concatenate([grad_other, grad_half], axis=0),
    )

    causal = position[:, None] >= position[None, :]
    flat = (cand_dev, cand_len, half_width)

    def pair(left, right):
        return jnp.einsum(
            "ctk,csk->cts", left.reshape(flat), right.reshape(flat),
            preferred_element_type=jnp.float32,
        )

    weight_sum = pair(decayed_g, x_high) + pair(decayed_g, x_low) + pair(g_low, x_high)
    weight_sum = jnp.where(causal[None], weight_sum, 0.0)
    sum_high, sum_low = split_bf16(weight_sum)

    def two_pass(spec, other):
        return jnp.einsum(spec, sum_high, other, preferred_element_type=jnp.float32) + jnp.einsum(
            spec, sum_low, other, preferred_element_type=jnp.float32
        )

    db_part = two_pass("cts,ctn->csn", c_cand)
    dc_part = two_pass("cts,csn->ctn", b_cand)

    amp_t = jnp.transpose(amplitude, (0, 2, 1))
    inv_t = jnp.transpose(inverse, (0, 2, 1))
    decay_mat = amp_t[:, :, :, None] * inv_t[:, :, None, :]
    kernel = jnp.where(causal[None, None], scores[:, None] * decay_mat, 0.0).astype(jnp.bfloat16)
    dx_cand = jnp.einsum("chts,cthp->cshp", kernel, g_heads, preferred_element_type=jnp.float32)
    dx_cand = dx_cand.astype(jnp.bfloat16).reshape(flat)

    dc_state = jnp.dot(
        decayed_g.reshape(cand_dev * cand_len, half_width),
        init_half.reshape(half_width, nstate),
        preferred_element_type=jnp.float32,
    )
    dc_total = dc_part + dc_state.reshape(cand_dev, cand_len, nstate)
    def token_half_sum(part):
        halves = part.reshape(cand_dev, 2, cand_len // 2, part.shape[2])
        own = lax.dynamic_index_in_dim(halves, seq_at, 1, keepdims=False)
        give = lax.dynamic_index_in_dim(halves, 1 - seq_at, 1, keepdims=False)
        return own + other_core(give)

    db_dc = token_half_sum(jnp.concatenate([db_part, dc_total], axis=2))
    db_cand, dc_cand = db_dc[:, :, :nstate], db_dc[:, :, nstate:]

    dx_prefix = jnp.einsum(
        "jhn,hpn->jhp", weighted_b, grad_state, preferred_element_type=jnp.float32
    )
    dx_prefix = dx_prefix.astype(jnp.bfloat16).reshape(pre_len, width)
    projected = jnp.einsum("jhp,hpn->jhn", x_heads, grad_state, preferred_element_type=jnp.float32)
    db_prefix = jnp.sum(projected * weight[:, :, None], axis=1)
    return (dx_prefix, db_prefix, dx_cand, db_cand, dc_cand)


def solution(mesh):
    return jax.shard_map(
        shards,
        mesh=mesh,
        in_specs=(
            P(("grp", "cand", "seq"), None),
            P(("grp", "cand", "seq"), None),
            P(("grp", "cand", "seq"), None),
            P(("grp", "cand"), None, "seq"),
            P(("grp", "cand"), None, None),
            P(("grp", "cand"), None, None),
            P(("grp", "cand"), None, "seq"),
            P(("grp", "cand")),
            P(("grp", "cand"), None, "seq"),
        ),
        out_specs=(
            P(("grp", "cand", "seq"), None),
            P(("grp", "cand", "seq"), None),
            P(("grp", "cand"), None, "seq"),
            P(("grp", "cand"), "seq", None),
            P(("grp", "cand"), "seq", None),
        ),
        check_vma=False,
    )
```

```python
import jax
import jax.numpy as jnp
from jax import lax
from jax.sharding import PartitionSpec as P

BLOCK = 256


def split_bf16(value):
    high = lax.reduce_precision(value, exponent_bits=8, mantissa_bits=7)
    low = (value - high).astype(jnp.bfloat16)
    return high.astype(jnp.bfloat16), low


def exact_sum_dot(ones, value, spec):
    high = lax.reduce_precision(value, exponent_bits=8, mantissa_bits=7)
    rest = value - high
    mid = lax.reduce_precision(rest, exponent_bits=8, mantissa_bits=7)
    low = rest - mid
    total = jnp.einsum(spec, ones, high.astype(jnp.bfloat16), preferred_element_type=jnp.float32)
    total = total + jnp.einsum(spec, ones, mid.astype(jnp.bfloat16), preferred_element_type=jnp.float32)
    return total + jnp.einsum(spec, ones, low.astype(jnp.bfloat16), preferred_element_type=jnp.float32)


def butterfly_sum(value, axis):
    count = lax.axis_size(axis)
    step = 1
    while step < count:
        partner = [(at, at ^ step) for at in range(count)]
        value = value + lax.ppermute(value, axis, partner)
        step *= 2
    return value


def suffix_sum(value, axis, works):
    count = lax.axis_size(axis)
    step = 1
    done = []
    rounds = 0
    while step < count:
        back = [(at, at - step) for at in range(step, count)]
        if rounds < len(works):
            fn, pick = works[rounds]
            value, args = lax.optimization_barrier((value, pick(done)))
        value = value + lax.ppermute(value, axis, back)
        if rounds < len(works):
            value, piece = lax.optimization_barrier((value, fn(*args)))
            done.append(piece)
        step *= 2
        rounds += 1
    return value, done


def bit_order(value, count, first_bits):
    nbits = count.bit_length() - 1
    rest = value.shape[1:]
    value = value.reshape((2,) * nbits + rest)
    axes = [nbits - 1 - bit for bit in first_bits]
    value = jnp.transpose(value, axes + list(range(nbits, nbits + len(rest))))
    return value.reshape((count,) + rest)


def halving_scatter(blocks, axis):
    count = lax.axis_size(axis)
    me = lax.axis_index(axis)
    rest = blocks.shape[1:]
    nbits = count.bit_length() - 1
    value = bit_order(blocks, count, list(range(nbits)))
    for bit in range(nbits):
        step = 1 << bit
        value = value.reshape((2, -1) + rest)
        upper = me // step % 2
        keep = lax.dynamic_index_in_dim(value, upper, 0, keepdims=False)
        give = lax.dynamic_index_in_dim(value, 1 - upper, 0, keepdims=False)
        value = keep + lax.ppermute(give, axis, [(at, at ^ step) for at in range(count)])
    return value[0]


def doubling_gather(piece, axis):
    count = lax.axis_size(axis)
    me = lax.axis_index(axis)
    nbits = count.bit_length() - 1
    value = piece[None]
    for bit in reversed(range(nbits)):
        step = 1 << bit
        other = lax.ppermute(value, axis, [(at, at ^ step) for at in range(count)])
        upper = me // step % 2 == 1
        value = jnp.where(
            upper, jnp.concatenate([other, value]), jnp.concatenate([value, other])
        )
    rest = piece.shape
    value = value.reshape((2,) * nbits + rest)
    axes = list(reversed(range(nbits)))
    value = jnp.transpose(value, axes + list(range(nbits, nbits + len(rest))))
    return value.reshape((count,) + rest)


def cand_sum_bf16(state):
    heads, size, width = state.shape
    count = lax.axis_size("cand")
    piece = size // count
    blocks = jnp.transpose(state.reshape(heads, count, piece, width), (1, 0, 2, 3))
    summed = halving_scatter(blocks, "cand").astype(jnp.bfloat16)
    gathered = doubling_gather(summed, "cand")
    return jnp.transpose(gathered, (1, 0, 2, 3)).reshape(heads, size, width)


def other_core(value):
    count = lax.axis_size("seq")
    return lax.ppermute(value, "seq", [(at, (at + 1) % count) for at in range(count)])


def shards(x_prefix, b_prefix, code_prefix, x_cand, b_cand, c_cand, code_cand, lengths, dy_cand):
    pre_len, width = x_prefix.shape
    heads_total = code_prefix.shape[1]
    head_size = width // heads_total
    nstate = b_prefix.shape[1]
    cand_dev, cand_len, half_width = x_cand.shape
    half_heads = code_cand.shape[2]
    pre_axes = ("cand", "seq")

    log_prefix = jnp.log1p(-code_prefix.astype(jnp.float32) * 1e-06)
    own_total = jnp.sum(log_prefix, axis=0)
    position = jnp.arange(cand_len, dtype=jnp.int32)

    def level_work(code_cand):
        rates = jnp.log1p(-code_cand.astype(jnp.float32) * 1e-06)
        lower = (position[:, None] >= position[None, :]).astype(jnp.bfloat16)
        level_all = exact_sum_dot(lower, rates, "ts,csh->cth")
        return jnp.exp(level_all), jnp.exp(-level_all)

    def g_work(dy_cand, lengths, amplitude, c_cand):
        valid_rows = position[None, :] < lengths[:, None] * BLOCK
        g_cand = jnp.where(valid_rows[:, :, None], dy_cand, jnp.zeros_like(dy_cand))
        g_heads = g_cand.reshape(cand_dev, cand_len, half_heads, head_size)
        scaled_g = g_heads.astype(jnp.float32) * amplitude[:, :, :, None]
        decayed_g, g_low = split_bf16(scaled_g)
        dstate = jnp.einsum("cthp,ctn->hpn", decayed_g, c_cand, preferred_element_type=jnp.float32)
        return g_heads, decayed_g, g_low, dstate

    def x_work(x_cand, inverse, c_cand, b_cand):
        xc_heads = x_cand.reshape(cand_dev, cand_len, half_heads, head_size)
        x_high, x_low = split_bf16(xc_heads.astype(jnp.float32) * inverse[:, :, :, None])
        scores = jnp.einsum("ctn,csn->cts", c_cand, b_cand, preferred_element_type=jnp.float32)
        return x_high, x_low, scores

    inclusive, (levels, g_parts, x_parts) = suffix_sum(
        own_total,
        pre_axes,
        [
            (level_work, lambda done: (code_cand,)),
            (g_work, lambda done: (dy_cand, lengths, done[0][0], c_cand)),
            (x_work, lambda done: (x_cand, done[0][1], c_cand, b_cand)),
        ],
    )
    amplitude, inverse = levels
    g_heads, decayed_g, g_low, dstate = g_parts
    x_high, x_low, scores = x_parts
    later_total = inclusive - own_total
    token_at = jnp.arange(pre_len, dtype=jnp.int32)
    later_rows = (token_at[None, :] > token_at[:, None]).astype(jnp.bfloat16)
    after_local = exact_sum_dot(later_rows, log_prefix, "ji,ih->jh")
    weight = jnp.exp(after_local + later_total[None, :])
    weighted_b = (weight[:, :, None] * b_prefix[:, None, :].astype(jnp.float32)).astype(
        jnp.bfloat16
    )
    x_heads = x_prefix.reshape(pre_len, heads_total, head_size)
    state_full = jnp.einsum("jhp,jhn->hpn", x_heads, weighted_b, preferred_element_type=jnp.float32)
    seq_at = lax.axis_index("seq")
    state_halves = state_full.reshape(2, half_heads, head_size, nstate)
    mine_first = seq_at == 0
    own_half = lax.dynamic_index_in_dim(state_halves, seq_at, 0, keepdims=False)
    give_half = lax.dynamic_index_in_dim(state_halves, 1 - seq_at, 0, keepdims=False)
    init_local = own_half + other_core(give_half)

    grad_half = cand_sum_bf16(dstate)
    init_half = cand_sum_bf16(init_local)
    grad_other = other_core(grad_half)
    grad_state = jnp.where(
        mine_first,
        jnp.concatenate([grad_half, grad_other], axis=0),
        jnp.concatenate([grad_other, grad_half], axis=0),
    )

    causal = position[:, None] >= position[None, :]
    flat = (cand_dev, cand_len, half_width)

    def pair(left, right):
        return jnp.einsum(
            "ctk,csk->cts", left.reshape(flat), right.reshape(flat),
            preferred_element_type=jnp.float32,
        )

    weight_sum = pair(decayed_g, x_high) + pair(decayed_g, x_low) + pair(g_low, x_high)
    weight_sum = jnp.where(causal[None], weight_sum, 0.0)
    sum_high, sum_low = split_bf16(weight_sum)

    def two_pass(spec, other):
        return jnp.einsum(spec, sum_high, other, preferred_element_type=jnp.float32) + jnp.einsum(
            spec, sum_low, other, preferred_element_type=jnp.float32
        )

    db_part = two_pass("cts,ctn->csn", c_cand)
    dc_part = two_pass("cts,csn->ctn", b_cand)

    amp_t = jnp.transpose(amplitude, (0, 2, 1))
    inv_t = jnp.transpose(inverse, (0, 2, 1))
    decay_mat = amp_t[:, :, :, None] * inv_t[:, :, None, :]
    kernel = jnp.where(causal[None, None], scores[:, None] * decay_mat, 0.0).astype(jnp.bfloat16)
    dx_cand = jnp.einsum("chts,cthp->cshp", kernel, g_heads, preferred_element_type=jnp.float32)
    dx_cand = dx_cand.astype(jnp.bfloat16).reshape(flat)

    dc_state = jnp.dot(
        decayed_g.reshape(cand_dev * cand_len, half_width),
        init_half.reshape(half_width, nstate),
        preferred_element_type=jnp.float32,
    )
    dc_total = dc_part + dc_state.reshape(cand_dev, cand_len, nstate)
    def token_half_sum(part):
        halves = part.reshape(cand_dev, 2, cand_len // 2, part.shape[2])
        own = lax.dynamic_index_in_dim(halves, seq_at, 1, keepdims=False)
        give = lax.dynamic_index_in_dim(halves, 1 - seq_at, 1, keepdims=False)
        return own + other_core(give)

    db_dc = token_half_sum(jnp.concatenate([db_part, dc_total], axis=2))
    db_cand, dc_cand = db_dc[:, :, :nstate], db_dc[:, :, nstate:]

    dx_prefix = jnp.einsum(
        "jhn,hpn->jhp", weighted_b, grad_state, preferred_element_type=jnp.float32
    )
    dx_prefix = dx_prefix.astype(jnp.bfloat16).reshape(pre_len, width)
    projected = jnp.einsum("jhp,hpn->jhn", x_heads, grad_state, preferred_element_type=jnp.float32)
    db_prefix = jnp.sum(projected * weight[:, :, None], axis=1)
    return (dx_prefix, db_prefix, dx_cand, db_cand, dc_cand)


def solution(mesh):
    return jax.shard_map(
        shards,
        mesh=mesh,
        in_specs=(
            P(("grp", "cand", "seq"), None),
            P(("grp", "cand", "seq"), None),
            P(("grp", "cand", "seq"), None),
            P(("grp", "cand"), None, "seq"),
            P(("grp", "cand"), None, None),
            P(("grp", "cand"), None, None),
            P(("grp", "cand"), None, "seq"),
            P(("grp", "cand")),
            P(("grp", "cand"), None, "seq"),
        ),
        out_specs=(
            P(("grp", "cand", "seq"), None),
            P(("grp", "cand", "seq"), None),
            P(("grp", "cand"), None, "seq"),
            P(("grp", "cand"), "seq", None),
            P(("grp", "cand"), "seq", None),
        ),
        check_vma=False,
    )
```

```python
import jax
import jax.numpy as jnp
from jax import lax
from jax.sharding import PartitionSpec as P

BLOCK = 256


def split_bf16(value):
    high = lax.reduce_precision(value, exponent_bits=8, mantissa_bits=7)
    low = (value - high).astype(jnp.bfloat16)
    return high.astype(jnp.bfloat16), low


def butterfly_sum(value, axis):
    count = lax.axis_size(axis)
    step = 1
    while step < count:
        partner = [(at, at ^ step) for at in range(count)]
        value = value + lax.ppermute(value, axis, partner)
        step *= 2
    return value


def suffix_sum(value, axis, works):
    count = lax.axis_size(axis)
    step = 1
    done = []
    rounds = 0
    while step < count:
        back = [(at, at - step) for at in range(step, count)]
        if rounds < len(works):
            fn, pick = works[rounds]
            value, args = lax.optimization_barrier((value, pick(done)))
        value = value + lax.ppermute(value, axis, back)
        if rounds < len(works):
            value, piece = lax.optimization_barrier((value, fn(*args)))
            done.append(piece)
        step *= 2
        rounds += 1
    return value, done


def bit_order(value, count, first_bits):
    nbits = count.bit_length() - 1
    rest = value.shape[1:]
    value = value.reshape((2,) * nbits + rest)
    axes = [nbits - 1 - bit for bit in first_bits]
    value = jnp.transpose(value, axes + list(range(nbits, nbits + len(rest))))
    return value.reshape((count,) + rest)


def halving_scatter(blocks, axis):
    count = lax.axis_size(axis)
    me = lax.axis_index(axis)
    rest = blocks.shape[1:]
    nbits = count.bit_length() - 1
    value = bit_order(blocks, count, list(range(nbits)))
    for bit in range(nbits):
        step = 1 << bit
        value = value.reshape((2, -1) + rest)
        upper = me // step % 2
        keep = lax.dynamic_index_in_dim(value, upper, 0, keepdims=False)
        give = lax.dynamic_index_in_dim(value, 1 - upper, 0, keepdims=False)
        value = keep + lax.ppermute(give, axis, [(at, at ^ step) for at in range(count)])
    return value[0]


def doubling_gather(piece, axis):
    count = lax.axis_size(axis)
    me = lax.axis_index(axis)
    nbits = count.bit_length() - 1
    value = piece[None]
    for bit in reversed(range(nbits)):
        step = 1 << bit
        other = lax.ppermute(value, axis, [(at, at ^ step) for at in range(count)])
        upper = me // step % 2 == 1
        value = jnp.where(
            upper, jnp.concatenate([other, value]), jnp.concatenate([value, other])
        )
    rest = piece.shape
    value = value.reshape((2,) * nbits + rest)
    axes = list(reversed(range(nbits)))
    value = jnp.transpose(value, axes + list(range(nbits, nbits + len(rest))))
    return value.reshape((count,) + rest)


def cand_sum_bf16(state):
    heads, size, width = state.shape
    count = lax.axis_size("cand")
    piece = size // count
    blocks = jnp.transpose(state.reshape(heads, count, piece, width), (1, 0, 2, 3))
    summed = halving_scatter(blocks, "cand").astype(jnp.bfloat16)
    gathered = doubling_gather(summed, "cand")
    return jnp.transpose(gathered, (1, 0, 2, 3)).reshape(heads, size, width)


def other_core(value):
    count = lax.axis_size("seq")
    return lax.ppermute(value, "seq", [(at, (at + 1) % count) for at in range(count)])


def shards(x_prefix, b_prefix, code_prefix, x_cand, b_cand, c_cand, code_cand, lengths, dy_cand):
    pre_len, width = x_prefix.shape
    heads_total = code_prefix.shape[1]
    head_size = width // heads_total
    nstate = b_prefix.shape[1]
    cand_dev, cand_len, half_width = x_cand.shape
    half_heads = code_cand.shape[2]
    pre_axes = ("cand", "seq")

    log_prefix = jnp.log1p(-code_prefix.astype(jnp.float32) * 1e-06)
    own_total = jnp.sum(log_prefix, axis=0)
    position = jnp.arange(cand_len, dtype=jnp.int32)

    def level_work(code_cand):
        rates = jnp.log1p(-code_cand.astype(jnp.float32) * 1e-06)
        lower = (position[:, None] >= position[None, :]).astype(jnp.float32)
        level_all = jnp.einsum("ts,csh->cth", lower, rates, precision=lax.Precision.HIGHEST)
        return jnp.exp(level_all), jnp.exp(-level_all)

    def g_work(dy_cand, lengths, amplitude, c_cand):
        valid_rows = position[None, :] < lengths[:, None] * BLOCK
        g_cand = jnp.where(valid_rows[:, :, None], dy_cand, jnp.zeros_like(dy_cand))
        g_heads = g_cand.reshape(cand_dev, cand_len, half_heads, head_size)
        scaled_g = g_heads.astype(jnp.float32) * amplitude[:, :, :, None]
        decayed_g, g_low = split_bf16(scaled_g)
        dstate = jnp.einsum("cthp,ctn->hpn", decayed_g, c_cand, preferred_element_type=jnp.float32)
        return g_heads, decayed_g, g_low, dstate

    def x_work(x_cand, inverse, c_cand, b_cand):
        xc_heads = x_cand.reshape(cand_dev, cand_len, half_heads, head_size)
        x_high, x_low = split_bf16(xc_heads.astype(jnp.float32) * inverse[:, :, :, None])
        scores = jnp.einsum("ctn,csn->cts", c_cand, b_cand, preferred_element_type=jnp.float32)
        return x_high, x_low, scores

    inclusive, (levels, g_parts, x_parts) = suffix_sum(
        own_total,
        pre_axes,
        [
            (level_work, lambda done: (code_cand,)),
            (g_work, lambda done: (dy_cand, lengths, done[0][0], c_cand)),
            (x_work, lambda done: (x_cand, done[0][1], c_cand, b_cand)),
        ],
    )
    amplitude, inverse = levels
    g_heads, decayed_g, g_low, dstate = g_parts
    x_high, x_low, scores = x_parts
    later_total = inclusive - own_total
    token_at = jnp.arange(pre_len, dtype=jnp.int32)
    later_rows = (token_at[None, :] > token_at[:, None]).astype(jnp.float32)
    after_local = jnp.dot(later_rows, log_prefix, precision=lax.Precision.HIGHEST)
    weight = jnp.exp(after_local + later_total[None, :])
    weighted_b = (weight[:, :, None] * b_prefix[:, None, :].astype(jnp.float32)).astype(
        jnp.bfloat16
    )
    x_heads = x_prefix.reshape(pre_len, heads_total, head_size)
    state_full = jnp.einsum("jhp,jhn->hpn", x_heads, weighted_b, preferred_element_type=jnp.float32)
    seq_at = lax.axis_index("seq")
    state_halves = state_full.reshape(2, half_heads, head_size, nstate)
    mine_first = seq_at == 0
    own_half = lax.dynamic_index_in_dim(state_halves, seq_at, 0, keepdims=False)
    give_half = lax.dynamic_index_in_dim(state_halves, 1 - seq_at, 0, keepdims=False)
    init_local = own_half + other_core(give_half)

    grad_half = cand_sum_bf16(dstate)
    init_half = cand_sum_bf16(init_local)
    grad_other = other_core(grad_half)
    grad_state = jnp.where(
        mine_first,
        jnp.concatenate([grad_half, grad_other], axis=0),
        jnp.concatenate([grad_other, grad_half], axis=0),
    )

    causal = position[:, None] >= position[None, :]
    flat = (cand_dev, cand_len, half_width)

    def pair(left, right):
        return jnp.einsum(
            "ctk,csk->cts", left.reshape(flat), right.reshape(flat),
            preferred_element_type=jnp.float32,
        )

    cross_left = jnp.concatenate([decayed_g.reshape(flat), g_low.reshape(flat)], axis=2)
    cross_right = jnp.concatenate([x_low.reshape(flat), x_high.reshape(flat)], axis=2)
    cross = jnp.einsum("ctk,csk->cts", cross_left, cross_right, preferred_element_type=jnp.float32)
    weight_sum = pair(decayed_g, x_high) + cross
    weight_sum = jnp.where(causal[None], weight_sum, 0.0)
    sum_high, sum_low = split_bf16(weight_sum)

    def two_pass(spec, other):
        return jnp.einsum(spec, sum_high, other, preferred_element_type=jnp.float32) + jnp.einsum(
            spec, sum_low, other, preferred_element_type=jnp.float32
        )

    db_part = two_pass("cts,ctn->csn", c_cand)
    dc_part = two_pass("cts,csn->ctn", b_cand)

    amp_t = jnp.transpose(amplitude, (0, 2, 1))
    inv_t = jnp.transpose(inverse, (0, 2, 1))
    decay_mat = amp_t[:, :, :, None] * inv_t[:, :, None, :]
    kernel = jnp.where(causal[None, None], scores[:, None] * decay_mat, 0.0).astype(jnp.bfloat16)
    dx_cand = jnp.einsum("chts,cthp->cshp", kernel, g_heads, preferred_element_type=jnp.float32)
    dx_cand = dx_cand.astype(jnp.bfloat16).reshape(flat)

    dc_state = jnp.dot(
        decayed_g.reshape(cand_dev * cand_len, half_width),
        init_half.reshape(half_width, nstate),
        preferred_element_type=jnp.float32,
    )
    dc_total = dc_part + dc_state.reshape(cand_dev, cand_len, nstate)
    def token_half_sum(part):
        halves = part.reshape(cand_dev, 2, cand_len // 2, part.shape[2])
        own = lax.dynamic_index_in_dim(halves, seq_at, 1, keepdims=False)
        give = lax.dynamic_index_in_dim(halves, 1 - seq_at, 1, keepdims=False)
        return own + other_core(give)

    db_dc = token_half_sum(jnp.concatenate([db_part, dc_total], axis=2))
    db_cand, dc_cand = db_dc[:, :, :nstate], db_dc[:, :, nstate:]

    dx_prefix = jnp.einsum(
        "jhn,hpn->jhp", weighted_b, grad_state, preferred_element_type=jnp.float32
    )
    dx_prefix = dx_prefix.astype(jnp.bfloat16).reshape(pre_len, width)
    projected = jnp.einsum("jhp,hpn->jhn", x_heads, grad_state, preferred_element_type=jnp.float32)
    db_prefix = jnp.sum(projected * weight[:, :, None], axis=1)
    return (dx_prefix, db_prefix, dx_cand, db_cand, dc_cand)


def solution(mesh):
    return jax.shard_map(
        shards,
        mesh=mesh,
        in_specs=(
            P(("grp", "cand", "seq"), None),
            P(("grp", "cand", "seq"), None),
            P(("grp", "cand", "seq"), None),
            P(("grp", "cand"), None, "seq"),
            P(("grp", "cand"), None, None),
            P(("grp", "cand"), None, None),
            P(("grp", "cand"), None, "seq"),
            P(("grp", "cand")),
            P(("grp", "cand"), None, "seq"),
        ),
        out_specs=(
            P(("grp", "cand", "seq"), None),
            P(("grp", "cand", "seq"), None),
            P(("grp", "cand"), None, "seq"),
            P(("grp", "cand"), "seq", None),
            P(("grp", "cand"), "seq", None),
        ),
        check_vma=False,
    )
```
